32 devices in a mesh: seq: 8 (over z, x), tp: 4 (over y, core).
Axes of the slice: x: 2, y: 2, z: 4, core: 2. Of those that a mesh axis runs over, the one named last changes fastest.
Arguments:
- queries: bfloat16 [1024, 4096], P('seq', 'tp'), may hold values from -600 to 600
- suffix_keys: bfloat16 [1024, 1024], P('seq', 'tp'), may hold values from -6 to 6
- suffix_values: bfloat16 [1024, 1024], P('seq', 'tp'), may hold values from -6 to 6
- prefix_keys: bfloat16 [512, 1024], P('seq', 'tp'), may hold values from -6 to 6
- prefix_values: bfloat16 [512, 1024], P('seq', 'tp'), may hold values from -6 to 6
- suffix_lengths: int32 [24], replicated, may hold values from 1 to 128, 1024 in all
- request_group: int32 [24], replicated, may hold values from 0 to 3
- block_group: int32 [8], replicated, may hold values from 0 to 3, as said below
Outputs:
- attended: bfloat16 [1024, 4096], P('seq', 'tp')
- cache_keys: bfloat16 [1024, 1024], P(('seq', 'tp'))
- cache_values: bfloat16 [1024, 1024], P(('seq', 'tp'))
The draws below stay inside these ranges and needn't reach their ends.
Inputs may be any that keep to these rules, and one draw needn't show every extreme that they name: `suffix_lengths`: the suffixes fill the 1024 packed tokens end to end in order; the longest has exactly 128 tokens. `block_group`: each prefix is held by exactly 2 blocks, in any order.
All inputs are finite; a program needn't handle non-finite values.
Results may differ from the reference program's by a relative error of at most 0.009.
The reference program's roundings to bfloat16 on the way (of `q_rot` and `weights`) count: a program that leaves them out, or rounds other values in their place, can miss the bound.
Values may be sent and summed in bfloat16 or wider, within the bound.
No kernel may reach another device: no remote copies, remote signals or barrier semaphores. Data moves between devices by JAX's collectives and lax.ppermute only.
A program may use at most 64 MiB of HBM per device.

```python
import math
import jax
import jax.numpy as jnp
import numpy as np
from jax import lax

QH = 32
KVH = 8
HD = 128
GROUPS = 4
TOK_DEV = 128
PBLK = 64
SPAN = 1
MOST_LEN = 128
TOKENS = 1024
REQS = 24
PREFIX = 128


def draw_queries(key, part):
    base = jax.random.normal(jax.random.fold_in(key, 11), (TOKENS, QH * HD), jnp.float32)
    base = jnp.clip(base, -6.0, 6.0)
    return base.astype(jnp.bfloat16)


def draw_block_group(key, part):
    order = jax.random.permutation(jax.random.fold_in(key, 21), GROUPS * PREFIX // PBLK)
    return (order % GROUPS).astype(jnp.int32)


def place_ends(array, rng, low, largest):
    longest = array.shape.index(max(array.shape))
    spots = []
    for shift in (0, 1):
        where = [jax.random.randint(jax.random.fold_in(rng, axis), (), 0, length) for axis, length in enumerate(array.shape)]
        where[longest] = (where[longest] + shift) % array.shape[longest]
        spots.append(tuple(where))
    return array.at[spots[0]].set(low).at[spots[1]].set(largest)


def block_scale(stream_key, shape, cuts, least, largest):
    level, own = 1.0, jax.random.fold_in(stream_key, 6)
    for dim, parts in cuts:
        draws = jnp.exp(jax.random.uniform(jax.random.fold_in(own, dim), (parts,), jnp.float32, least / len(cuts), largest / len(cuts)))
        level = level * jnp.repeat(draws, shape[dim] // parts).reshape([-1 if axis == dim else 1 for axis in range(len(shape))])
    return level


def length_profile(amount, total, reach, slope):
    weights = [(1 << 20) // math.isqrt(rank ** slope) + 1 for rank in range(2, amount + 1)]
    rest, counts = total - reach - (amount - 1), [1] * (amount - 1)
    while rest > 0:
        movable = [i for i in range(amount - 1) if counts[i] < reach]
        whole, left = sum([weights[i] for i in movable]), rest
        for i in movable:
            extra = min(reach - counts[i], max(1, left * weights[i] // whole), rest)
            counts[i] = counts[i] + extra
            rest = rest - extra
    return np.array([reach] + counts)


def ragged_sizes(stream_key, amount, total, bound, slope):
    if amount == 2:
        one = jax.random.randint(stream_key, (), max(1, total - bound), min(bound, total - 1) + 1)
        return jnp.stack([one, total - one])
    sizes = jnp.asarray(length_profile(amount, total, bound, slope), jnp.int32)
    twos = (amount - 1) // 2
    source_of, receiver = sizes[1:1 + 2 * twos:2], sizes[2:2 + 2 * twos:2]
    room = jnp.minimum(source_of - 1, bound - receiver)
    passed = jax.random.randint(jax.random.fold_in(stream_key, 1), (twos,), 0, 1 << 20) % (room + 1)
    sizes = sizes.at[1:1 + 2 * twos:2].set(source_of - passed).at[2:2 + 2 * twos:2].set(receiver + passed)
    return sizes[jax.random.permutation(jax.random.fold_in(stream_key, 2), amount)]


def centred(stream_key, dims, deviation, reach, shards=(), held_as=jnp.bfloat16):
    loudness = block_scale(stream_key, dims, shards, -0.22, 0.18) if shards else 1.0
    array = jax.random.normal(stream_key, dims, jnp.float32) * deviation * loudness
    return jnp.minimum(jnp.maximum(array, -reach), reach).astype(held_as)


def setup_inputs(seed: int = 0) -> dict:
    key_of = jax.random.split(jax.random.key(seed), 9)
    return {
        "queries": draw_queries(jax.random.fold_in(key_of[8], 71), 0),
        "suffix_keys": centred(key_of[1], (TOKENS, KVH * HD), 1.0, 6.0, ((0, 8), (1, 4))),
        "suffix_values": centred(key_of[2], (TOKENS, KVH * HD), 1.0, 6.0, ((0, 8), (1, 4))),
        "prefix_keys": centred(key_of[3], (GROUPS * PREFIX, KVH * HD), 1.0, 6.0, ((0, 8), (1, 4))),
        "prefix_values": centred(key_of[4], (GROUPS * PREFIX, KVH * HD), 1.0, 6.0, ((0, 8), (1, 4))),
        "suffix_lengths": ragged_sizes(key_of[5], REQS, TOKENS, MOST_LEN, 2).astype(jnp.int32),
        "request_group": place_ends(jax.random.randint(key_of[6], (REQS,), 0, GROUPS), jax.random.fold_in(key_of[6], 1), 0, GROUPS - 1).astype(jnp.int32),
        "block_group": draw_block_group(jax.random.fold_in(key_of[8], 71), 0),
    }


BIG_NEGATIVE = -1.0e30


def rotate(values, position):
    half = values.shape[-1] // 2
    freq = jnp.exp(jnp.arange(half, dtype=jnp.float32) * (-2.0 * math.log(500000.0) / values.shape[-1]))
    angle = position.astype(jnp.float32)[:, None] * freq[None, :]
    cosine = jnp.cos(angle)[:, None, :]
    sine = jnp.sin(angle)[:, None, :]
    floats = values.astype(jnp.float32)
    lower = floats[..., :half]
    upper = floats[..., half:]
    return jnp.concatenate([lower * cosine - upper * sine, upper * cosine + lower * sine], axis=-1).astype(jnp.bfloat16)


def token_info(index, suffix_lengths, request_group):
    ends = jnp.cumsum(suffix_lengths)
    request = jnp.sum((index[:, None] >= ends[None, :]).astype(jnp.int32), axis=1)
    onehot = request[:, None] == jnp.arange(suffix_lengths.shape[0], dtype=jnp.int32)[None, :]
    first = jnp.sum(jnp.where(onehot, (ends - suffix_lengths)[None, :], 0), axis=1)
    group = jnp.sum(jnp.where(onehot, request_group[None, :], 0), axis=1)
    return request, index - first, group


def reference(queries, suffix_keys, suffix_values, prefix_keys, prefix_values, suffix_lengths, request_group, block_group):
    repeat = QH // KVH
    scale = HD ** -0.5
    index = jnp.arange(TOKENS, dtype=jnp.int32)
    request, offset, group = token_info(index, suffix_lengths, request_group)
    position = offset + PREFIX
    q_rot = rotate(queries.reshape(TOKENS, QH, HD), position)
    cache_keys = rotate(suffix_keys.reshape(TOKENS, KVH, HD), position).reshape(TOKENS, KVH * HD)
    margin = SPAN * TOK_DEV
    keys_padded = jnp.concatenate([jnp.zeros((margin, KVH * HD), jnp.bfloat16), cache_keys], axis=0)
    values_padded = jnp.concatenate([jnp.zeros((margin, KVH * HD), jnp.bfloat16), suffix_values], axis=0)
    request_padded = jnp.concatenate([jnp.full((margin,), -1, jnp.int32), request], axis=0)
    prefix_rows = GROUPS * PREFIX
    row_group = block_group[jnp.arange(prefix_rows, dtype=jnp.int32) // PBLK]
    prefix_k = prefix_keys.reshape(prefix_rows, KVH, HD).astype(jnp.float32)
    prefix_v = prefix_values.reshape(prefix_rows, KVH, HD).astype(jnp.float32)
    window = (SPAN + 1) * TOK_DEV

    def one_block(block):
        low = (block * TOK_DEV).astype(jnp.int32)
        query = lax.dynamic_slice_in_dim(q_rot, low, TOK_DEV, 0).astype(jnp.float32).reshape(TOK_DEV, KVH, repeat, HD)
        tok_index = low + jnp.arange(TOK_DEV, dtype=jnp.int32)
        tok_request = lax.dynamic_slice_in_dim(request, low, TOK_DEV, 0)
        tok_group = lax.dynamic_slice_in_dim(group, low, TOK_DEV, 0)
        near_k = lax.dynamic_slice_in_dim(keys_padded, low, window, 0).reshape(window, KVH, HD).astype(jnp.float32)
        near_v = lax.dynamic_slice_in_dim(values_padded, low, window, 0).reshape(window, KVH, HD).astype(jnp.float32)
        key_index = low - margin + jnp.arange(window, dtype=jnp.int32)
        key_request = lax.dynamic_slice_in_dim(request_padded, low, window, 0)
        near_mask = (key_request[None, :] == tok_request[:, None]) & (key_index[None, :] <= tok_index[:, None])
        far_mask = row_group[None, :] == tok_group[:, None]
        mask = jnp.concatenate([far_mask, near_mask], axis=1)[:, None, None, :]
        keys = jnp.concatenate([prefix_k, near_k], axis=0)
        values = jnp.concatenate([prefix_v, near_v], axis=0)
        scores = jnp.einsum("bgrd,kgd->bgrk", query, keys) * scale
        scores = jnp.where(mask, scores, BIG_NEGATIVE)
        high = jnp.max(scores, axis=-1, keepdims=True)
        weights = jnp.where(mask, jnp.exp(scores - high), 0.0)
        totals = jnp.sum(weights, axis=-1)
        rounded = lax.optimization_barrier(weights.astype(jnp.bfloat16))
        summed = jnp.einsum("bgrk,kgd->bgrd", rounded.astype(jnp.float32), values)
        return (summed / totals[..., None]).reshape(TOK_DEV, QH * HD).astype(jnp.bfloat16)

    attended = lax.map(one_block, jnp.arange(TOKENS // TOK_DEV, dtype=jnp.int32)).reshape(TOKENS, QH * HD)
    return (attended, cache_keys, suffix_values)
```

```python
import math

import jax
import jax.numpy as jnp
from jax import lax
from jax.sharding import PartitionSpec as P

HD = 128
GROUPS = 4


BIG_NEGATIVE = -1e30


def rotate(values, position):
    half = values.shape[-1] // 2
    freq = jnp.exp(
        jnp.arange(half, dtype=jnp.float32) * (-2.0 * math.log(500000.0) / values.shape[-1])
    )
    angle = position.astype(jnp.float32)[:, None] * freq[None, :]
    cosine = jnp.cos(angle)[:, None, :]
    sine = jnp.sin(angle)[:, None, :]
    floats = values.astype(jnp.float32)
    lower = floats[..., :half]
    upper = floats[..., half:]
    return jnp.concatenate(
        [lower * cosine - upper * sine, upper * cosine + lower * sine], axis=-1
    ).astype(jnp.bfloat16)


def token_info(index, suffix_lengths, request_group):
    ends = jnp.cumsum(suffix_lengths)
    request = jnp.sum((index[:, None] >= ends[None, :]).astype(jnp.int32), axis=1)
    onehot = request[:, None] == jnp.arange(suffix_lengths.shape[0], dtype=jnp.int32)[None, :]
    first = jnp.sum(jnp.where(onehot, (ends - suffix_lengths)[None, :], 0), axis=1)
    group = jnp.sum(jnp.where(onehot, request_group[None, :], 0), axis=1)
    return (request, index - first, group)


def shifted(array, axis, by, wrap):
    length = lax.axis_size(axis)
    pairs = [(i, (i + by) % length) for i in range(length) if wrap or i + by < length]
    return lax.ppermute(array, axis, pairs)


def body(
    queries,
    suffix_keys,
    suffix_values,
    prefix_keys,
    prefix_values,
    suffix_lengths,
    request_group,
    block_group,
):
    rows = queries.shape[0]
    kv_cols = suffix_keys.shape[1]
    kv_heads = kv_cols // HD
    q_heads = queries.shape[1] // HD
    repeat = q_heads // kv_heads
    devices = lax.axis_size("seq")
    me = lax.axis_index("seq")
    block_rows = prefix_keys.shape[0]
    prefix_len = block_rows * devices // GROUPS
    span = max(1, min(2048 // rows, devices // 8))
    scale = HD ** (-0.5)
    index = me * rows + jnp.arange(rows, dtype=jnp.int32)
    request, offset, group = token_info(index, suffix_lengths, request_group)

    prefix_kv = jnp.concatenate([prefix_keys, prefix_values], axis=1)
    suffix_kv = jnp.concatenate([suffix_keys, suffix_values], axis=1)

    prefix_parts = []
    suffix_parts = [(0, suffix_kv)]
    if devices <= 16:
        prefix_parts.append((me, prefix_kv))
        for by in range(1, devices):
            if by <= span:
                both = shifted(jnp.concatenate([prefix_kv, suffix_kv], axis=0), "seq", by, True)
                prefix_parts.append(((me - by) % devices, both[:block_rows]))
                suffix_parts.append((by, both[block_rows:]))
            else:
                part = shifted(prefix_kv, "seq", by, True)
                prefix_parts.append(((me - by) % devices, part))
    else:
        gathered = lax.all_gather(prefix_kv, "seq", axis=0, tiled=True)
        prefix_parts.append((None, gathered))
        for by in range(1, span + 1):
            suffix_parts.append((by, shifted(suffix_kv, "seq", by, False)))

    position = offset + prefix_len
    q_rot = rotate(queries.reshape(rows, q_heads, HD), position).reshape(rows, kv_heads, repeat, HD)

    key_chunks, value_chunks, visible_chunks = [], [], []
    for holder, kv in prefix_parts:
        count = kv.shape[0]
        if holder is None:
            holder_index = jnp.arange(count, dtype=jnp.int32) // block_rows
            row_group = jnp.take(block_group, holder_index)
            visible = row_group[None, :] == group[:, None]
        else:
            row_group = lax.dynamic_index_in_dim(block_group, holder, keepdims=False)
            visible = jnp.broadcast_to((group == row_group)[:, None], (rows, count))
        key_chunks.append(kv[:, :kv_cols])
        value_chunks.append(kv[:, kv_cols:])
        visible_chunks.append(visible)

    own_k_rot = None
    for back, kv in suffix_parts:
        key_index = (me - back) * rows + jnp.arange(rows, dtype=jnp.int32)
        key_request, key_offset, _ = token_info(key_index, suffix_lengths, request_group)
        k_rot = rotate(kv[:, :kv_cols].reshape(rows, kv_heads, HD), key_offset + prefix_len).reshape(
            rows, kv_cols
        )
        if back == 0:
            own_k_rot = k_rot
        visible = (
            (key_index[None, :] >= 0)
            & (key_request[None, :] == request[:, None])
            & (key_index[None, :] <= index[:, None])
        )
        key_chunks.append(k_rot)
        value_chunks.append(kv[:, kv_cols:])
        visible_chunks.append(visible)

    cache = lax.all_to_all(
        jnp.stack([own_k_rot, suffix_values], axis=0), "tp", split_axis=1, concat_axis=2, tiled=True
    )

    def scores_of(keys, visible):
        keys_split = keys.reshape(keys.shape[0], kv_heads, HD)
        scores = (
            jnp.einsum("bgrd,kgd->bgrk", q_rot, keys_split, preferred_element_type=jnp.float32)
            * scale
        )
        return jnp.where(visible[:, None, None, :], scores, BIG_NEGATIVE)

    def summed_of(scores, high, values, visible):
        weights = jnp.where(visible[:, None, None, :], jnp.exp(scores - high[..., None]), 0.0)
        summed = jnp.einsum(
            "bgrk,kgd->bgrd",
            weights.astype(jnp.bfloat16),
            values.reshape(values.shape[0], kv_heads, HD),
            preferred_element_type=jnp.float32,
        )
        return jnp.sum(weights, axis=-1), summed

    keys = jnp.concatenate(key_chunks, axis=0)
    values = jnp.concatenate(value_chunks, axis=0)
    visible = jnp.concatenate(visible_chunks, axis=1)
    count = keys.shape[0]
    if count * rows * q_heads * 4 <= (8 << 20):
        scores = scores_of(keys, visible)
        high = jnp.max(scores, axis=-1)
        total, summed = summed_of(scores, high, values, visible)
    else:
        width = 512
        steps = count // width
        tail = steps * width
        piece_k = keys[:tail].reshape(steps, width, kv_cols)
        piece_v = values[:tail].reshape(steps, width, kv_cols)
        piece_m = jnp.moveaxis(visible[:, :tail].reshape(rows, steps, width), 1, 0)

        def high_step(high, piece):
            k, m = piece
            return jnp.maximum(high, jnp.max(scores_of(k, m), axis=-1)), None

        high = jnp.max(scores_of(keys[tail:], visible[:, tail:]), axis=-1)
        high, _ = lax.scan(high_step, high, (piece_k, piece_m))

        def sum_step(carry, piece):
            k, v, m = piece
            total, summed = summed_of(scores_of(k, m), high, v, m)
            return (carry[0] + total, carry[1] + summed), None

        start = summed_of(scores_of(keys[tail:], visible[:, tail:]), high, values[tail:], visible[:, tail:])
        (total, summed), _ = lax.scan(sum_step, start, (piece_k, piece_v, piece_m))
    attended = (summed / total[..., None]).reshape(rows, q_heads * HD).astype(jnp.bfloat16)
    return (attended, cache[0], cache[1])


def solution(mesh):
    return jax.shard_map(
        body,
        mesh=mesh,
        in_specs=(
            P("seq", "tp"),
            P("seq", "tp"),
            P("seq", "tp"),
            P("seq", "tp"),
            P("seq", "tp"),
            P(),
            P(),
            P(),
        ),
        out_specs=(P("seq", "tp"), P(("seq", "tp"), None), P(("seq", "tp"), None)),
        check_vma=False,
    )
```

```python
import functools
import math

import jax
import jax.numpy as jnp
from jax import lax
from jax.experimental import pallas as pl
from jax.experimental.pallas import tpu as pltpu
from jax.sharding import PartitionSpec as P

HD = 128
GROUPS = 4


BIG_NEGATIVE = -1e30


def rotate(values, position):
    half = values.shape[-1] // 2
    freq = jnp.exp(
        jnp.arange(half, dtype=jnp.float32) * (-2.0 * math.log(500000.0) / values.shape[-1])
    )
    angle = position.astype(jnp.float32)[:, None] * freq[None, :]
    cosine = jnp.cos(angle)[:, None, :]
    sine = jnp.sin(angle)[:, None, :]
    floats = values.astype(jnp.float32)
    lower = floats[..., :half]
    upper = floats[..., half:]
    return jnp.concatenate(
        [lower * cosine - upper * sine, upper * cosine + lower * sine], axis=-1
    ).astype(jnp.bfloat16)


def attend_kernel(pieces, q_heads, repeat, scale, *refs):
    q_ref, cq_ref, sq_ref, tok_ref, key_ref = refs[:5]
    data = refs[5 : len(refs) - 3]
    out_ref, kscr, vscr = refs[len(refs) - 3 :]
    at = 0
    for k_at, k_row, k_col, v_at, v_row, v_col, count in pieces:
        kscr[at : at + count, :] = data[k_at][k_row : k_row + count, k_col : k_col + kscr.shape[1]]
        vscr[at : at + count, :] = data[v_at][v_row : v_row + count, v_col : v_col + vscr.shape[1]]
        at += count
    tok = tok_ref[...]
    keym = key_ref[...]
    visible = (keym[0:1, :] == tok[:, 1:2]) | (
        (keym[1:2, :] == tok[:, 0:1]) & (keym[2:3, :] <= tok[:, 2:3])
    )
    cq = cq_ref[...]
    sq = sq_ref[...]
    for h in range(q_heads):
        g = h // repeat
        x = q_ref[:, h * HD : (h + 1) * HD].astype(jnp.float32)
        q = (x * cq + pltpu.roll(x, HD // 2, 1) * sq).astype(jnp.bfloat16)
        k = kscr[:, g * HD : (g + 1) * HD]
        scores = lax.dot_general(
            q, k, (((1,), (1,)), ((), ())), preferred_element_type=jnp.float32
        ) * scale
        scores = jnp.where(visible, scores, BIG_NEGATIVE)
        high = jnp.max(scores, axis=1, keepdims=True)
        weights = jnp.where(visible, jnp.exp(scores - high), 0.0)
        total = jnp.sum(weights, axis=1, keepdims=True)
        v = vscr[:, g * HD : (g + 1) * HD]
        summed = jnp.dot(weights.astype(jnp.bfloat16), v, preferred_element_type=jnp.float32)
        out_ref[:, h * HD : (h + 1) * HD] = (summed / total).astype(out_ref.dtype)


def attend(queries, cq, sq, tok, keym, data, pieces, kv_cols, repeat, scale):
    rows = queries.shape[0]
    q_heads = queries.shape[1] // HD
    count = keym.shape[1]
    flops = 4 * rows * count * HD * q_heads
    nbytes = sum(a.size * a.dtype.itemsize for a in [queries, cq, sq, tok, keym, *data])
    return pl.pallas_call(
        functools.partial(attend_kernel, tuple(pieces), q_heads, repeat, scale),
        out_shape=jax.ShapeDtypeStruct(queries.shape, jnp.bfloat16),
        scratch_shapes=[
            pltpu.VMEM((count, kv_cols), jnp.bfloat16),
            pltpu.VMEM((count, kv_cols), jnp.bfloat16),
        ],
        cost_estimate=pl.CostEstimate(
            flops=flops,
            transcendentals=rows * count * q_heads,
            bytes_accessed=nbytes + queries.size * 2,
        ),
    )(queries, cq, sq, tok, keym, *data)


def token_info(index, suffix_lengths, request_group):
    ends = jnp.cumsum(suffix_lengths)
    request = jnp.sum((index[:, None] >= ends[None, :]).astype(jnp.int32), axis=1)
    onehot = request[:, None] == jnp.arange(suffix_lengths.shape[0], dtype=jnp.int32)[None, :]
    first = jnp.sum(jnp.where(onehot, (ends - suffix_lengths)[None, :], 0), axis=1)
    group = jnp.sum(jnp.where(onehot, request_group[None, :], 0), axis=1)
    return (request, index - first, group)


def shifted(array, axis, by, wrap):
    length = lax.axis_size(axis)
    pairs = [(i, (i + by) % length) for i in range(length) if wrap or i + by < length]
    return lax.ppermute(array, axis, pairs)


def body(
    queries,
    suffix_keys,
    suffix_values,
    prefix_keys,
    prefix_values,
    suffix_lengths,
    request_group,
    block_group,
):
    rows = queries.shape[0]
    kv_cols = suffix_keys.shape[1]
    kv_heads = kv_cols // HD
    q_heads = queries.shape[1] // HD
    repeat = q_heads // kv_heads
    devices = lax.axis_size("seq")
    me = lax.axis_index("seq")
    block_rows = prefix_keys.shape[0]
    prefix_len = block_rows * devices // GROUPS
    span = max(1, min(2048 // rows, devices // 8))
    scale = HD ** (-0.5)
    index = me * rows + jnp.arange(rows, dtype=jnp.int32)
    request, offset, group = token_info(index, suffix_lengths, request_group)

    prefix_kv = jnp.concatenate([prefix_keys, prefix_values], axis=1)
    suffix_kv = jnp.concatenate([suffix_keys, suffix_values], axis=1)

    def rotated_keys(raw, back):
        key_index = (me - back) * rows + jnp.arange(rows, dtype=jnp.int32)
        key_request, key_offset, _ = token_info(key_index, suffix_lengths, request_group)
        k_rot = rotate(raw.reshape(rows, kv_heads, HD), key_offset + prefix_len).reshape(rows, kv_cols)
        return key_index, key_request, k_rot

    if devices <= 16:
        own_index, own_request, own_k_rot = rotated_keys(suffix_keys, 0)
        cache = lax.all_to_all(
            jnp.stack([own_k_rot, suffix_values], axis=0), "tp", split_axis=1, concat_axis=2, tiled=True
        )
        data = [prefix_kv]
        pieces = [(0, 0, 0, 0, 0, kv_cols, block_rows)]
        groups = [jnp.broadcast_to(lax.dynamic_index_in_dim(block_group, me, keepdims=False), (block_rows,))]
        tails = []
        for by in range(1, devices):
            if by <= span:
                part = shifted(jnp.concatenate([prefix_kv, suffix_kv], axis=0), "seq", by, True)
                key_index, key_request, k_rot = rotated_keys(part[block_rows:, :kv_cols], by)
                tails.append((len(data), k_rot, key_index, key_request))
            else:
                part = shifted(prefix_kv, "seq", by, True)
            data.append(part)
            pieces.append((len(data) - 1, 0, 0, len(data) - 1, 0, kv_cols, block_rows))
            holder = (me - by) % devices
            groups.append(jnp.broadcast_to(lax.dynamic_index_in_dim(block_group, holder, keepdims=False), (block_rows,)))
        data.append(own_k_rot)
        data.append(suffix_values)
        pieces.append((len(data) - 2, 0, 0, len(data) - 1, 0, 0, rows))
        requests = [jnp.full((block_rows * devices,), -2, jnp.int32), own_request]
        indices = [jnp.zeros((block_rows * devices,), jnp.int32), own_index]
        for at, k_rot, key_index, key_request in tails:
            data.append(k_rot)
            pieces.append((len(data) - 1, 0, 0, at, block_rows, kv_cols, rows))
            requests.append(jnp.where(key_index >= 0, key_request, -2))
            indices.append(key_index)
        suffix_count = rows * (1 + len(tails))
        groups.append(jnp.full((suffix_count,), -1, jnp.int32))
        keym = jnp.stack(
            [jnp.concatenate(groups), jnp.concatenate(requests), jnp.concatenate(indices)], axis=0
        )
        keym = jnp.pad(keym, ((0, 5), (0, 0)))
        tok = jnp.pad(jnp.stack([request, group, index], axis=1), ((0, 0), (0, 125)))
        half = HD // 2
        freq = jnp.exp(
            jnp.arange(half, dtype=jnp.float32) * (-2.0 * math.log(500000.0) / HD)
        )
        angle = (offset + prefix_len).astype(jnp.float32)[:, None] * freq[None, :]
        cosine = jnp.cos(angle)
        sine = jnp.sin(angle)
        cq = jnp.concatenate([cosine, cosine], axis=1)
        sq = jnp.concatenate([-sine, sine], axis=1)
        attended = attend(queries, cq, sq, tok, keym, data, pieces, kv_cols, repeat, scale)
        return (attended, cache[0], cache[1])

    prefix_parts = []
    suffix_parts = [(0, suffix_kv)]
    gathered = lax.all_gather(prefix_kv, "seq", axis=0, tiled=True)
    prefix_parts.append((None, gathered))
    for by in range(1, span + 1):
        suffix_parts.append((by, shifted(suffix_kv, "seq", by, False)))

    position = offset + prefix_len
    q_rot = rotate(queries.reshape(rows, q_heads, HD), position).reshape(rows, kv_heads, repeat, HD)

    key_chunks, value_chunks, visible_chunks = [], [], []
    for holder, kv in prefix_parts:
        count = kv.shape[0]
        if holder is None:
            holder_index = jnp.arange(count, dtype=jnp.int32) // block_rows
            row_group = jnp.take(block_group, holder_index)
            visible = row_group[None, :] == group[:, None]
        else:
            row_group = lax.dynamic_index_in_dim(block_group, holder, keepdims=False)
            visible = jnp.broadcast_to((group == row_group)[:, None], (rows, count))
        key_chunks.append(kv[:, :kv_cols])
        value_chunks.append(kv[:, kv_cols:])
        visible_chunks.append(visible)

    own_k_rot = None
    for back, kv in suffix_parts:
        key_index = (me - back) * rows + jnp.arange(rows, dtype=jnp.int32)
        key_request, key_offset, _ = token_info(key_index, suffix_lengths, request_group)
        k_rot = rotate(kv[:, :kv_cols].reshape(rows, kv_heads, HD), key_offset + prefix_len).reshape(
            rows, kv_cols
        )
        if back == 0:
            own_k_rot = k_rot
        visible = (
            (key_index[None, :] >= 0)
            & (key_request[None, :] == request[:, None])
            & (key_index[None, :] <= index[:, None])
        )
        key_chunks.append(k_rot)
        value_chunks.append(kv[:, kv_cols:])
        visible_chunks.append(visible)

    cache = lax.all_to_all(
        jnp.stack([own_k_rot, suffix_values], axis=0), "tp", split_axis=1, concat_axis=2, tiled=True
    )

    def scores_of(keys, visible):
        keys_split = keys.reshape(keys.shape[0], kv_heads, HD)
        scores = (
            jnp.einsum("bgrd,kgd->bgrk", q_rot, keys_split, preferred_element_type=jnp.float32)
            * scale
        )
        return jnp.where(visible[:, None, None, :], scores, BIG_NEGATIVE)

    def summed_of(scores, high, values, visible):
        weights = jnp.where(visible[:, None, None, :], jnp.exp(scores - high[..., None]), 0.0)
        summed = jnp.einsum(
            "bgrk,kgd->bgrd",
            weights.astype(jnp.bfloat16),
            values.reshape(values.shape[0], kv_heads, HD),
            preferred_element_type=jnp.float32,
        )
        return jnp.sum(weights, axis=-1), summed

    keys = jnp.concatenate(key_chunks, axis=0)
    values = jnp.concatenate(value_chunks, axis=0)
    visible = jnp.concatenate(visible_chunks, axis=1)
    count = keys.shape[0]
    if count * rows * q_heads * 4 <= (8 << 20):
        scores = scores_of(keys, visible)
        high = jnp.max(scores, axis=-1)
        total, summed = summed_of(scores, high, values, visible)
    else:
        width = 512
        steps = count // width
        tail = steps * width
        piece_k = keys[:tail].reshape(steps, width, kv_cols)
        piece_v = values[:tail].reshape(steps, width, kv_cols)
        piece_m = jnp.moveaxis(visible[:, :tail].reshape(rows, steps, width), 1, 0)

        def high_step(high, piece):
            k, m = piece
            return jnp.maximum(high, jnp.max(scores_of(k, m), axis=-1)), None

        high = jnp.max(scores_of(keys[tail:], visible[:, tail:]), axis=-1)
        high, _ = lax.scan(high_step, high, (piece_k, piece_m))

        def sum_step(carry, piece):
            k, v, m = piece
            total, summed = summed_of(scores_of(k, m), high, v, m)
            return (carry[0] + total, carry[1] + summed), None

        start = summed_of(scores_of(keys[tail:], visible[:, tail:]), high, values[tail:], visible[:, tail:])
        (total, summed), _ = lax.scan(sum_step, start, (piece_k, piece_v, piece_m))
    attended = (summed / total[..., None]).reshape(rows, q_heads * HD).astype(jnp.bfloat16)
    return (attended, cache[0], cache[1])


def solution(mesh):
    return jax.shard_map(
        body,
        mesh=mesh,
        in_specs=(
            P("seq", "tp"),
            P("seq", "tp"),
            P("seq", "tp"),
            P("seq", "tp"),
            P("seq", "tp"),
            P(),
            P(),
            P(),
        ),
        out_specs=(P("seq", "tp"), P(("seq", "tp"), None), P(("seq", "tp"), None)),
        check_vma=False,
    )
```

```python
import functools
import math

import jax
import jax.numpy as jnp
from jax import lax
from jax.experimental import pallas as pl
from jax.experimental.pallas import tpu as pltpu
from jax.sharding import PartitionSpec as P

HD = 128
GROUPS = 4


BIG_NEGATIVE = -1e30


def rotate(values, position):
    half = values.shape[-1] // 2
    freq = jnp.exp(
        jnp.arange(half, dtype=jnp.float32) * (-2.0 * math.log(500000.0) / values.shape[-1])
    )
    angle = position.astype(jnp.float32)[:, None] * freq[None, :]
    cosine = jnp.cos(angle)[:, None, :]
    sine = jnp.sin(angle)[:, None, :]
    floats = values.astype(jnp.float32)
    lower = floats[..., :half]
    upper = floats[..., half:]
    return jnp.concatenate(
        [lower * cosine - upper * sine, upper * cosine + lower * sine], axis=-1
    ).astype(jnp.bfloat16)


def attend_kernel(meta, *refs):
    devices, block_rows, rows, tails, prefix_len, repeat, scale = meta
    me_ref, lens_ref, rg_ref, bg_ref, freq_ref, q_ref, own_k_ref, own_v_ref = refs[:8]
    data = refs[8 : 8 + devices]
    out_ref, kscr, vscr = refs[8 + devices :]
    kv_cols = kscr.shape[1]
    count = kscr.shape[0]
    base = devices * block_rows
    q_heads = q_ref.shape[1] // HD
    me = me_ref[0]
    starts, at = [], 0
    for j in range(lens_ref.shape[0]):
        starts.append(at)
        at = at + lens_ref[j]

    def info(index):
        request = jnp.full(index.shape, -2, jnp.int32)
        first = jnp.zeros(index.shape, jnp.int32)
        group = jnp.full(index.shape, -1, jnp.int32)
        for j, start in enumerate(starts):
            after = index >= start
            request = jnp.where(after, j, request)
            first = jnp.where(after, start, first)
            group = jnp.where(after, rg_ref[j], group)
        return request, index - first, group

    freq = freq_ref[...]
    lane = lax.broadcasted_iota(jnp.int32, (1, HD), 1)
    sign = jnp.where(lane < HD // 2, -1.0, 1.0).astype(jnp.float32)

    def tables(offset):
        angle = (offset + prefix_len).astype(jnp.float32) * freq
        return jnp.cos(angle), jnp.sin(angle) * sign

    def rotated(x, cosine, sine):
        return (x * cosine + pltpu.roll(x, HD // 2, 1) * sine).astype(jnp.bfloat16)

    for c in range(devices):
        kscr[c * block_rows : (c + 1) * block_rows, :] = data[c][0:block_rows, 0:kv_cols]
        vscr[c * block_rows : (c + 1) * block_rows, :] = data[c][0:block_rows, kv_cols : 2 * kv_cols]
    kscr[base : base + rows, :] = own_k_ref[...]
    vscr[base : base + rows, :] = own_v_ref[...]
    for b in range(1, tails + 1):
        low = base + b * rows
        index = (me - b) * rows + lax.broadcasted_iota(jnp.int32, (rows, 1), 0)
        _, offset, _ = info(index)
        cosine, sine = tables(offset)
        for g in range(kv_cols // HD):
            x = data[b][block_rows : block_rows + rows, g * HD : (g + 1) * HD].astype(jnp.float32)
            kscr[low : low + rows, g * HD : (g + 1) * HD] = rotated(x, cosine, sine)
        vscr[low : low + rows, :] = data[b][block_rows : block_rows + rows, kv_cols : 2 * kv_cols]

    token = me * rows + lax.broadcasted_iota(jnp.int32, (rows, 1), 0)
    request, offset, group = info(token)
    col = lax.broadcasted_iota(jnp.int32, (1, count), 1)
    key_group = jnp.full((1, count), -1, jnp.int32)
    for c in range(devices):
        holder = lax.rem(me - c + devices, devices)
        key_group = jnp.where(col >= c * block_rows, bg_ref[holder], key_group)
    key_index = jnp.full((1, count), -1, jnp.int32)
    for b in range(tails + 1):
        low = base + b * rows
        key_index = jnp.where(col >= low, (me - b) * rows + col - low, key_index)
    key_request, _, _ = info(key_index)
    visible = ((col < base) & (key_group == group)) | (
        (key_request == request) & (key_index <= token)
    )
    cosine, sine = tables(offset)
    for h in range(q_heads):
        g = h // repeat
        q = rotated(q_ref[:, h * HD : (h + 1) * HD].astype(jnp.float32), cosine, sine)
        k = kscr[:, g * HD : (g + 1) * HD]
        scores = lax.dot_general(
            q, k, (((1,), (1,)), ((), ())), preferred_element_type=jnp.float32
        ) * scale
        scores = jnp.where(visible, scores, BIG_NEGATIVE)
        high = jnp.max(scores, axis=1, keepdims=True)
        weights = jnp.where(visible, jnp.exp(scores - high), 0.0)
        total = jnp.sum(weights, axis=1, keepdims=True)
        v = vscr[:, g * HD : (g + 1) * HD]
        summed = jnp.dot(weights.astype(jnp.bfloat16), v, preferred_element_type=jnp.float32)
        out_ref[:, h * HD : (h + 1) * HD] = (summed / total).astype(out_ref.dtype)


def attend(meta, scalars, freq, queries, own_k, own_v, data):
    devices, block_rows, rows, tails = meta[:4]
    kv_cols = own_k.shape[1]
    q_heads = queries.shape[1] // HD
    count = devices * block_rows + rows * (1 + tails)
    flops = 4 * rows * count * HD * q_heads
    arrays = [queries, own_k, own_v, *data]
    nbytes = sum(a.size * a.dtype.itemsize for a in arrays)
    smem = pl.BlockSpec(memory_space=pltpu.SMEM)
    vmem = pl.BlockSpec(memory_space=pltpu.VMEM)
    return pl.pallas_call(
        functools.partial(attend_kernel, meta),
        out_shape=jax.ShapeDtypeStruct(queries.shape, jnp.bfloat16),
        in_specs=[smem] * len(scalars) + [vmem] * (1 + len(arrays)),
        out_specs=vmem,
        scratch_shapes=[
            pltpu.VMEM((count, kv_cols), jnp.bfloat16),
            pltpu.VMEM((count, kv_cols), jnp.bfloat16),
        ],
        cost_estimate=pl.CostEstimate(
            flops=flops,
            transcendentals=rows * count * q_heads,
            bytes_accessed=nbytes + queries.size * 2,
        ),
    )(*scalars, freq, *arrays)


def token_info(index, suffix_lengths, request_group):
    ends = jnp.cumsum(suffix_lengths)
    request = jnp.sum((index[:, None] >= ends[None, :]).astype(jnp.int32), axis=1)
    onehot = request[:, None] == jnp.arange(suffix_lengths.shape[0], dtype=jnp.int32)[None, :]
    first = jnp.sum(jnp.where(onehot, (ends - suffix_lengths)[None, :], 0), axis=1)
    group = jnp.sum(jnp.where(onehot, request_group[None, :], 0), axis=1)
    return (request, index - first, group)


def shifted(array, axis, by, wrap):
    length = lax.axis_size(axis)
    pairs = [(i, (i + by) % length) for i in range(length) if wrap or i + by < length]
    return lax.ppermute(array, axis, pairs)


def body(
    queries,
    suffix_keys,
    suffix_values,
    prefix_keys,
    prefix_values,
    suffix_lengths,
    request_group,
    block_group,
):
    rows = queries.shape[0]
    kv_cols = suffix_keys.shape[1]
    kv_heads = kv_cols // HD
    q_heads = queries.shape[1] // HD
    repeat = q_heads // kv_heads
    devices = lax.axis_size("seq")
    me = lax.axis_index("seq")
    block_rows = prefix_keys.shape[0]
    prefix_len = block_rows * devices // GROUPS
    span = max(1, min(2048 // rows, devices // 8))
    scale = HD ** (-0.5)
    index = me * rows + jnp.arange(rows, dtype=jnp.int32)
    request, offset, group = token_info(index, suffix_lengths, request_group)

    prefix_kv = jnp.concatenate([prefix_keys, prefix_values], axis=1)
    suffix_kv = jnp.concatenate([suffix_keys, suffix_values], axis=1)

    def rotated_keys(raw, back):
        key_index = (me - back) * rows + jnp.arange(rows, dtype=jnp.int32)
        key_request, key_offset, _ = token_info(key_index, suffix_lengths, request_group)
        k_rot = rotate(raw.reshape(rows, kv_heads, HD), key_offset + prefix_len).reshape(rows, kv_cols)
        return key_index, key_request, k_rot

    if devices <= 16:
        _, own_offset, _ = token_info(index, suffix_lengths, request_group)
        own_k_rot = rotate(suffix_keys.reshape(rows, kv_heads, HD), own_offset + prefix_len).reshape(
            rows, kv_cols
        )
        cache = lax.all_to_all(
            jnp.stack([own_k_rot, suffix_values], axis=0), "tp", split_axis=1, concat_axis=2, tiled=True
        )
        data = [prefix_kv]
        for by in range(1, devices):
            if by <= span:
                data.append(shifted(jnp.concatenate([prefix_kv, suffix_kv], axis=0), "seq", by, True))
            else:
                data.append(shifted(prefix_kv, "seq", by, True))
        half = HD // 2
        freq = jnp.exp(jnp.arange(half, dtype=jnp.float32) * (-2.0 * math.log(500000.0) / HD))
        freq = jnp.concatenate([freq, freq])[None, :]
        scalars = [me.astype(jnp.int32).reshape(1), suffix_lengths, request_group, block_group]
        meta = (devices, block_rows, rows, min(span, devices - 1), prefix_len, repeat, scale)
        attended = attend(meta, scalars, freq, queries, own_k_rot, suffix_values, data)
        return (attended, cache[0], cache[1])

    prefix_parts = []
    suffix_parts = [(0, suffix_kv)]
    gathered = lax.all_gather(prefix_kv, "seq", axis=0, tiled=True)
    prefix_parts.append((None, gathered))
    for by in range(1, span + 1):
        suffix_parts.append((by, shifted(suffix_kv, "seq", by, False)))

    position = offset + prefix_len
    q_rot = rotate(queries.reshape(rows, q_heads, HD), position).reshape(rows, kv_heads, repeat, HD)

    key_chunks, value_chunks, visible_chunks = [], [], []
    for holder, kv in prefix_parts:
        count = kv.shape[0]
        if holder is None:
            holder_index = jnp.arange(count, dtype=jnp.int32) // block_rows
            row_group = jnp.take(block_group, holder_index)
            visible = row_group[None, :] == group[:, None]
        else:
            row_group = lax.dynamic_index_in_dim(block_group, holder, keepdims=False)
            visible = jnp.broadcast_to((group == row_group)[:, None], (rows, count))
        key_chunks.append(kv[:, :kv_cols])
        value_chunks.append(kv[:, kv_cols:])
        visible_chunks.append(visible)

    own_k_rot = None
    for back, kv in suffix_parts:
        key_index = (me - back) * rows + jnp.arange(rows, dtype=jnp.int32)
        key_request, key_offset, _ = token_info(key_index, suffix_lengths, request_group)
        k_rot = rotate(kv[:, :kv_cols].reshape(rows, kv_heads, HD), key_offset + prefix_len).reshape(
            rows, kv_cols
        )
        if back == 0:
            own_k_rot = k_rot
        visible = (
            (key_index[None, :] >= 0)
            & (key_request[None, :] == request[:, None])
            & (key_index[None, :] <= index[:, None])
        )
        key_chunks.append(k_rot)
        value_chunks.append(kv[:, kv_cols:])
        visible_chunks.append(visible)

    cache = lax.all_to_all(
        jnp.stack([own_k_rot, suffix_values], axis=0), "tp", split_axis=1, concat_axis=2, tiled=True
    )

    def scores_of(keys, visible):
        keys_split = keys.reshape(keys.shape[0], kv_heads, HD)
        scores = (
            jnp.einsum("bgrd,kgd->bgrk", q_rot, keys_split, preferred_element_type=jnp.float32)
            * scale
        )
        return jnp.where(visible[:, None, None, :], scores, BIG_NEGATIVE)

    def summed_of(scores, high, values, visible):
        weights = jnp.where(visible[:, None, None, :], jnp.exp(scores - high[..., None]), 0.0)
        summed = jnp.einsum(
            "bgrk,kgd->bgrd",
            weights.astype(jnp.bfloat16),
            values.reshape(values.shape[0], kv_heads, HD),
            preferred_element_type=jnp.float32,
        )
        return jnp.sum(weights, axis=-1), summed

    keys = jnp.concatenate(key_chunks, axis=0)
    values = jnp.concatenate(value_chunks, axis=0)
    visible = jnp.concatenate(visible_chunks, axis=1)
    count = keys.shape[0]
    if count * rows * q_heads * 4 <= (8 << 20):
        scores = scores_of(keys, visible)
        high = jnp.max(scores, axis=-1)
        total, summed = summed_of(scores, high, values, visible)
    else:
        width = 512
        steps = count // width
        tail = steps * width
        piece_k = keys[:tail].reshape(steps, width, kv_cols)
        piece_v = values[:tail].reshape(steps, width, kv_cols)
        piece_m = jnp.moveaxis(visible[:, :tail].reshape(rows, steps, width), 1, 0)

        def high_step(high, piece):
            k, m = piece
            return jnp.maximum(high, jnp.max(scores_of(k, m), axis=-1)), None

        high = jnp.max(scores_of(keys[tail:], visible[:, tail:]), axis=-1)
        high, _ = lax.scan(high_step, high, (piece_k, piece_m))

        def sum_step(carry, piece):
            k, v, m = piece
            total, summed = summed_of(scores_of(k, m), high, v, m)
            return (carry[0] + total, carry[1] + summed), None

        start = summed_of(scores_of(keys[tail:], visible[:, tail:]), high, values[tail:], visible[:, tail:])
        (total, summed), _ = lax.scan(sum_step, start, (piece_k, piece_v, piece_m))
    attended = (summed / total[..., None]).reshape(rows, q_heads * HD).astype(jnp.bfloat16)
    return (attended, cache[0], cache[1])


def solution(mesh):
    return jax.shard_map(
        body,
        mesh=mesh,
        in_specs=(
            P("seq", "tp"),
            P("seq", "tp"),
            P("seq", "tp"),
            P("seq", "tp"),
            P("seq", "tp"),
            P(),
            P(),
            P(),
        ),
        out_specs=(P("seq", "tp"), P(("seq", "tp"), None), P(("seq", "tp"), None)),
        check_vma=False,
    )
```

```python
import functools
import math

import jax
import jax.numpy as jnp
from jax import lax
from jax.experimental import pallas as pl
from jax.experimental.pallas import tpu as pltpu
from jax.sharding import PartitionSpec as P

HD = 128
GROUPS = 4


BIG_NEGATIVE = -1e30


def rotate(values, position):
    half = values.shape[-1] // 2
    freq = jnp.exp(
        jnp.arange(half, dtype=jnp.float32) * (-2.0 * math.log(500000.0) / values.shape[-1])
    )
    angle = position.astype(jnp.float32)[:, None] * freq[None, :]
    cosine = jnp.cos(angle)[:, None, :]
    sine = jnp.sin(angle)[:, None, :]
    floats = values.astype(jnp.float32)
    lower = floats[..., :half]
    upper = floats[..., half:]
    return jnp.concatenate(
        [lower * cosine - upper * sine, upper * cosine + lower * sine], axis=-1
    ).astype(jnp.bfloat16)


def attend_kernel(meta, *refs):
    devices, block_rows, rows, tails, prefix_len, repeat, scale = meta
    me_ref, lens_ref, rg_ref, bg_ref, freq_ref, q_ref, own_k_ref, own_v_ref = refs[:8]
    data = refs[8 : 8 + devices]
    out_ref, kscr, vscr = refs[8 + devices :]
    kv_cols = kscr.shape[1]
    count = kscr.shape[0]
    base = devices * block_rows
    q_heads = q_ref.shape[1] // HD
    me = me_ref[0]
    starts, at = [], 0
    for j in range(lens_ref.shape[0]):
        starts.append(at)
        at = at + lens_ref[j]

    def info(index):
        request = jnp.full(index.shape, -2, jnp.int32)
        first = jnp.zeros(index.shape, jnp.int32)
        group = jnp.full(index.shape, -1, jnp.int32)
        for j, start in enumerate(starts):
            after = index >= start
            request = jnp.where(after, j, request)
            first = jnp.where(after, start, first)
            group = jnp.where(after, rg_ref[j], group)
        return request, index - first, group

    freq = freq_ref[...]
    lane = lax.broadcasted_iota(jnp.int32, (1, HD), 1)
    sign = jnp.where(lane < HD // 2, -1.0, 1.0).astype(jnp.float32)

    def tables(offset):
        angle = (offset + prefix_len).astype(jnp.float32) * freq
        return jnp.cos(angle), jnp.sin(angle) * sign

    def rotated(x, cosine, sine):
        return (x * cosine + pltpu.roll(x, HD // 2, 1) * sine).astype(jnp.bfloat16)

    for c in range(devices):
        kscr[c * block_rows : (c + 1) * block_rows, :] = data[c][0:block_rows, 0:kv_cols]
        vscr[c * block_rows : (c + 1) * block_rows, :] = data[c][0:block_rows, kv_cols : 2 * kv_cols]
    kscr[base : base + rows, :] = own_k_ref[...]
    vscr[base : base + rows, :] = own_v_ref[...]
    for b in range(1, tails + 1):
        low = base + b * rows
        index = (me - b) * rows + lax.broadcasted_iota(jnp.int32, (rows, 1), 0)
        _, offset, _ = info(index)
        cosine, sine = tables(offset)
        for g in range(kv_cols // HD):
            x = data[b][block_rows : block_rows + rows, g * HD : (g + 1) * HD].astype(jnp.float32)
            kscr[low : low + rows, g * HD : (g + 1) * HD] = rotated(x, cosine, sine)
        vscr[low : low + rows, :] = data[b][block_rows : block_rows + rows, kv_cols : 2 * kv_cols]

    token = me * rows + lax.broadcasted_iota(jnp.int32, (rows, 1), 0)
    request, offset, group = info(token)
    col = lax.broadcasted_iota(jnp.int32, (1, count), 1)
    key_group = jnp.full((1, count), -1, jnp.int32)
    for c in range(devices):
        holder = lax.rem(me - c + devices, devices)
        key_group = jnp.where(col >= c * block_rows, bg_ref[holder], key_group)
    key_index = jnp.full((1, count), -1, jnp.int32)
    for b in range(tails + 1):
        low = base + b * rows
        key_index = jnp.where(col >= low, (me - b) * rows + col - low, key_index)
    key_request, _, _ = info(key_index)
    visible = ((col < base) & (key_group == group)) | (
        (key_request == request) & (key_index <= token)
    )
    cosine, sine = tables(offset)
    for h in range(q_heads):
        g = h // repeat
        q = rotated(q_ref[:, h * HD : (h + 1) * HD].astype(jnp.float32), cosine, sine)
        k = kscr[:, g * HD : (g + 1) * HD]
        scores = lax.dot_general(
            q, k, (((1,), (1,)), ((), ())), preferred_element_type=jnp.float32
        ) * scale
        scores = jnp.where(visible, scores, BIG_NEGATIVE)
        high = jnp.max(scores, axis=1, keepdims=True)
        weights = jnp.where(visible, jnp.exp(scores - high), 0.0)
        total = jnp.sum(weights, axis=1, keepdims=True)
        v = vscr[:, g * HD : (g + 1) * HD]
        summed = jnp.dot(weights.astype(jnp.bfloat16), v, preferred_element_type=jnp.float32)
        out_ref[:, h * HD : (h + 1) * HD] = (summed / total).astype(out_ref.dtype)


def attend(meta, scalars, freq, queries, own_k, own_v, data):
    devices, block_rows, rows, tails = meta[:4]
    kv_cols = own_k.shape[1]
    q_heads = queries.shape[1] // HD
    count = devices * block_rows + rows * (1 + tails)
    flops = 4 * rows * count * HD * q_heads
    arrays = [queries, own_k, own_v, *data]
    nbytes = sum(a.size * a.dtype.itemsize for a in arrays)
    smem = pl.BlockSpec(memory_space=pltpu.SMEM)
    vmem = pl.BlockSpec(memory_space=pltpu.VMEM)
    return pl.pallas_call(
        functools.partial(attend_kernel, meta),
        out_shape=jax.ShapeDtypeStruct(queries.shape, jnp.bfloat16),
        in_specs=[smem] * len(scalars) + [vmem] * (1 + len(arrays)),
        out_specs=vmem,
        scratch_shapes=[
            pltpu.VMEM((count, kv_cols), jnp.bfloat16),
            pltpu.VMEM((count, kv_cols), jnp.bfloat16),
        ],
        cost_estimate=pl.CostEstimate(
            flops=flops,
            transcendentals=rows * count * q_heads,
            bytes_accessed=nbytes + queries.size * 2,
        ),
    )(*scalars, freq, *arrays)


def token_info(index, suffix_lengths, request_group):
    ends = jnp.cumsum(suffix_lengths)
    request = jnp.sum((index[:, None] >= ends[None, :]).astype(jnp.int32), axis=1)
    onehot = request[:, None] == jnp.arange(suffix_lengths.shape[0], dtype=jnp.int32)[None, :]
    first = jnp.sum(jnp.where(onehot, (ends - suffix_lengths)[None, :], 0), axis=1)
    group = jnp.sum(jnp.where(onehot, request_group[None, :], 0), axis=1)
    return (request, index - first, group)


def shifted(array, axis, by, wrap):
    length = lax.axis_size(axis)
    pairs = [(i, (i + by) % length) for i in range(length) if wrap or i + by < length]
    return lax.ppermute(array, axis, pairs)


def body(
    queries,
    suffix_keys,
    suffix_values,
    prefix_keys,
    prefix_values,
    suffix_lengths,
    request_group,
    block_group,
):
    rows = queries.shape[0]
    kv_cols = suffix_keys.shape[1]
    kv_heads = kv_cols // HD
    q_heads = queries.shape[1] // HD
    repeat = q_heads // kv_heads
    devices = lax.axis_size("seq")
    me = lax.axis_index("seq")
    block_rows = prefix_keys.shape[0]
    prefix_len = block_rows * devices // GROUPS
    span = max(1, min(2048 // rows, devices // 8))
    scale = HD ** (-0.5)
    index = me * rows + jnp.arange(rows, dtype=jnp.int32)
    request, offset, group = token_info(index, suffix_lengths, request_group)

    prefix_kv = jnp.concatenate([prefix_keys, prefix_values], axis=1)
    suffix_kv = jnp.concatenate([suffix_keys, suffix_values], axis=1)

    def rotated_keys(raw, back):
        key_index = (me - back) * rows + jnp.arange(rows, dtype=jnp.int32)
        key_request, key_offset, _ = token_info(key_index, suffix_lengths, request_group)
        k_rot = rotate(raw.reshape(rows, kv_heads, HD), key_offset + prefix_len).reshape(rows, kv_cols)
        return key_index, key_request, k_rot

    if devices <= 16:
        _, own_offset, _ = token_info(index, suffix_lengths, request_group)
        own_k_rot = rotate(suffix_keys.reshape(rows, kv_heads, HD), own_offset + prefix_len).reshape(
            rows, kv_cols
        )
        cache = lax.all_to_all(
            jnp.stack([own_k_rot, suffix_values], axis=0), "tp", split_axis=1, concat_axis=2, tiled=True
        )
        received = {}
        late = list(range(span + 1, devices))[: max(0, devices - 1 - 5)]
        for by in range(1, devices):
            if by <= span:
                received[by] = shifted(jnp.concatenate([prefix_kv, suffix_kv], axis=0), "seq", by, True)
            elif by not in late:
                received[by] = shifted(prefix_kv, "seq", by, True)
        for i, by in enumerate(late):
            gate = received[devices - 1 - i]
            gate, payload = lax.optimization_barrier((gate, prefix_kv))
            received[devices - 1 - i] = gate
            received[by] = shifted(payload, "seq", by, True)
        data = [prefix_kv] + [received[by] for by in range(1, devices)]
        half = HD // 2
        freq = jnp.exp(jnp.arange(half, dtype=jnp.float32) * (-2.0 * math.log(500000.0) / HD))
        freq = jnp.concatenate([freq, freq])[None, :]
        scalars = [me.astype(jnp.int32).reshape(1), suffix_lengths, request_group, block_group]
        meta = (devices, block_rows, rows, min(span, devices - 1), prefix_len, repeat, scale)
        attended = attend(meta, scalars, freq, queries, own_k_rot, suffix_values, data)
        return (attended, cache[0], cache[1])

    prefix_parts = []
    suffix_parts = [(0, suffix_kv)]
    gathered = lax.all_gather(prefix_kv, "seq", axis=0, tiled=True)
    prefix_parts.append((None, gathered))
    for by in range(1, span + 1):
        suffix_parts.append((by, shifted(suffix_kv, "seq", by, False)))

    position = offset + prefix_len
    q_rot = rotate(queries.reshape(rows, q_heads, HD), position).reshape(rows, kv_heads, repeat, HD)

    key_chunks, value_chunks, visible_chunks = [], [], []
    for holder, kv in prefix_parts:
        count = kv.shape[0]
        if holder is None:
            holder_index = jnp.arange(count, dtype=jnp.int32) // block_rows
            row_group = jnp.take(block_group, holder_index)
            visible = row_group[None, :] == group[:, None]
        else:
            row_group = lax.dynamic_index_in_dim(block_group, holder, keepdims=False)
            visible = jnp.broadcast_to((group == row_group)[:, None], (rows, count))
        key_chunks.append(kv[:, :kv_cols])
        value_chunks.append(kv[:, kv_cols:])
        visible_chunks.append(visible)

    own_k_rot = None
    for back, kv in suffix_parts:
        key_index = (me - back) * rows + jnp.arange(rows, dtype=jnp.int32)
        key_request, key_offset, _ = token_info(key_index, suffix_lengths, request_group)
        k_rot = rotate(kv[:, :kv_cols].reshape(rows, kv_heads, HD), key_offset + prefix_len).reshape(
            rows, kv_cols
        )
        if back == 0:
            own_k_rot = k_rot
        visible = (
            (key_index[None, :] >= 0)
            & (key_request[None, :] == request[:, None])
            & (key_index[None, :] <= index[:, None])
        )
        key_chunks.append(k_rot)
        value_chunks.append(kv[:, kv_cols:])
        visible_chunks.append(visible)

    cache = lax.all_to_all(
        jnp.stack([own_k_rot, suffix_values], axis=0), "tp", split_axis=1, concat_axis=2, tiled=True
    )

    def scores_of(keys, visible):
        keys_split = keys.reshape(keys.shape[0], kv_heads, HD)
        scores = (
            jnp.einsum("bgrd,kgd->bgrk", q_rot, keys_split, preferred_element_type=jnp.float32)
            * scale
        )
        return jnp.where(visible[:, None, None, :], scores, BIG_NEGATIVE)

    def summed_of(scores, high, values, visible):
        weights = jnp.where(visible[:, None, None, :], jnp.exp(scores - high[..., None]), 0.0)
        summed = jnp.einsum(
            "bgrk,kgd->bgrd",
            weights.astype(jnp.bfloat16),
            values.reshape(values.shape[0], kv_heads, HD),
            preferred_element_type=jnp.float32,
        )
        return jnp.sum(weights, axis=-1), summed

    keys = jnp.concatenate(key_chunks, axis=0)
    values = jnp.concatenate(value_chunks, axis=0)
    visible = jnp.concatenate(visible_chunks, axis=1)
    count = keys.shape[0]
    if count * rows * q_heads * 4 <= (8 << 20):
        scores = scores_of(keys, visible)
        high = jnp.max(scores, axis=-1)
        total, summed = summed_of(scores, high, values, visible)
    else:
        width = 512
        steps = count // width
        tail = steps * width
        piece_k = keys[:tail].reshape(steps, width, kv_cols)
        piece_v = values[:tail].reshape(steps, width, kv_cols)
        piece_m = jnp.moveaxis(visible[:, :tail].reshape(rows, steps, width), 1, 0)

        def high_step(high, piece):
            k, m = piece
            return jnp.maximum(high, jnp.max(scores_of(k, m), axis=-1)), None

        high = jnp.max(scores_of(keys[tail:], visible[:, tail:]), axis=-1)
        high, _ = lax.scan(high_step, high, (piece_k, piece_m))

        def sum_step(carry, piece):
            k, v, m = piece
            total, summed = summed_of(scores_of(k, m), high, v, m)
            return (carry[0] + total, carry[1] + summed), None

        start = summed_of(scores_of(keys[tail:], visible[:, tail:]), high, values[tail:], visible[:, tail:])
        (total, summed), _ = lax.scan(sum_step, start, (piece_k, piece_v, piece_m))
    attended = (summed / total[..., None]).reshape(rows, q_heads * HD).astype(jnp.bfloat16)
    return (attended, cache[0], cache[1])


def solution(mesh):
    return jax.shard_map(
        body,
        mesh=mesh,
        in_specs=(
            P("seq", "tp"),
            P("seq", "tp"),
            P("seq", "tp"),
            P("seq", "tp"),
            P("seq", "tp"),
            P(),
            P(),
            P(),
        ),
        out_specs=(P("seq", "tp"), P(("seq", "tp"), None), P(("seq", "tp"), None)),
        check_vma=False,
    )
```

```python
import functools
import math

import jax
import jax.numpy as jnp
from jax import lax
from jax.experimental import pallas as pl
from jax.experimental.pallas import tpu as pltpu
from jax.sharding import PartitionSpec as P

HD = 128
GROUPS = 4


BIG_NEGATIVE = -1e30


def rotate(values, position):
    half = values.shape[-1] // 2
    freq = jnp.exp(
        jnp.arange(half, dtype=jnp.float32) * (-2.0 * math.log(500000.0) / values.shape[-1])
    )
    angle = position.astype(jnp.float32)[:, None] * freq[None, :]
    cosine = jnp.cos(angle)[:, None, :]
    sine = jnp.sin(angle)[:, None, :]
    floats = values.astype(jnp.float32)
    lower = floats[..., :half]
    upper = floats[..., half:]
    return jnp.concatenate(
        [lower * cosine - upper * sine, upper * cosine + lower * sine], axis=-1
    ).astype(jnp.bfloat16)


def attend_kernel(meta, *refs):
    devices, block_rows, rows, tails, prefix_len, repeat, scale = meta
    me_ref, lens_ref, rg_ref, bg_ref, freq_ref, q_ref, own_k_ref, own_v_ref = refs[:8]
    data = refs[8 : 8 + devices]
    out_ref, kscr, vscr = refs[8 + devices :]
    kv_cols = kscr.shape[1]
    count = kscr.shape[0]
    base = devices * block_rows
    q_heads = q_ref.shape[1] // HD
    me = me_ref[0]
    starts, at = [], 0
    for j in range(lens_ref.shape[0]):
        starts.append(at)
        at = at + lens_ref[j]

    def info(index):
        request = jnp.full(index.shape, -2, jnp.int32)
        first = jnp.zeros(index.shape, jnp.int32)
        group = jnp.full(index.shape, -1, jnp.int32)
        for j, start in enumerate(starts):
            after = index >= start
            request = jnp.where(after, j, request)
            first = jnp.where(after, start, first)
            group = jnp.where(after, rg_ref[j], group)
        return request, index - first, group

    freq = freq_ref[...]
    lane = lax.broadcasted_iota(jnp.int32, (1, HD), 1)
    sign = jnp.where(lane < HD // 2, -1.0, 1.0).astype(jnp.float32)

    def tables(offset):
        angle = (offset + prefix_len).astype(jnp.float32) * freq
        return jnp.cos(angle), jnp.sin(angle) * sign

    def rotated(x, cosine, sine):
        return (x * cosine + pltpu.roll(x, HD // 2, 1) * sine).astype(jnp.bfloat16)

    for c in range(devices):
        kscr[c * block_rows : (c + 1) * block_rows, :] = data[c][0:block_rows, 0:kv_cols]
        vscr[c * block_rows : (c + 1) * block_rows, :] = data[c][0:block_rows, kv_cols : 2 * kv_cols]
    kscr[base : base + rows, :] = own_k_ref[...]
    vscr[base : base + rows, :] = own_v_ref[...]
    for b in range(1, tails + 1):
        low = base + b * rows
        index = (me - b) * rows + lax.broadcasted_iota(jnp.int32, (rows, 1), 0)
        _, offset, _ = info(index)
        cosine, sine = tables(offset)
        for g in range(kv_cols // HD):
            x = data[b][block_rows : block_rows + rows, g * HD : (g + 1) * HD].astype(jnp.float32)
            kscr[low : low + rows, g * HD : (g + 1) * HD] = rotated(x, cosine, sine)
        vscr[low : low + rows, :] = data[b][block_rows : block_rows + rows, kv_cols : 2 * kv_cols]

    token = me * rows + lax.broadcasted_iota(jnp.int32, (rows, 1), 0)
    request, offset, group = info(token)
    col = lax.broadcasted_iota(jnp.int32, (1, count), 1)
    key_group = jnp.full((1, count), -1, jnp.int32)
    for c in range(devices):
        holder = lax.rem(me - c + devices, devices)
        key_group = jnp.where(col >= c * block_rows, bg_ref[holder], key_group)
    key_index = jnp.full((1, count), -1, jnp.int32)
    for b in range(tails + 1):
        low = base + b * rows
        key_index = jnp.where(col >= low, (me - b) * rows + col - low, key_index)
    key_request, _, _ = info(key_index)
    visible = ((col < base) & (key_group == group)) | (
        (key_request == request) & (key_index <= token)
    )
    cosine, sine = tables(offset)
    for h in range(q_heads):
        g = h // repeat
        q = rotated(q_ref[:, h * HD : (h + 1) * HD].astype(jnp.float32), cosine, sine)
        k = kscr[:, g * HD : (g + 1) * HD]
        scores = lax.dot_general(
            q, k, (((1,), (1,)), ((), ())), preferred_element_type=jnp.float32
        ) * scale
        scores = jnp.where(visible, scores, BIG_NEGATIVE)
        high = jnp.max(scores, axis=1, keepdims=True)
        weights = jnp.where(visible, jnp.exp(scores - high), 0.0)
        total = jnp.sum(weights, axis=1, keepdims=True)
        v = vscr[:, g * HD : (g + 1) * HD]
        summed = jnp.dot(weights.astype(jnp.bfloat16), v, preferred_element_type=jnp.float32)
        out_ref[:, h * HD : (h + 1) * HD] = (summed / total).astype(out_ref.dtype)


def attend(meta, scalars, freq, queries, own_k, own_v, data):
    devices, block_rows, rows, tails = meta[:4]
    kv_cols = own_k.shape[1]
    q_heads = queries.shape[1] // HD
    count = devices * block_rows + rows * (1 + tails)
    flops = 4 * rows * count * HD * q_heads
    arrays = [queries, own_k, own_v, *data]
    nbytes = sum(a.size * a.dtype.itemsize for a in arrays)
    smem = pl.BlockSpec(memory_space=pltpu.SMEM)
    vmem = pl.BlockSpec(memory_space=pltpu.VMEM)
    return pl.pallas_call(
        functools.partial(attend_kernel, meta),
        out_shape=jax.ShapeDtypeStruct(queries.shape, jnp.bfloat16),
        in_specs=[smem] * len(scalars) + [vmem] * (1 + len(arrays)),
        out_specs=vmem,
        scratch_shapes=[
            pltpu.VMEM((count, kv_cols), jnp.bfloat16),
            pltpu.VMEM((count, kv_cols), jnp.bfloat16),
        ],
        cost_estimate=pl.CostEstimate(
            flops=flops,
            transcendentals=rows * count * q_heads,
            bytes_accessed=nbytes + queries.size * 2,
        ),
    )(*scalars, freq, *arrays)


def token_info(index, suffix_lengths, request_group):
    ends = jnp.cumsum(suffix_lengths)
    request = jnp.sum((index[:, None] >= ends[None, :]).astype(jnp.int32), axis=1)
    onehot = request[:, None] == jnp.arange(suffix_lengths.shape[0], dtype=jnp.int32)[None, :]
    first = jnp.sum(jnp.where(onehot, (ends - suffix_lengths)[None, :], 0), axis=1)
    group = jnp.sum(jnp.where(onehot, request_group[None, :], 0), axis=1)
    return (request, index - first, group)


def shifted(array, axis, by, wrap):
    length = lax.axis_size(axis)
    pairs = [(i, (i + by) % length) for i in range(length) if wrap or i + by < length]
    return lax.ppermute(array, axis, pairs)


def body(
    queries,
    suffix_keys,
    suffix_values,
    prefix_keys,
    prefix_values,
    suffix_lengths,
    request_group,
    block_group,
):
    rows = queries.shape[0]
    kv_cols = suffix_keys.shape[1]
    kv_heads = kv_cols // HD
    q_heads = queries.shape[1] // HD
    repeat = q_heads // kv_heads
    devices = lax.axis_size("seq")
    me = lax.axis_index("seq")
    block_rows = prefix_keys.shape[0]
    prefix_len = block_rows * devices // GROUPS
    span = max(1, min(2048 // rows, devices // 8))
    scale = HD ** (-0.5)
    index = me * rows + jnp.arange(rows, dtype=jnp.int32)
    request, offset, group = token_info(index, suffix_lengths, request_group)

    prefix_kv = jnp.concatenate([prefix_keys, prefix_values], axis=1)
    suffix_kv = jnp.concatenate([suffix_keys, suffix_values], axis=1)

    def rotated_keys(raw, back):
        key_index = (me - back) * rows + jnp.arange(rows, dtype=jnp.int32)
        key_request, key_offset, _ = token_info(key_index, suffix_lengths, request_group)
        k_rot = rotate(raw.reshape(rows, kv_heads, HD), key_offset + prefix_len).reshape(rows, kv_cols)
        return key_index, key_request, k_rot

    if devices <= 16:
        received = {}
        late = list(range(span + 1, devices))[: max(0, devices - 1 - 5)]
        for by in range(1, devices):
            if by <= span:
                received[by] = shifted(jnp.concatenate([prefix_kv, suffix_kv], axis=0), "seq", by, True)
            elif by not in late:
                received[by] = shifted(prefix_kv, "seq", by, True)
        gates = tuple(received[devices - 1 - i] for i in range(len(late)))
        gates, payload, cache_keys_in, cache_values_in = lax.optimization_barrier(
            (gates, prefix_kv, suffix_keys, suffix_values)
        )
        for i, by in enumerate(late):
            received[devices - 1 - i] = gates[i]
            received[by] = shifted(payload, "seq", by, True)
        data = [prefix_kv] + [received[by] for by in range(1, devices)]
        if not late:
            cache_keys_in, cache_values_in = suffix_keys, suffix_values
        _, own_offset, _ = token_info(index, suffix_lengths, request_group)
        own_k_rot = rotate(cache_keys_in.reshape(rows, kv_heads, HD), own_offset + prefix_len).reshape(
            rows, kv_cols
        )
        cache = lax.all_to_all(
            jnp.stack([own_k_rot, cache_values_in], axis=0), "tp", split_axis=1, concat_axis=2, tiled=True
        )
        half = HD // 2
        freq = jnp.exp(jnp.arange(half, dtype=jnp.float32) * (-2.0 * math.log(500000.0) / HD))
        freq = jnp.concatenate([freq, freq])[None, :]
        scalars = [me.astype(jnp.int32).reshape(1), suffix_lengths, request_group, block_group]
        meta = (devices, block_rows, rows, min(span, devices - 1), prefix_len, repeat, scale)
        attended = attend(meta, scalars, freq, queries, own_k_rot, suffix_values, data)
        return (attended, cache[0], cache[1])

    prefix_parts = []
    suffix_parts = [(0, suffix_kv)]
    gathered = lax.all_gather(prefix_kv, "seq", axis=0, tiled=True)
    prefix_parts.append((None, gathered))
    for by in range(1, span + 1):
        suffix_parts.append((by, shifted(suffix_kv, "seq", by, False)))

    position = offset + prefix_len
    q_rot = rotate(queries.reshape(rows, q_heads, HD), position).reshape(rows, kv_heads, repeat, HD)

    key_chunks, value_chunks, visible_chunks = [], [], []
    for holder, kv in prefix_parts:
        count = kv.shape[0]
        if holder is None:
            holder_index = jnp.arange(count, dtype=jnp.int32) // block_rows
            row_group = jnp.take(block_group, holder_index)
            visible = row_group[None, :] == group[:, None]
        else:
            row_group = lax.dynamic_index_in_dim(block_group, holder, keepdims=False)
            visible = jnp.broadcast_to((group == row_group)[:, None], (rows, count))
        key_chunks.append(kv[:, :kv_cols])
        value_chunks.append(kv[:, kv_cols:])
        visible_chunks.append(visible)

    own_k_rot = None
    for back, kv in suffix_parts:
        key_index = (me - back) * rows + jnp.arange(rows, dtype=jnp.int32)
        key_request, key_offset, _ = token_info(key_index, suffix_lengths, request_group)
        k_rot = rotate(kv[:, :kv_cols].reshape(rows, kv_heads, HD), key_offset + prefix_len).reshape(
            rows, kv_cols
        )
        if back == 0:
            own_k_rot = k_rot
        visible = (
            (key_index[None, :] >= 0)
            & (key_request[None, :] == request[:, None])
            & (key_index[None, :] <= index[:, None])
        )
        key_chunks.append(k_rot)
        value_chunks.append(kv[:, kv_cols:])
        visible_chunks.append(visible)

    cache = lax.all_to_all(
        jnp.stack([own_k_rot, suffix_values], axis=0), "tp", split_axis=1, concat_axis=2, tiled=True
    )

    def scores_of(keys, visible):
        keys_split = keys.reshape(keys.shape[0], kv_heads, HD)
        scores = (
            jnp.einsum("bgrd,kgd->bgrk", q_rot, keys_split, preferred_element_type=jnp.float32)
            * scale
        )
        return jnp.where(visible[:, None, None, :], scores, BIG_NEGATIVE)

    def summed_of(scores, high, values, visible):
        weights = jnp.where(visible[:, None, None, :], jnp.exp(scores - high[..., None]), 0.0)
        summed = jnp.einsum(
            "bgrk,kgd->bgrd",
            weights.astype(jnp.bfloat16),
            values.reshape(values.shape[0], kv_heads, HD),
            preferred_element_type=jnp.float32,
        )
        return jnp.sum(weights, axis=-1), summed

    keys = jnp.concatenate(key_chunks, axis=0)
    values = jnp.concatenate(value_chunks, axis=0)
    visible = jnp.concatenate(visible_chunks, axis=1)
    count = keys.shape[0]
    if count * rows * q_heads * 4 <= (8 << 20):
        scores = scores_of(keys, visible)
        high = jnp.max(scores, axis=-1)
        total, summed = summed_of(scores, high, values, visible)
    else:
        width = 512
        steps = count // width
        tail = steps * width
        piece_k = keys[:tail].reshape(steps, width, kv_cols)
        piece_v = values[:tail].reshape(steps, width, kv_cols)
        piece_m = jnp.moveaxis(visible[:, :tail].reshape(rows, steps, width), 1, 0)

        def high_step(high, piece):
            k, m = piece
            return jnp.maximum(high, jnp.max(scores_of(k, m), axis=-1)), None

        high = jnp.max(scores_of(keys[tail:], visible[:, tail:]), axis=-1)
        high, _ = lax.scan(high_step, high, (piece_k, piece_m))

        def sum_step(carry, piece):
            k, v, m = piece
            total, summed = summed_of(scores_of(k, m), high, v, m)
            return (carry[0] + total, carry[1] + summed), None

        start = summed_of(scores_of(keys[tail:], visible[:, tail:]), high, values[tail:], visible[:, tail:])
        (total, summed), _ = lax.scan(sum_step, start, (piece_k, piece_v, piece_m))
    attended = (summed / total[..., None]).reshape(rows, q_heads * HD).astype(jnp.bfloat16)
    return (attended, cache[0], cache[1])


def solution(mesh):
    return jax.shard_map(
        body,
        mesh=mesh,
        in_specs=(
            P("seq", "tp"),
            P("seq", "tp"),
            P("seq", "tp"),
            P("seq", "tp"),
            P("seq", "tp"),
            P(),
            P(),
            P(),
        ),
        out_specs=(P("seq", "tp"), P(("seq", "tp"), None), P(("seq", "tp"), None)),
        check_vma=False,
    )
```

```python
import functools
import math

import jax
import jax.numpy as jnp
from jax import lax
from jax.experimental import pallas as pl
from jax.experimental.pallas import tpu as pltpu
from jax.sharding import PartitionSpec as P

HD = 128
GROUPS = 4


BIG_NEGATIVE = -1e30


def rotate(values, position):
    half = values.shape[-1] // 2
    freq = jnp.exp(
        jnp.arange(half, dtype=jnp.float32) * (-2.0 * math.log(500000.0) / values.shape[-1])
    )
    angle = position.astype(jnp.float32)[:, None] * freq[None, :]
    cosine = jnp.cos(angle)[:, None, :]
    sine = jnp.sin(angle)[:, None, :]
    floats = values.astype(jnp.float32)
    lower = floats[..., :half]
    upper = floats[..., half:]
    return jnp.concatenate(
        [lower * cosine - upper * sine, upper * cosine + lower * sine], axis=-1
    ).astype(jnp.bfloat16)


def attend_kernel(meta, *refs):
    devices, block_rows, rows, tails, prefix_len, repeat, scale = meta
    me_ref, lens_ref, rg_ref, bg_ref, q_ref, own_k_ref, own_v_ref = refs[:7]
    data = refs[7 : 7 + devices]
    out_ref, kscr, vscr = refs[7 + devices :]
    kv_cols = kscr.shape[1]
    count = kscr.shape[0]
    base = devices * block_rows
    q_heads = q_ref.shape[1] // HD
    me = me_ref[0]
    starts, at = [], 0
    for j in range(lens_ref.shape[0]):
        starts.append(at)
        at = at + lens_ref[j]

    def info(index):
        request = jnp.full(index.shape, -2, jnp.int32)
        first = jnp.zeros(index.shape, jnp.int32)
        group = jnp.full(index.shape, -1, jnp.int32)
        for j, start in enumerate(starts):
            after = index >= start
            request = jnp.where(after, j, request)
            first = jnp.where(after, start, first)
            group = jnp.where(after, rg_ref[j], group)
        return request, index - first, group

    lane = lax.broadcasted_iota(jnp.int32, (1, HD), 1)
    pair = jnp.where(lane < HD // 2, lane, lane - HD // 2)
    freq = jnp.exp(pair.astype(jnp.float32) * (-2.0 * math.log(500000.0) / HD))
    sign = jnp.where(lane < HD // 2, -1.0, 1.0).astype(jnp.float32)

    def tables(offset):
        angle = (offset + prefix_len).astype(jnp.float32) * freq
        return jnp.cos(angle), jnp.sin(angle) * sign

    def rotated(x, cosine, sine):
        return (x * cosine + pltpu.roll(x, HD // 2, 1) * sine).astype(jnp.bfloat16)

    for c in range(devices):
        kscr[c * block_rows : (c + 1) * block_rows, :] = data[c][0:block_rows, 0:kv_cols]
        vscr[c * block_rows : (c + 1) * block_rows, :] = data[c][0:block_rows, kv_cols : 2 * kv_cols]
    for b in range(0, tails + 1):
        low = base + b * rows
        index = (me - b) * rows + lax.broadcasted_iota(jnp.int32, (rows, 1), 0)
        _, offset, _ = info(index)
        cosine, sine = tables(offset)
        for g in range(kv_cols // HD):
            if b == 0:
                x = own_k_ref[:, g * HD : (g + 1) * HD]
            else:
                x = data[b][block_rows : block_rows + rows, g * HD : (g + 1) * HD]
            kscr[low : low + rows, g * HD : (g + 1) * HD] = rotated(x.astype(jnp.float32), cosine, sine)
        if b == 0:
            vscr[low : low + rows, :] = own_v_ref[...]
        else:
            vscr[low : low + rows, :] = data[b][block_rows : block_rows + rows, kv_cols : 2 * kv_cols]

    token = me * rows + lax.broadcasted_iota(jnp.int32, (rows, 1), 0)
    request, offset, group = info(token)
    col = lax.broadcasted_iota(jnp.int32, (1, count), 1)
    key_group = jnp.full((1, count), -1, jnp.int32)
    for c in range(devices):
        holder = lax.rem(me - c + devices, devices)
        key_group = jnp.where(col >= c * block_rows, bg_ref[holder], key_group)
    key_index = jnp.full((1, count), -1, jnp.int32)
    for b in range(tails + 1):
        low = base + b * rows
        key_index = jnp.where(col >= low, (me - b) * rows + col - low, key_index)
    key_request, _, _ = info(key_index)
    visible = ((col < base) & (key_group == group)) | (
        (key_request == request) & (key_index <= token)
    )
    cosine, sine = tables(offset)
    for g in range(q_heads // repeat):
        heads = range(g * repeat, (g + 1) * repeat)
        q = jnp.concatenate(
            [rotated(q_ref[:, h * HD : (h + 1) * HD].astype(jnp.float32), cosine, sine) for h in heads],
            axis=0,
        )
        k = kscr[:, g * HD : (g + 1) * HD]
        scores = lax.dot_general(
            q, k, (((1,), (1,)), ((), ())), preferred_element_type=jnp.float32
        ) * scale
        weights, totals = [], []
        for r in range(repeat):
            part = jnp.where(visible, scores[r * rows : (r + 1) * rows], BIG_NEGATIVE)
            high = jnp.max(part, axis=1, keepdims=True)
            part = jnp.exp(part - high)
            totals.append(jnp.sum(part, axis=1, keepdims=True))
            weights.append(part.astype(jnp.bfloat16))
        v = vscr[:, g * HD : (g + 1) * HD]
        summed = jnp.dot(jnp.concatenate(weights, axis=0), v, preferred_element_type=jnp.float32)
        for r, h in enumerate(heads):
            out_ref[:, h * HD : (h + 1) * HD] = (summed[r * rows : (r + 1) * rows] / totals[r]).astype(
                out_ref.dtype
            )


def attend(meta, scalars, queries, own_k, own_v, data):
    devices, block_rows, rows, tails = meta[:4]
    kv_cols = own_k.shape[1]
    q_heads = queries.shape[1] // HD
    count = devices * block_rows + rows * (1 + tails)
    flops = 4 * rows * count * HD * q_heads
    arrays = [queries, own_k, own_v, *data]
    nbytes = sum(a.size * a.dtype.itemsize for a in arrays)
    smem = pl.BlockSpec(memory_space=pltpu.SMEM)
    vmem = pl.BlockSpec(memory_space=pltpu.VMEM)
    return pl.pallas_call(
        functools.partial(attend_kernel, meta),
        out_shape=jax.ShapeDtypeStruct(queries.shape, jnp.bfloat16),
        in_specs=[smem] * len(scalars) + [vmem] * len(arrays),
        out_specs=vmem,
        scratch_shapes=[
            pltpu.VMEM((count, kv_cols), jnp.bfloat16),
            pltpu.VMEM((count, kv_cols), jnp.bfloat16),
        ],
        cost_estimate=pl.CostEstimate(
            flops=flops,
            transcendentals=rows * count * q_heads,
            bytes_accessed=nbytes + queries.size * 2,
        ),
    )(*scalars, *arrays)


def token_info(index, suffix_lengths, request_group):
    ends = jnp.cumsum(suffix_lengths)
    request = jnp.sum((index[:, None] >= ends[None, :]).astype(jnp.int32), axis=1)
    onehot = request[:, None] == jnp.arange(suffix_lengths.shape[0], dtype=jnp.int32)[None, :]
    first = jnp.sum(jnp.where(onehot, (ends - suffix_lengths)[None, :], 0), axis=1)
    group = jnp.sum(jnp.where(onehot, request_group[None, :], 0), axis=1)
    return (request, index - first, group)


def shifted(array, axis, by, wrap):
    length = lax.axis_size(axis)
    pairs = [(i, (i + by) % length) for i in range(length) if wrap or i + by < length]
    return lax.ppermute(array, axis, pairs)


def body(
    queries,
    suffix_keys,
    suffix_values,
    prefix_keys,
    prefix_values,
    suffix_lengths,
    request_group,
    block_group,
):
    rows = queries.shape[0]
    kv_cols = suffix_keys.shape[1]
    kv_heads = kv_cols // HD
    q_heads = queries.shape[1] // HD
    repeat = q_heads // kv_heads
    devices = lax.axis_size("seq")
    me = lax.axis_index("seq")
    block_rows = prefix_keys.shape[0]
    prefix_len = block_rows * devices // GROUPS
    span = max(1, min(2048 // rows, devices // 8))
    scale = HD ** (-0.5)
    index = me * rows + jnp.arange(rows, dtype=jnp.int32)
    request, offset, group = token_info(index, suffix_lengths, request_group)

    prefix_kv = jnp.concatenate([prefix_keys, prefix_values], axis=1)
    suffix_kv = jnp.concatenate([suffix_keys, suffix_values], axis=1)

    def rotated_keys(raw, back):
        key_index = (me - back) * rows + jnp.arange(rows, dtype=jnp.int32)
        key_request, key_offset, _ = token_info(key_index, suffix_lengths, request_group)
        k_rot = rotate(raw.reshape(rows, kv_heads, HD), key_offset + prefix_len).reshape(rows, kv_cols)
        return key_index, key_request, k_rot

    if devices <= 16:
        received = {}
        late = list(range(span + 1, devices))[: max(0, devices - 1 - 5)]
        for by in range(1, devices):
            if by <= span:
                received[by] = shifted(jnp.concatenate([prefix_kv, suffix_kv], axis=0), "seq", by, True)
            elif by not in late:
                received[by] = shifted(prefix_kv, "seq", by, True)
        gates = tuple(received[devices - 1 - i] for i in range(len(late)))
        gates, payload, cache_keys_in, cache_values_in = lax.optimization_barrier(
            (gates, prefix_kv, suffix_keys, suffix_values)
        )
        for i, by in enumerate(late):
            received[devices - 1 - i] = gates[i]
            received[by] = shifted(payload, "seq", by, True)
        data = [prefix_kv] + [received[by] for by in range(1, devices)]
        if not late:
            cache_keys_in, cache_values_in = suffix_keys, suffix_values
        _, own_offset, _ = token_info(index, suffix_lengths, request_group)
        own_k_rot = rotate(cache_keys_in.reshape(rows, kv_heads, HD), own_offset + prefix_len).reshape(
            rows, kv_cols
        )
        cache = lax.all_to_all(
            jnp.stack([own_k_rot, cache_values_in], axis=0), "tp", split_axis=1, concat_axis=2, tiled=True
        )
        scalars = [me.astype(jnp.int32).reshape(1), suffix_lengths, request_group, block_group]
        meta = (devices, block_rows, rows, min(span, devices - 1), prefix_len, repeat, scale)
        attended = attend(meta, scalars, queries, suffix_keys, suffix_values, data)
        return (attended, cache[0], cache[1])

    prefix_parts = []
    suffix_parts = [(0, suffix_kv)]
    gathered = lax.all_gather(prefix_kv, "seq", axis=0, tiled=True)
    prefix_parts.append((None, gathered))
    for by in range(1, span + 1):
        suffix_parts.append((by, shifted(suffix_kv, "seq", by, False)))

    position = offset + prefix_len
    q_rot = rotate(queries.reshape(rows, q_heads, HD), position).reshape(rows, kv_heads, repeat, HD)

    key_chunks, value_chunks, visible_chunks = [], [], []
    for holder, kv in prefix_parts:
        count = kv.shape[0]
        if holder is None:
            holder_index = jnp.arange(count, dtype=jnp.int32) // block_rows
            row_group = jnp.take(block_group, holder_index)
            visible = row_group[None, :] == group[:, None]
        else:
            row_group = lax.dynamic_index_in_dim(block_group, holder, keepdims=False)
            visible = jnp.broadcast_to((group == row_group)[:, None], (rows, count))
        key_chunks.append(kv[:, :kv_cols])
        value_chunks.append(kv[:, kv_cols:])
        visible_chunks.append(visible)

    own_k_rot = None
    for back, kv in suffix_parts:
        key_index = (me - back) * rows + jnp.arange(rows, dtype=jnp.int32)
        key_request, key_offset, _ = token_info(key_index, suffix_lengths, request_group)
        k_rot = rotate(kv[:, :kv_cols].reshape(rows, kv_heads, HD), key_offset + prefix_len).reshape(
            rows, kv_cols
        )
        if back == 0:
            own_k_rot = k_rot
        visible = (
            (key_index[None, :] >= 0)
            & (key_request[None, :] == request[:, None])
            & (key_index[None, :] <= index[:, None])
        )
        key_chunks.append(k_rot)
        value_chunks.append(kv[:, kv_cols:])
        visible_chunks.append(visible)

    cache = lax.all_to_all(
        jnp.stack([own_k_rot, suffix_values], axis=0), "tp", split_axis=1, concat_axis=2, tiled=True
    )

    def scores_of(keys, visible):
        keys_split = keys.reshape(keys.shape[0], kv_heads, HD)
        scores = (
            jnp.einsum("bgrd,kgd->bgrk", q_rot, keys_split, preferred_element_type=jnp.float32)
            * scale
        )
        return jnp.where(visible[:, None, None, :], scores, BIG_NEGATIVE)

    def summed_of(scores, high, values, visible):
        weights = jnp.where(visible[:, None, None, :], jnp.exp(scores - high[..., None]), 0.0)
        summed = jnp.einsum(
            "bgrk,kgd->bgrd",
            weights.astype(jnp.bfloat16),
            values.reshape(values.shape[0], kv_heads, HD),
            preferred_element_type=jnp.float32,
        )
        return jnp.sum(weights, axis=-1), summed

    keys = jnp.concatenate(key_chunks, axis=0)
    values = jnp.concatenate(value_chunks, axis=0)
    visible = jnp.concatenate(visible_chunks, axis=1)
    count = keys.shape[0]
    if count * rows * q_heads * 4 <= (8 << 20):
        scores = scores_of(keys, visible)
        high = jnp.max(scores, axis=-1)
        total, summed = summed_of(scores, high, values, visible)
    else:
        width = 512
        steps = count // width
        tail = steps * width
        piece_k = keys[:tail].reshape(steps, width, kv_cols)
        piece_v = values[:tail].reshape(steps, width, kv_cols)
        piece_m = jnp.moveaxis(visible[:, :tail].reshape(rows, steps, width), 1, 0)

        def high_step(high, piece):
            k, m = piece
            return jnp.maximum(high, jnp.max(scores_of(k, m), axis=-1)), None

        high = jnp.max(scores_of(keys[tail:], visible[:, tail:]), axis=-1)
        high, _ = lax.scan(high_step, high, (piece_k, piece_m))

        def sum_step(carry, piece):
            k, v, m = piece
            total, summed = summed_of(scores_of(k, m), high, v, m)
            return (carry[0] + total, carry[1] + summed), None

        start = summed_of(scores_of(keys[tail:], visible[:, tail:]), high, values[tail:], visible[:, tail:])
        (total, summed), _ = lax.scan(sum_step, start, (piece_k, piece_v, piece_m))
    attended = (summed / total[..., None]).reshape(rows, q_heads * HD).astype(jnp.bfloat16)
    return (attended, cache[0], cache[1])


def solution(mesh):
    return jax.shard_map(
        body,
        mesh=mesh,
        in_specs=(
            P("seq", "tp"),
            P("seq", "tp"),
            P("seq", "tp"),
            P("seq", "tp"),
            P("seq", "tp"),
            P(),
            P(),
            P(),
        ),
        out_specs=(P("seq", "tp"), P(("seq", "tp"), None), P(("seq", "tp"), None)),
        check_vma=False,
    )
```

```python
import functools
import math

import jax
import jax.numpy as jnp
from jax import lax
from jax.experimental import pallas as pl
from jax.experimental.pallas import tpu as pltpu
from jax.sharding import PartitionSpec as P

HD = 128
GROUPS = 4


BIG_NEGATIVE = -1e30


def rotate(values, position):
    half = values.shape[-1] // 2
    freq = jnp.exp(
        jnp.arange(half, dtype=jnp.float32) * (-2.0 * math.log(500000.0) / values.shape[-1])
    )
    angle = position.astype(jnp.float32)[:, None] * freq[None, :]
    cosine = jnp.cos(angle)[:, None, :]
    sine = jnp.sin(angle)[:, None, :]
    floats = values.astype(jnp.float32)
    lower = floats[..., :half]
    upper = floats[..., half:]
    return jnp.concatenate(
        [lower * cosine - upper * sine, upper * cosine + lower * sine], axis=-1
    ).astype(jnp.bfloat16)


def attend_kernel(meta, *refs):
    devices, block_rows, rows, tails, prefix_len, repeat, scale = meta
    me_ref, lens_ref, rg_ref, bg_ref, q_ref, own_k_ref, own_v_ref = refs[:7]
    data = refs[7 : 7 + devices]
    out_ref, kscr, vscr = refs[7 + devices :]
    kv_cols = kscr.shape[1]
    count = kscr.shape[0]
    base = devices * block_rows
    q_heads = q_ref.shape[1] // HD
    me = me_ref[0]
    starts, at = [], 0
    for j in range(lens_ref.shape[0]):
        starts.append(at)
        at = at + lens_ref[j]

    def info(index):
        request = jnp.full(index.shape, -2, jnp.int32)
        first = jnp.zeros(index.shape, jnp.int32)
        group = jnp.full(index.shape, -1, jnp.int32)
        for j, start in enumerate(starts):
            after = index >= start
            request = jnp.where(after, j, request)
            first = jnp.where(after, start, first)
            group = jnp.where(after, rg_ref[j], group)
        return request, index - first, group

    lane = lax.broadcasted_iota(jnp.int32, (1, HD), 1)
    pair = jnp.where(lane < HD // 2, lane, lane - HD // 2)
    freq = jnp.exp(pair.astype(jnp.float32) * (-2.0 * math.log(500000.0) / HD))
    sign = jnp.where(lane < HD // 2, -1.0, 1.0).astype(jnp.float32)

    def tables(offset):
        angle = (offset + prefix_len).astype(jnp.float32) * freq
        return jnp.cos(angle), jnp.sin(angle) * sign

    def rotated(x, cosine, sine):
        return (x * cosine + pltpu.roll(x, HD // 2, 1) * sine).astype(jnp.bfloat16)

    for c in range(devices):
        kscr[c * block_rows : (c + 1) * block_rows, :] = data[c][0:block_rows, 0:kv_cols]
        vscr[c * block_rows : (c + 1) * block_rows, :] = data[c][0:block_rows, kv_cols : 2 * kv_cols]
    for b in range(0, tails + 1):
        low = base + b * rows
        index = (me - b) * rows + lax.broadcasted_iota(jnp.int32, (rows, 1), 0)
        _, offset, _ = info(index)
        cosine, sine = tables(offset)
        for g in range(kv_cols // HD):
            if b == 0:
                x = own_k_ref[:, g * HD : (g + 1) * HD]
            else:
                x = data[b][block_rows : block_rows + rows, g * HD : (g + 1) * HD]
            kscr[low : low + rows, g * HD : (g + 1) * HD] = rotated(x.astype(jnp.float32), cosine, sine)
        if b == 0:
            vscr[low : low + rows, :] = own_v_ref[...]
        else:
            vscr[low : low + rows, :] = data[b][block_rows : block_rows + rows, kv_cols : 2 * kv_cols]

    token = me * rows + lax.broadcasted_iota(jnp.int32, (rows, 1), 0)
    request, offset, group = info(token)
    col = lax.broadcasted_iota(jnp.int32, (1, count), 1)
    key_group = jnp.full((1, count), -1, jnp.int32)
    for c in range(devices):
        holder = lax.rem(me - c + devices, devices)
        key_group = jnp.where(col >= c * block_rows, bg_ref[holder], key_group)
    key_index = jnp.full((1, count), -1, jnp.int32)
    for b in range(tails + 1):
        low = base + b * rows
        key_index = jnp.where(col >= low, (me - b) * rows + col - low, key_index)
    key_request, _, _ = info(key_index)
    visible = ((col < base) & (key_group == group)) | (
        (key_request == request) & (key_index <= token)
    )
    cosine, sine = tables(offset)
    for g in range(q_heads // repeat):
        heads = range(g * repeat, (g + 1) * repeat)
        q = jnp.concatenate(
            [rotated(q_ref[:, h * HD : (h + 1) * HD].astype(jnp.float32), cosine, sine) for h in heads],
            axis=0,
        )
        k = kscr[:, g * HD : (g + 1) * HD]
        scores = lax.dot_general(
            q, k, (((1,), (1,)), ((), ())), preferred_element_type=jnp.float32
        ) * scale
        weights, totals = [], []
        for r in range(repeat):
            part = jnp.where(visible, scores[r * rows : (r + 1) * rows], BIG_NEGATIVE)
            high = jnp.max(part, axis=1, keepdims=True)
            part = jnp.exp(part - high)
            totals.append(jnp.sum(part, axis=1, keepdims=True))
            weights.append(part.astype(jnp.bfloat16))
        v = vscr[:, g * HD : (g + 1) * HD]
        summed = jnp.dot(jnp.concatenate(weights, axis=0), v, preferred_element_type=jnp.float32)
        for r, h in enumerate(heads):
            out_ref[:, h * HD : (h + 1) * HD] = (summed[r * rows : (r + 1) * rows] / totals[r]).astype(
                out_ref.dtype
            )


def attend(meta, scalars, queries, own_k, own_v, data):
    devices, block_rows, rows, tails = meta[:4]
    kv_cols = own_k.shape[1]
    q_heads = queries.shape[1] // HD
    count = devices * block_rows + rows * (1 + tails)
    flops = 4 * rows * count * HD * q_heads
    arrays = [queries, own_k, own_v, *data]
    nbytes = sum(a.size * a.dtype.itemsize for a in arrays)
    smem = pl.BlockSpec(memory_space=pltpu.SMEM)
    vmem = pl.BlockSpec(memory_space=pltpu.VMEM)
    return pl.pallas_call(
        functools.partial(attend_kernel, meta),
        out_shape=jax.ShapeDtypeStruct(queries.shape, jnp.bfloat16),
        in_specs=[smem] * len(scalars) + [vmem] * len(arrays),
        out_specs=vmem,
        scratch_shapes=[
            pltpu.VMEM((count, kv_cols), jnp.bfloat16),
            pltpu.VMEM((count, kv_cols), jnp.bfloat16),
        ],
        cost_estimate=pl.CostEstimate(
            flops=flops,
            transcendentals=rows * count * q_heads,
            bytes_accessed=nbytes + queries.size * 2,
        ),
    )(*scalars, *arrays)


def token_info(index, suffix_lengths, request_group):
    ends = jnp.cumsum(suffix_lengths)
    request = jnp.sum((index[:, None] >= ends[None, :]).astype(jnp.int32), axis=1)
    onehot = request[:, None] == jnp.arange(suffix_lengths.shape[0], dtype=jnp.int32)[None, :]
    first = jnp.sum(jnp.where(onehot, (ends - suffix_lengths)[None, :], 0), axis=1)
    group = jnp.sum(jnp.where(onehot, request_group[None, :], 0), axis=1)
    return (request, index - first, group)


def shifted(array, axis, by, wrap):
    length = lax.axis_size(axis)
    pairs = [(i, (i + by) % length) for i in range(length) if wrap or i + by < length]
    return lax.ppermute(array, axis, pairs)


def body(
    queries,
    suffix_keys,
    suffix_values,
    prefix_keys,
    prefix_values,
    suffix_lengths,
    request_group,
    block_group,
):
    rows = queries.shape[0]
    kv_cols = suffix_keys.shape[1]
    kv_heads = kv_cols // HD
    q_heads = queries.shape[1] // HD
    repeat = q_heads // kv_heads
    devices = lax.axis_size("seq")
    me = lax.axis_index("seq")
    block_rows = prefix_keys.shape[0]
    prefix_len = block_rows * devices // GROUPS
    span = max(1, min(2048 // rows, devices // 8))
    scale = HD ** (-0.5)
    index = me * rows + jnp.arange(rows, dtype=jnp.int32)
    request, offset, group = token_info(index, suffix_lengths, request_group)

    prefix_kv = jnp.concatenate([prefix_keys, prefix_values], axis=1)
    suffix_kv = jnp.concatenate([suffix_keys, suffix_values], axis=1)

    def rotated_keys(raw, back):
        key_index = (me - back) * rows + jnp.arange(rows, dtype=jnp.int32)
        key_request, key_offset, _ = token_info(key_index, suffix_lengths, request_group)
        k_rot = rotate(raw.reshape(rows, kv_heads, HD), key_offset + prefix_len).reshape(rows, kv_cols)
        return key_index, key_request, k_rot

    if devices <= 16:
        _, own_offset, _ = token_info(index, suffix_lengths, request_group)
        own_k_rot = rotate(suffix_keys.reshape(rows, kv_heads, HD), own_offset + prefix_len).reshape(
            rows, kv_cols
        )
        stacked, both, early_kv = lax.optimization_barrier(
            (
                jnp.stack([own_k_rot, suffix_values], axis=0),
                jnp.concatenate([prefix_kv, suffix_kv], axis=0),
                prefix_kv,
            )
        )
        cache = lax.all_to_all(stacked, "tp", split_axis=1, concat_axis=2, tiled=True)
        received = {}
        late = list(range(span + 1, devices))[: max(0, devices - 1 - 5)]
        for by in range(1, devices):
            if by <= span:
                received[by] = shifted(both, "seq", by, True)
            elif by not in late:
                received[by] = shifted(early_kv, "seq", by, True)
        gates = tuple(received[devices - 1 - i] for i in range(len(late)))
        gates, payload = lax.optimization_barrier((gates, prefix_kv))
        for i, by in enumerate(late):
            received[devices - 1 - i] = gates[i]
            received[by] = shifted(payload, "seq", by, True)
        data = [prefix_kv] + [received[by] for by in range(1, devices)]
        scalars = [me.astype(jnp.int32).reshape(1), suffix_lengths, request_group, block_group]
        meta = (devices, block_rows, rows, min(span, devices - 1), prefix_len, repeat, scale)
        attended = attend(meta, scalars, queries, suffix_keys, suffix_values, data)
        return (attended, cache[0], cache[1])

    prefix_parts = []
    suffix_parts = [(0, suffix_kv)]
    gathered = lax.all_gather(prefix_kv, "seq", axis=0, tiled=True)
    prefix_parts.append((None, gathered))
    for by in range(1, span + 1):
        suffix_parts.append((by, shifted(suffix_kv, "seq", by, False)))

    position = offset + prefix_len
    q_rot = rotate(queries.reshape(rows, q_heads, HD), position).reshape(rows, kv_heads, repeat, HD)

    key_chunks, value_chunks, visible_chunks = [], [], []
    for holder, kv in prefix_parts:
        count = kv.shape[0]
        if holder is None:
            holder_index = jnp.arange(count, dtype=jnp.int32) // block_rows
            row_group = jnp.take(block_group, holder_index)
            visible = row_group[None, :] == group[:, None]
        else:
            row_group = lax.dynamic_index_in_dim(block_group, holder, keepdims=False)
            visible = jnp.broadcast_to((group == row_group)[:, None], (rows, count))
        key_chunks.append(kv[:, :kv_cols])
        value_chunks.append(kv[:, kv_cols:])
        visible_chunks.append(visible)

    own_k_rot = None
    for back, kv in suffix_parts:
        key_index = (me - back) * rows + jnp.arange(rows, dtype=jnp.int32)
        key_request, key_offset, _ = token_info(key_index, suffix_lengths, request_group)
        k_rot = rotate(kv[:, :kv_cols].reshape(rows, kv_heads, HD), key_offset + prefix_len).reshape(
            rows, kv_cols
        )
        if back == 0:
            own_k_rot = k_rot
        visible = (
            (key_index[None, :] >= 0)
            & (key_request[None, :] == request[:, None])
            & (key_index[None, :] <= index[:, None])
        )
        key_chunks.append(k_rot)
        value_chunks.append(kv[:, kv_cols:])
        visible_chunks.append(visible)

    cache = lax.all_to_all(
        jnp.stack([own_k_rot, suffix_values], axis=0), "tp", split_axis=1, concat_axis=2, tiled=True
    )

    def scores_of(keys, visible):
        keys_split = keys.reshape(keys.shape[0], kv_heads, HD)
        scores = (
            jnp.einsum("bgrd,kgd->bgrk", q_rot, keys_split, preferred_element_type=jnp.float32)
            * scale
        )
        return jnp.where(visible[:, None, None, :], scores, BIG_NEGATIVE)

    def summed_of(scores, high, values, visible):
        weights = jnp.where(visible[:, None, None, :], jnp.exp(scores - high[..., None]), 0.0)
        summed = jnp.einsum(
            "bgrk,kgd->bgrd",
            weights.astype(jnp.bfloat16),
            values.reshape(values.shape[0], kv_heads, HD),
            preferred_element_type=jnp.float32,
        )
        return jnp.sum(weights, axis=-1), summed

    keys = jnp.concatenate(key_chunks, axis=0)
    values = jnp.concatenate(value_chunks, axis=0)
    visible = jnp.concatenate(visible_chunks, axis=1)
    count = keys.shape[0]
    if count * rows * q_heads * 4 <= (8 << 20):
        scores = scores_of(keys, visible)
        high = jnp.max(scores, axis=-1)
        total, summed = summed_of(scores, high, values, visible)
    else:
        width = 512
        steps = count // width
        tail = steps * width
        piece_k = keys[:tail].reshape(steps, width, kv_cols)
        piece_v = values[:tail].reshape(steps, width, kv_cols)
        piece_m = jnp.moveaxis(visible[:, :tail].reshape(rows, steps, width), 1, 0)

        def high_step(high, piece):
            k, m = piece
            return jnp.maximum(high, jnp.max(scores_of(k, m), axis=-1)), None

        high = jnp.max(scores_of(keys[tail:], visible[:, tail:]), axis=-1)
        high, _ = lax.scan(high_step, high, (piece_k, piece_m))

        def sum_step(carry, piece):
            k, v, m = piece
            total, summed = summed_of(scores_of(k, m), high, v, m)
            return (carry[0] + total, carry[1] + summed), None

        start = summed_of(scores_of(keys[tail:], visible[:, tail:]), high, values[tail:], visible[:, tail:])
        (total, summed), _ = lax.scan(sum_step, start, (piece_k, piece_v, piece_m))
    attended = (summed / total[..., None]).reshape(rows, q_heads * HD).astype(jnp.bfloat16)
    return (attended, cache[0], cache[1])


def solution(mesh):
    return jax.shard_map(
        body,
        mesh=mesh,
        in_specs=(
            P("seq", "tp"),
            P("seq", "tp"),
            P("seq", "tp"),
            P("seq", "tp"),
            P("seq", "tp"),
            P(),
            P(),
            P(),
        ),
        out_specs=(P("seq", "tp"), P(("seq", "tp"), None), P(("seq", "tp"), None)),
        check_vma=False,
    )
```

```python
import functools
import math

import jax
import jax.numpy as jnp
from jax import lax
from jax.experimental import pallas as pl
from jax.experimental.pallas import tpu as pltpu
from jax.sharding import PartitionSpec as P

HD = 128
GROUPS = 4


BIG_NEGATIVE = -1e30


def rotate(values, position):
    half = values.shape[-1] // 2
    freq = jnp.exp(
        jnp.arange(half, dtype=jnp.float32) * (-2.0 * math.log(500000.0) / values.shape[-1])
    )
    angle = position.astype(jnp.float32)[:, None] * freq[None, :]
    cosine = jnp.cos(angle)[:, None, :]
    sine = jnp.sin(angle)[:, None, :]
    floats = values.astype(jnp.float32)
    lower = floats[..., :half]
    upper = floats[..., half:]
    return jnp.concatenate(
        [lower * cosine - upper * sine, upper * cosine + lower * sine], axis=-1
    ).astype(jnp.bfloat16)


def attend_kernel(meta, *refs):
    devices, block_rows, rows, tails, prefix_len, repeat, scale, where_block, arrays = meta
    me_ref, lens_ref, rg_ref, bg_ref, q_ref, own_k_ref, own_v_ref = refs[:7]
    data = refs[7 : 7 + arrays]
    out_ref, kscr, vscr = refs[7 + arrays :]
    kv_cols = kscr.shape[1]
    count = kscr.shape[0]
    base = devices * block_rows
    q_heads = q_ref.shape[1] // HD
    me = me_ref[0]
    starts, at = [], 0
    for j in range(lens_ref.shape[0]):
        starts.append(at)
        at = at + lens_ref[j]

    def info(index):
        request = jnp.full(index.shape, -2, jnp.int32)
        first = jnp.zeros(index.shape, jnp.int32)
        group = jnp.full(index.shape, -1, jnp.int32)
        for j, start in enumerate(starts):
            after = index >= start
            request = jnp.where(after, j, request)
            first = jnp.where(after, start, first)
            group = jnp.where(after, rg_ref[j], group)
        return request, index - first, group

    lane = lax.broadcasted_iota(jnp.int32, (1, HD), 1)
    pair = jnp.where(lane < HD // 2, lane, lane - HD // 2)
    freq = jnp.exp(pair.astype(jnp.float32) * (-2.0 * math.log(500000.0) / HD))
    sign = jnp.where(lane < HD // 2, -1.0, 1.0).astype(jnp.float32)

    def tables(offset):
        angle = (offset + prefix_len).astype(jnp.float32) * freq
        return jnp.cos(angle), jnp.sin(angle) * sign

    def rotated(x, cosine, sine):
        return (x * cosine + pltpu.roll(x, HD // 2, 1) * sine).astype(jnp.bfloat16)

    for c in range(devices):
        at, row = where_block[c]
        kscr[c * block_rows : (c + 1) * block_rows, :] = data[at][row : row + block_rows, 0:kv_cols]
        vscr[c * block_rows : (c + 1) * block_rows, :] = data[at][row : row + block_rows, kv_cols : 2 * kv_cols]
    for b in range(0, tails + 1):
        low = base + b * rows
        index = (me - b) * rows + lax.broadcasted_iota(jnp.int32, (rows, 1), 0)
        _, offset, _ = info(index)
        cosine, sine = tables(offset)
        for g in range(kv_cols // HD):
            if b == 0:
                x = own_k_ref[:, g * HD : (g + 1) * HD]
            else:
                at, row = where_block[devices + b - 1]
                x = data[at][row : row + rows, g * HD : (g + 1) * HD]
            kscr[low : low + rows, g * HD : (g + 1) * HD] = rotated(x.astype(jnp.float32), cosine, sine)
        if b == 0:
            vscr[low : low + rows, :] = own_v_ref[...]
        else:
            at, row = where_block[devices + b - 1]
            vscr[low : low + rows, :] = data[at][row : row + rows, kv_cols : 2 * kv_cols]

    token = me * rows + lax.broadcasted_iota(jnp.int32, (rows, 1), 0)
    request, offset, group = info(token)
    col = lax.broadcasted_iota(jnp.int32, (1, count), 1)
    key_group = jnp.full((1, count), -1, jnp.int32)
    for c in range(devices):
        holder = lax.rem(me - c + devices, devices)
        key_group = jnp.where(col >= c * block_rows, bg_ref[holder], key_group)
    key_index = jnp.full((1, count), -1, jnp.int32)
    for b in range(tails + 1):
        low = base + b * rows
        key_index = jnp.where(col >= low, (me - b) * rows + col - low, key_index)
    key_request, _, _ = info(key_index)
    visible = ((col < base) & (key_group == group)) | (
        (key_request == request) & (key_index <= token)
    )
    cosine, sine = tables(offset)
    for g in range(q_heads // repeat):
        heads = range(g * repeat, (g + 1) * repeat)
        q = jnp.concatenate(
            [rotated(q_ref[:, h * HD : (h + 1) * HD].astype(jnp.float32), cosine, sine) for h in heads],
            axis=0,
        )
        k = kscr[:, g * HD : (g + 1) * HD]
        scores = lax.dot_general(
            q, k, (((1,), (1,)), ((), ())), preferred_element_type=jnp.float32
        ) * scale
        weights, totals = [], []
        for r in range(repeat):
            part = jnp.where(visible, scores[r * rows : (r + 1) * rows], BIG_NEGATIVE)
            high = jnp.max(part, axis=1, keepdims=True)
            part = jnp.exp(part - high)
            totals.append(jnp.sum(part, axis=1, keepdims=True))
            weights.append(part.astype(jnp.bfloat16))
        v = vscr[:, g * HD : (g + 1) * HD]
        summed = jnp.dot(jnp.concatenate(weights, axis=0), v, preferred_element_type=jnp.float32)
        for r, h in enumerate(heads):
            out_ref[:, h * HD : (h + 1) * HD] = (summed[r * rows : (r + 1) * rows] / totals[r]).astype(
                out_ref.dtype
            )


def attend(meta, scalars, queries, own_k, own_v, data):
    devices, block_rows, rows, tails = meta[:4]
    kv_cols = own_k.shape[1]
    q_heads = queries.shape[1] // HD
    count = devices * block_rows + rows * (1 + tails)
    flops = 4 * rows * count * HD * q_heads
    arrays = [queries, own_k, own_v, *data]
    nbytes = sum(a.size * a.dtype.itemsize for a in arrays)
    smem = pl.BlockSpec(memory_space=pltpu.SMEM)
    vmem = pl.BlockSpec(memory_space=pltpu.VMEM)
    return pl.pallas_call(
        functools.partial(attend_kernel, meta),
        out_shape=jax.ShapeDtypeStruct(queries.shape, jnp.bfloat16),
        in_specs=[smem] * len(scalars) + [vmem] * len(arrays),
        out_specs=vmem,
        scratch_shapes=[
            pltpu.VMEM((count, kv_cols), jnp.bfloat16),
            pltpu.VMEM((count, kv_cols), jnp.bfloat16),
        ],
        cost_estimate=pl.CostEstimate(
            flops=flops,
            transcendentals=rows * count * q_heads,
            bytes_accessed=nbytes + queries.size * 2,
        ),
    )(*scalars, *arrays)


def token_info(index, suffix_lengths, request_group):
    ends = jnp.cumsum(suffix_lengths)
    request = jnp.sum((index[:, None] >= ends[None, :]).astype(jnp.int32), axis=1)
    onehot = request[:, None] == jnp.arange(suffix_lengths.shape[0], dtype=jnp.int32)[None, :]
    first = jnp.sum(jnp.where(onehot, (ends - suffix_lengths)[None, :], 0), axis=1)
    group = jnp.sum(jnp.where(onehot, request_group[None, :], 0), axis=1)
    return (request, index - first, group)


def shifted(array, axis, by, wrap):
    length = lax.axis_size(axis)
    pairs = [(i, (i + by) % length) for i in range(length) if wrap or i + by < length]
    return lax.ppermute(array, axis, pairs)


def body(
    queries,
    suffix_keys,
    suffix_values,
    prefix_keys,
    prefix_values,
    suffix_lengths,
    request_group,
    block_group,
):
    rows = queries.shape[0]
    kv_cols = suffix_keys.shape[1]
    kv_heads = kv_cols // HD
    q_heads = queries.shape[1] // HD
    repeat = q_heads // kv_heads
    devices = lax.axis_size("seq")
    me = lax.axis_index("seq")
    block_rows = prefix_keys.shape[0]
    prefix_len = block_rows * devices // GROUPS
    span = max(1, min(2048 // rows, devices // 8))
    scale = HD ** (-0.5)
    index = me * rows + jnp.arange(rows, dtype=jnp.int32)
    request, offset, group = token_info(index, suffix_lengths, request_group)

    prefix_kv = jnp.concatenate([prefix_keys, prefix_values], axis=1)
    suffix_kv = jnp.concatenate([suffix_keys, suffix_values], axis=1)

    def rotated_keys(raw, back):
        key_index = (me - back) * rows + jnp.arange(rows, dtype=jnp.int32)
        key_request, key_offset, _ = token_info(key_index, suffix_lengths, request_group)
        k_rot = rotate(raw.reshape(rows, kv_heads, HD), key_offset + prefix_len).reshape(rows, kv_cols)
        return key_index, key_request, k_rot

    if devices <= 16:
        _, own_offset, _ = token_info(index, suffix_lengths, request_group)
        own_k_rot = rotate(suffix_keys.reshape(rows, kv_heads, HD), own_offset + prefix_len).reshape(
            rows, kv_cols
        )
        stacked, both, early_kv = lax.optimization_barrier(
            (
                jnp.stack([own_k_rot, suffix_values], axis=0),
                jnp.concatenate([prefix_kv, suffix_kv], axis=0),
                prefix_kv,
            )
        )
        cache = lax.all_to_all(stacked, "tp", split_axis=1, concat_axis=2, tiled=True)
        received = {}
        late = list(range(span + 1, devices))[: max(0, devices - 1 - 5)]
        for by in range(1, devices):
            if by <= span:
                received[by] = shifted(both, "seq", by, True)
            elif by not in late:
                received[by] = shifted(early_kv, "seq", by, True)
        relay = [devices - i for i in range(1, len(late))]
        if set(relay) & set(late):
            gates = tuple(received[devices - 1 - i] for i in range(len(late)))
            gates, payload = lax.optimization_barrier((gates, prefix_kv))
            for i, by in enumerate(late):
                received[devices - 1 - i] = gates[i]
                received[by] = shifted(payload, "seq", by, True)
            late = []
        order = [by for by in range(1, devices) if by in received]
        data = [prefix_kv] + [received[by] for by in order]
        where_block = {0: (0, 0)}
        for at, by in enumerate(order):
            where_block[by] = (at + 1, 0)
        for back in range(1, min(span, devices - 1) + 1):
            where_block[devices + back - 1] = (order.index(back) + 1, block_rows)
        if late:
            pieces = [prefix_kv] + [received[by] for by in relay]
            gates = tuple(received[by] for by in relay)
            gates, payload = lax.optimization_barrier((gates, jnp.concatenate(pieces, axis=0)))
            data.append(shifted(payload, "seq", late[-1], True))
            for i, by in enumerate(reversed(late)):
                where_block[by] = (len(data) - 1, i * block_rows)
        where_block = tuple(where_block[c] for c in range(devices + min(span, devices - 1)))
        scalars = [me.astype(jnp.int32).reshape(1), suffix_lengths, request_group, block_group]
        meta = (
            devices, block_rows, rows, min(span, devices - 1), prefix_len, repeat, scale, where_block, len(data)
        )
        attended = attend(meta, scalars, queries, suffix_keys, suffix_values, data)
        return (attended, cache[0], cache[1])

    prefix_parts = []
    suffix_parts = [(0, suffix_kv)]
    gathered = lax.all_gather(prefix_kv, "seq", axis=0, tiled=True)
    prefix_parts.append((None, gathered))
    for by in range(1, span + 1):
        suffix_parts.append((by, shifted(suffix_kv, "seq", by, False)))

    position = offset + prefix_len
    q_rot = rotate(queries.reshape(rows, q_heads, HD), position).reshape(rows, kv_heads, repeat, HD)

    key_chunks, value_chunks, visible_chunks = [], [], []
    for holder, kv in prefix_parts:
        count = kv.shape[0]
        if holder is None:
            holder_index = jnp.arange(count, dtype=jnp.int32) // block_rows
            row_group = jnp.take(block_group, holder_index)
            visible = row_group[None, :] == group[:, None]
        else:
            row_group = lax.dynamic_index_in_dim(block_group, holder, keepdims=False)
            visible = jnp.broadcast_to((group == row_group)[:, None], (rows, count))
        key_chunks.append(kv[:, :kv_cols])
        value_chunks.append(kv[:, kv_cols:])
        visible_chunks.append(visible)

    own_k_rot = None
    for back, kv in suffix_parts:
        key_index = (me - back) * rows + jnp.arange(rows, dtype=jnp.int32)
        key_request, key_offset, _ = token_info(key_index, suffix_lengths, request_group)
        k_rot = rotate(kv[:, :kv_cols].reshape(rows, kv_heads, HD), key_offset + prefix_len).reshape(
            rows, kv_cols
        )
        if back == 0:
            own_k_rot = k_rot
        visible = (
            (key_index[None, :] >= 0)
            & (key_request[None, :] == request[:, None])
            & (key_index[None, :] <= index[:, None])
        )
        key_chunks.append(k_rot)
        value_chunks.append(kv[:, kv_cols:])
        visible_chunks.append(visible)

    cache = lax.all_to_all(
        jnp.stack([own_k_rot, suffix_values], axis=0), "tp", split_axis=1, concat_axis=2, tiled=True
    )

    def scores_of(keys, visible):
        keys_split = keys.reshape(keys.shape[0], kv_heads, HD)
        scores = (
            jnp.einsum("bgrd,kgd->bgrk", q_rot, keys_split, preferred_element_type=jnp.float32)
            * scale
        )
        return jnp.where(visible[:, None, None, :], scores, BIG_NEGATIVE)

    def summed_of(scores, high, values, visible):
        weights = jnp.where(visible[:, None, None, :], jnp.exp(scores - high[..., None]), 0.0)
        summed = jnp.einsum(
            "bgrk,kgd->bgrd",
            weights.astype(jnp.bfloat16),
            values.reshape(values.shape[0], kv_heads, HD),
            preferred_element_type=jnp.float32,
        )
        return jnp.sum(weights, axis=-1), summed

    keys = jnp.concatenate(key_chunks, axis=0)
    values = jnp.concatenate(value_chunks, axis=0)
    visible = jnp.concatenate(visible_chunks, axis=1)
    count = keys.shape[0]
    if count * rows * q_heads * 4 <= (8 << 20):
        scores = scores_of(keys, visible)
        high = jnp.max(scores, axis=-1)
        total, summed = summed_of(scores, high, values, visible)
    else:
        width = 512
        steps = count // width
        tail = steps * width
        piece_k = keys[:tail].reshape(steps, width, kv_cols)
        piece_v = values[:tail].reshape(steps, width, kv_cols)
        piece_m = jnp.moveaxis(visible[:, :tail].reshape(rows, steps, width), 1, 0)

        def high_step(high, piece):
            k, m = piece
            return jnp.maximum(high, jnp.max(scores_of(k, m), axis=-1)), None

        high = jnp.max(scores_of(keys[tail:], visible[:, tail:]), axis=-1)
        high, _ = lax.scan(high_step, high, (piece_k, piece_m))

        def sum_step(carry, piece):
            k, v, m = piece
            total, summed = summed_of(scores_of(k, m), high, v, m)
            return (carry[0] + total, carry[1] + summed), None

        start = summed_of(scores_of(keys[tail:], visible[:, tail:]), high, values[tail:], visible[:, tail:])
        (total, summed), _ = lax.scan(sum_step, start, (piece_k, piece_v, piece_m))
    attended = (summed / total[..., None]).reshape(rows, q_heads * HD).astype(jnp.bfloat16)
    return (attended, cache[0], cache[1])


def solution(mesh):
    return jax.shard_map(
        body,
        mesh=mesh,
        in_specs=(
            P("seq", "tp"),
            P("seq", "tp"),
            P("seq", "tp"),
            P("seq", "tp"),
            P("seq", "tp"),
            P(),
            P(),
            P(),
        ),
        out_specs=(P("seq", "tp"), P(("seq", "tp"), None), P(("seq", "tp"), None)),
        check_vma=False,
    )
```

```python
import functools
import math

import jax
import jax.numpy as jnp
from jax import lax
from jax.experimental import pallas as pl
from jax.experimental.pallas import tpu as pltpu
from jax.sharding import PartitionSpec as P

HD = 128
GROUPS = 4


BIG_NEGATIVE = -1e30


def rotate(values, position):
    half = values.shape[-1] // 2
    freq = jnp.exp(
        jnp.arange(half, dtype=jnp.float32) * (-2.0 * math.log(500000.0) / values.shape[-1])
    )
    angle = position.astype(jnp.float32)[:, None] * freq[None, :]
    cosine = jnp.cos(angle)[:, None, :]
    sine = jnp.sin(angle)[:, None, :]
    floats = values.astype(jnp.float32)
    lower = floats[..., :half]
    upper = floats[..., half:]
    return jnp.concatenate(
        [lower * cosine - upper * sine, upper * cosine + lower * sine], axis=-1
    ).astype(jnp.bfloat16)


def attend_kernel(meta, *refs):
    devices, block_rows, rows, tails, prefix_len, repeat, scale, shifts, first, last = meta
    me_ref, lens_ref, rg_ref, bg_ref, q_ref, own_k_ref, own_v_ref = refs[:7]
    data = refs[7 : 7 + len(shifts)]
    rest = refs[7 + len(shifts) :]
    if not first:
        acc_in, high_in, total_in = rest[:3]
        rest = rest[3:]
    if last:
        out_ref, kscr, vscr = rest
    else:
        acc_out, high_out, total_out, kscr, vscr = rest
    kv_cols = kscr.shape[1]
    count = kscr.shape[0]
    base = len(shifts) * block_rows
    q_heads = q_ref.shape[1] // HD
    me = me_ref[0]
    starts, at = [], 0
    for j in range(lens_ref.shape[0]):
        starts.append(at)
        at = at + lens_ref[j]

    def info(index):
        request = jnp.full(index.shape, -2, jnp.int32)
        first_row = jnp.zeros(index.shape, jnp.int32)
        group = jnp.full(index.shape, -1, jnp.int32)
        for j, start in enumerate(starts):
            after = index >= start
            request = jnp.where(after, j, request)
            first_row = jnp.where(after, start, first_row)
            group = jnp.where(after, rg_ref[j], group)
        return request, index - first_row, group

    lane = lax.broadcasted_iota(jnp.int32, (1, HD), 1)
    pair = jnp.where(lane < HD // 2, lane, lane - HD // 2)
    freq = jnp.exp(pair.astype(jnp.float32) * (-2.0 * math.log(500000.0) / HD))
    sign = jnp.where(lane < HD // 2, -1.0, 1.0).astype(jnp.float32)

    def tables(offset):
        angle = (offset + prefix_len).astype(jnp.float32) * freq
        return jnp.cos(angle), jnp.sin(angle) * sign

    def rotated(x, cosine, sine):
        return (x * cosine + pltpu.roll(x, HD // 2, 1) * sine).astype(jnp.bfloat16)

    for c in range(len(shifts)):
        kscr[c * block_rows : (c + 1) * block_rows, :] = data[c][0:block_rows, 0:kv_cols]
        vscr[c * block_rows : (c + 1) * block_rows, :] = data[c][0:block_rows, kv_cols : 2 * kv_cols]
    suffix_blocks = range(tails + 1) if first else range(0)
    for b in suffix_blocks:
        low = base + b * rows
        index = (me - b) * rows + lax.broadcasted_iota(jnp.int32, (rows, 1), 0)
        _, offset, _ = info(index)
        cosine, sine = tables(offset)
        for g in range(kv_cols // HD):
            if b == 0:
                x = own_k_ref[:, g * HD : (g + 1) * HD]
            else:
                x = data[shifts.index(b)][block_rows : block_rows + rows, g * HD : (g + 1) * HD]
            kscr[low : low + rows, g * HD : (g + 1) * HD] = rotated(x.astype(jnp.float32), cosine, sine)
        if b == 0:
            vscr[low : low + rows, :] = own_v_ref[...]
        else:
            vscr[low : low + rows, :] = data[shifts.index(b)][block_rows : block_rows + rows, kv_cols : 2 * kv_cols]

    token = me * rows + lax.broadcasted_iota(jnp.int32, (rows, 1), 0)
    request, offset, group = info(token)
    col = lax.broadcasted_iota(jnp.int32, (1, count), 1)
    key_group = jnp.full((1, count), -1, jnp.int32)
    for c, by in enumerate(shifts):
        holder = lax.rem(me - by + devices, devices)
        key_group = jnp.where(col >= c * block_rows, bg_ref[holder], key_group)
    visible = (col < base) & (key_group == group)
    if first:
        key_index = jnp.full((1, count), -1, jnp.int32)
        for b in suffix_blocks:
            low = base + b * rows
            key_index = jnp.where(col >= low, (me - b) * rows + col - low, key_index)
        key_request, _, _ = info(key_index)
        visible = visible | ((key_request == request) & (key_index <= token))
    cosine, sine = tables(offset)
    for g in range(q_heads // repeat):
        heads = range(g * repeat, (g + 1) * repeat)
        q = jnp.concatenate(
            [rotated(q_ref[:, h * HD : (h + 1) * HD].astype(jnp.float32), cosine, sine) for h in heads],
            axis=0,
        )
        k = kscr[:, g * HD : (g + 1) * HD]
        scores = lax.dot_general(
            q, k, (((1,), (1,)), ((), ())), preferred_element_type=jnp.float32
        ) * scale
        weights, totals, highs, factors = [], [], [], []
        for r, h in enumerate(heads):
            part = jnp.where(visible, scores[r * rows : (r + 1) * rows], BIG_NEGATIVE)
            high = jnp.max(part, axis=1, keepdims=True)
            if not first:
                earlier = high_in[:, h : h + 1]
                high = jnp.maximum(high, earlier)
                factors.append(jnp.exp(earlier - high))
            part = jnp.exp(part - high)
            highs.append(high)
            totals.append(jnp.sum(part, axis=1, keepdims=True))
            weights.append(part.astype(jnp.bfloat16))
        v = vscr[:, g * HD : (g + 1) * HD]
        summed = jnp.dot(jnp.concatenate(weights, axis=0), v, preferred_element_type=jnp.float32)
        for r, h in enumerate(heads):
            part = summed[r * rows : (r + 1) * rows]
            total = totals[r]
            if not first:
                part = acc_in[:, h * HD : (h + 1) * HD] * factors[r] + part
                total = total_in[:, h : h + 1] * factors[r] + total
            if last:
                out_ref[:, h * HD : (h + 1) * HD] = (part / total).astype(out_ref.dtype)
            else:
                acc_out[:, h * HD : (h + 1) * HD] = part
                high_out[:, h : h + 1] = highs[r]
                total_out[:, h : h + 1] = total


def attend(meta, scalars, queries, own_k, own_v, data, partial=None):
    devices, block_rows, rows, tails = meta[:4]
    shifts, first, last = meta[7:]
    kv_cols = own_k.shape[1]
    q_heads = queries.shape[1] // HD
    count = len(shifts) * block_rows + (rows * (1 + tails) if first else 0)
    flops = 4 * rows * count * HD * q_heads
    arrays = [queries, own_k, own_v, *data] + (list(partial) if partial is not None else [])
    nbytes = sum(a.size * a.dtype.itemsize for a in arrays)
    smem = pl.BlockSpec(memory_space=pltpu.SMEM)
    vmem = pl.BlockSpec(memory_space=pltpu.VMEM)
    if last:
        out_shape = jax.ShapeDtypeStruct(queries.shape, jnp.bfloat16)
        out_specs = vmem
    else:
        out_shape = (
            jax.ShapeDtypeStruct(queries.shape, jnp.float32),
            jax.ShapeDtypeStruct((rows, q_heads), jnp.float32),
            jax.ShapeDtypeStruct((rows, q_heads), jnp.float32),
        )
        out_specs = (vmem, vmem, vmem)
    return pl.pallas_call(
        functools.partial(attend_kernel, meta),
        out_shape=out_shape,
        in_specs=[smem] * len(scalars) + [vmem] * len(arrays),
        out_specs=out_specs,
        scratch_shapes=[
            pltpu.VMEM((count, kv_cols), jnp.bfloat16),
            pltpu.VMEM((count, kv_cols), jnp.bfloat16),
        ],
        cost_estimate=pl.CostEstimate(
            flops=flops,
            transcendentals=rows * count * q_heads,
            bytes_accessed=nbytes + queries.size * 2,
        ),
    )(*scalars, *arrays)


def token_info(index, suffix_lengths, request_group):
    ends = jnp.cumsum(suffix_lengths)
    request = jnp.sum((index[:, None] >= ends[None, :]).astype(jnp.int32), axis=1)
    onehot = request[:, None] == jnp.arange(suffix_lengths.shape[0], dtype=jnp.int32)[None, :]
    first = jnp.sum(jnp.where(onehot, (ends - suffix_lengths)[None, :], 0), axis=1)
    group = jnp.sum(jnp.where(onehot, request_group[None, :], 0), axis=1)
    return (request, index - first, group)


def shifted(array, axis, by, wrap):
    length = lax.axis_size(axis)
    pairs = [(i, (i + by) % length) for i in range(length) if wrap or i + by < length]
    return lax.ppermute(array, axis, pairs)


def body(
    queries,
    suffix_keys,
    suffix_values,
    prefix_keys,
    prefix_values,
    suffix_lengths,
    request_group,
    block_group,
):
    rows = queries.shape[0]
    kv_cols = suffix_keys.shape[1]
    kv_heads = kv_cols // HD
    q_heads = queries.shape[1] // HD
    repeat = q_heads // kv_heads
    devices = lax.axis_size("seq")
    me = lax.axis_index("seq")
    block_rows = prefix_keys.shape[0]
    prefix_len = block_rows * devices // GROUPS
    span = max(1, min(2048 // rows, devices // 8))
    scale = HD ** (-0.5)
    index = me * rows + jnp.arange(rows, dtype=jnp.int32)
    request, offset, group = token_info(index, suffix_lengths, request_group)

    prefix_kv = jnp.concatenate([prefix_keys, prefix_values], axis=1)
    suffix_kv = jnp.concatenate([suffix_keys, suffix_values], axis=1)

    def rotated_keys(raw, back):
        key_index = (me - back) * rows + jnp.arange(rows, dtype=jnp.int32)
        key_request, key_offset, _ = token_info(key_index, suffix_lengths, request_group)
        k_rot = rotate(raw.reshape(rows, kv_heads, HD), key_offset + prefix_len).reshape(rows, kv_cols)
        return key_index, key_request, k_rot

    if devices <= 16:
        _, own_offset, _ = token_info(index, suffix_lengths, request_group)
        own_k_rot = rotate(suffix_keys.reshape(rows, kv_heads, HD), own_offset + prefix_len).reshape(
            rows, kv_cols
        )
        stacked, both, early_kv = lax.optimization_barrier(
            (
                jnp.stack([own_k_rot, suffix_values], axis=0),
                jnp.concatenate([prefix_kv, suffix_kv], axis=0),
                prefix_kv,
            )
        )
        cache = lax.all_to_all(stacked, "tp", split_axis=1, concat_axis=2, tiled=True)
        received = {}
        late = list(range(span + 1, devices))[: max(0, devices - 1 - 5)]
        for by in range(1, devices):
            if by <= span:
                received[by] = shifted(both, "seq", by, True)
            elif by not in late:
                received[by] = shifted(early_kv, "seq", by, True)
        gates = tuple(received[devices - 1 - i] for i in range(len(late)))
        gates, payload = lax.optimization_barrier((gates, prefix_kv))
        for i, by in enumerate(late):
            received[devices - 1 - i] = gates[i]
            received[by] = shifted(payload, "seq", by, True)
        received[0] = prefix_kv
        scalars = [me.astype(jnp.int32).reshape(1), suffix_lengths, request_group, block_group]
        tails = min(span, devices - 1)
        common = (devices, block_rows, rows, tails, prefix_len, repeat, scale)
        shifts = tuple(by for by in range(devices) if by not in late)
        if late:
            partial = attend(
                common + (shifts, True, False), scalars, queries, suffix_keys, suffix_values,
                [received[by] for by in shifts],
            )
            attended = attend(
                common + (tuple(late), False, True), scalars, queries, suffix_keys, suffix_values,
                [received[by] for by in late], partial,
            )
        else:
            attended = attend(
                common + (shifts, True, True), scalars, queries, suffix_keys, suffix_values,
                [received[by] for by in shifts],
            )
        return (attended, cache[0], cache[1])

    prefix_parts = []
    suffix_parts = [(0, suffix_kv)]
    gathered = lax.all_gather(prefix_kv, "seq", axis=0, tiled=True)
    prefix_parts.append((None, gathered))
    for by in range(1, span + 1):
        suffix_parts.append((by, shifted(suffix_kv, "seq", by, False)))

    position = offset + prefix_len
    q_rot = rotate(queries.reshape(rows, q_heads, HD), position).reshape(rows, kv_heads, repeat, HD)

    key_chunks, value_chunks, visible_chunks = [], [], []
    for holder, kv in prefix_parts:
        count = kv.shape[0]
        if holder is None:
            holder_index = jnp.arange(count, dtype=jnp.int32) // block_rows
            row_group = jnp.take(block_group, holder_index)
            visible = row_group[None, :] == group[:, None]
        else:
            row_group = lax.dynamic_index_in_dim(block_group, holder, keepdims=False)
            visible = jnp.broadcast_to((group == row_group)[:, None], (rows, count))
        key_chunks.append(kv[:, :kv_cols])
        value_chunks.append(kv[:, kv_cols:])
        visible_chunks.append(visible)

    own_k_rot = None
    for back, kv in suffix_parts:
        key_index = (me - back) * rows + jnp.arange(rows, dtype=jnp.int32)
        key_request, key_offset, _ = token_info(key_index, suffix_lengths, request_group)
        k_rot = rotate(kv[:, :kv_cols].reshape(rows, kv_heads, HD), key_offset + prefix_len).reshape(
            rows, kv_cols
        )
        if back == 0:
            own_k_rot = k_rot
        visible = (
            (key_index[None, :] >= 0)
            & (key_request[None, :] == request[:, None])
            & (key_index[None, :] <= index[:, None])
        )
        key_chunks.append(k_rot)
        value_chunks.append(kv[:, kv_cols:])
        visible_chunks.append(visible)

    cache = lax.all_to_all(
        jnp.stack([own_k_rot, suffix_values], axis=0), "tp", split_axis=1, concat_axis=2, tiled=True
    )

    def scores_of(keys, visible):
        keys_split = keys.reshape(keys.shape[0], kv_heads, HD)
        scores = (
            jnp.einsum("bgrd,kgd->bgrk", q_rot, keys_split, preferred_element_type=jnp.float32)
            * scale
        )
        return jnp.where(visible[:, None, None, :], scores, BIG_NEGATIVE)

    def summed_of(scores, high, values, visible):
        weights = jnp.where(visible[:, None, None, :], jnp.exp(scores - high[..., None]), 0.0)
        summed = jnp.einsum(
            "bgrk,kgd->bgrd",
            weights.astype(jnp.bfloat16),
            values.reshape(values.shape[0], kv_heads, HD),
            preferred_element_type=jnp.float32,
        )
        return jnp.sum(weights, axis=-1), summed

    keys = jnp.concatenate(key_chunks, axis=0)
    values = jnp.concatenate(value_chunks, axis=0)
    visible = jnp.concatenate(visible_chunks, axis=1)
    count = keys.shape[0]
    if count * rows * q_heads * 4 <= (8 << 20):
        scores = scores_of(keys, visible)
        high = jnp.max(scores, axis=-1)
        total, summed = summed_of(scores, high, values, visible)
    else:
        width = 512
        steps = count // width
        tail = steps * width
        piece_k = keys[:tail].reshape(steps, width, kv_cols)
        piece_v = values[:tail].reshape(steps, width, kv_cols)
        piece_m = jnp.moveaxis(visible[:, :tail].reshape(rows, steps, width), 1, 0)

        def high_step(high, piece):
            k, m = piece
            return jnp.maximum(high, jnp.max(scores_of(k, m), axis=-1)), None

        high = jnp.max(scores_of(keys[tail:], visible[:, tail:]), axis=-1)
        high, _ = lax.scan(high_step, high, (piece_k, piece_m))

        def sum_step(carry, piece):
            k, v, m = piece
            total, summed = summed_of(scores_of(k, m), high, v, m)
            return (carry[0] + total, carry[1] + summed), None

        start = summed_of(scores_of(keys[tail:], visible[:, tail:]), high, values[tail:], visible[:, tail:])
        (total, summed), _ = lax.scan(sum_step, start, (piece_k, piece_v, piece_m))
    attended = (summed / total[..., None]).reshape(rows, q_heads * HD).astype(jnp.bfloat16)
    return (attended, cache[0], cache[1])


def solution(mesh):
    return jax.shard_map(
        body,
        mesh=mesh,
        in_specs=(
            P("seq", "tp"),
            P("seq", "tp"),
            P("seq", "tp"),
            P("seq", "tp"),
            P("seq", "tp"),
            P(),
            P(),
            P(),
        ),
        out_specs=(P("seq", "tp"), P(("seq", "tp"), None), P(("seq", "tp"), None)),
        check_vma=False,
    )
```

```python
import functools
import math

import jax
import jax.numpy as jnp
from jax import lax
from jax.experimental import pallas as pl
from jax.experimental.pallas import tpu as pltpu
from jax.sharding import PartitionSpec as P

HD = 128
GROUPS = 4


BIG_NEGATIVE = -1e30


def rotate(values, position):
    half = values.shape[-1] // 2
    freq = jnp.exp(
        jnp.arange(half, dtype=jnp.float32) * (-2.0 * math.log(500000.0) / values.shape[-1])
    )
    angle = position.astype(jnp.float32)[:, None] * freq[None, :]
    cosine = jnp.cos(angle)[:, None, :]
    sine = jnp.sin(angle)[:, None, :]
    floats = values.astype(jnp.float32)
    lower = floats[..., :half]
    upper = floats[..., half:]
    return jnp.concatenate(
        [lower * cosine - upper * sine, upper * cosine + lower * sine], axis=-1
    ).astype(jnp.bfloat16)


def attend_kernel(meta, *refs):
    devices, block_rows, rows, tails, prefix_len, repeat, scale = meta
    me_ref, lens_ref, rg_ref, bg_ref, q_ref, own_k_ref, own_v_ref = refs[:7]
    data = refs[7 : 7 + devices]
    out_ref, kscr, vscr = refs[7 + devices :]
    kv_cols = kscr.shape[1]
    count = kscr.shape[0]
    base = devices * block_rows
    q_heads = q_ref.shape[1] // HD
    me = me_ref[0]
    reqs = lens_ref.shape[0]
    width = -(-reqs // HD) * HD
    height = -(-reqs // 8) * 8
    never = 1 << 30
    lane = lax.broadcasted_iota(jnp.int32, (1, width), 1)
    sub = lax.broadcasted_iota(jnp.int32, (height, 1), 0)
    start_row = jnp.full((1, width), never, jnp.int32)
    group_row = jnp.zeros((1, width), jnp.int32)
    start_col = jnp.full((height, 1), never, jnp.int32)
    at = 0
    for j in range(reqs):
        start_row = jnp.where(lane == j, at, start_row)
        group_row = jnp.where(lane == j, rg_ref[j], group_row)
        start_col = jnp.where(sub == j, at, start_col)
        at = at + lens_ref[j]

    def info(index):
        after = index >= start_row
        request = jnp.sum(after.astype(jnp.float32), axis=1, keepdims=True).astype(jnp.int32) - 1
        first = jnp.max(jnp.where(after, start_row, 0).astype(jnp.float32), axis=1, keepdims=True)
        group = jnp.sum(
            jnp.where(lane == request, group_row, 0).astype(jnp.float32), axis=1, keepdims=True
        )
        return request, index - first.astype(jnp.int32), group.astype(jnp.int32)

    def request_of_row(index):
        after = index >= start_col
        return jnp.sum(after.astype(jnp.float32), axis=0, keepdims=True).astype(jnp.int32) - 1

    head_lane = lax.broadcasted_iota(jnp.int32, (1, HD), 1)
    pair = jnp.where(head_lane < HD // 2, head_lane, head_lane - HD // 2)
    freq = jnp.exp(pair.astype(jnp.float32) * (-2.0 * math.log(500000.0) / HD))
    sign = jnp.where(head_lane < HD // 2, -1.0, 1.0).astype(jnp.float32)

    def tables(offset):
        angle = (offset + prefix_len).astype(jnp.float32) * freq
        return jnp.cos(angle), jnp.sin(angle) * sign

    def rotated(x, cosine, sine):
        return (x * cosine + pltpu.roll(x, HD // 2, 1) * sine).astype(jnp.bfloat16)

    for c in range(devices):
        kscr[c * block_rows : (c + 1) * block_rows, :] = data[c][0:block_rows, 0:kv_cols]
        vscr[c * block_rows : (c + 1) * block_rows, :] = data[c][0:block_rows, kv_cols : 2 * kv_cols]
    for b in range(0, tails + 1):
        low = base + b * rows
        index = (me - b) * rows + lax.broadcasted_iota(jnp.int32, (rows, 1), 0)
        _, offset, _ = info(index)
        cosine, sine = tables(offset)
        for g in range(kv_cols // HD):
            if b == 0:
                x = own_k_ref[:, g * HD : (g + 1) * HD]
            else:
                x = data[b][block_rows : block_rows + rows, g * HD : (g + 1) * HD]
            kscr[low : low + rows, g * HD : (g + 1) * HD] = rotated(x.astype(jnp.float32), cosine, sine)
        if b == 0:
            vscr[low : low + rows, :] = own_v_ref[...]
        else:
            vscr[low : low + rows, :] = data[b][block_rows : block_rows + rows, kv_cols : 2 * kv_cols]

    token = me * rows + lax.broadcasted_iota(jnp.int32, (rows, 1), 0)
    request, offset, group = info(token)
    col = lax.broadcasted_iota(jnp.int32, (1, count), 1)
    key_group = jnp.full((1, count), -1, jnp.int32)
    for c in range(devices):
        holder = lax.rem(me - c + devices, devices)
        key_group = jnp.where(col >= c * block_rows, bg_ref[holder], key_group)
    key_index = jnp.full((1, count), -1, jnp.int32)
    for b in range(tails + 1):
        low = base + b * rows
        key_index = jnp.where(col >= low, (me - b) * rows + col - low, key_index)
    key_request = request_of_row(key_index)
    visible = ((col < base) & (key_group == group)) | (
        (key_request == request) & (key_index <= token)
    )
    cosine, sine = tables(offset)
    for g in range(q_heads // repeat):
        heads = range(g * repeat, (g + 1) * repeat)
        q = jnp.concatenate(
            [rotated(q_ref[:, h * HD : (h + 1) * HD].astype(jnp.float32), cosine, sine) for h in heads],
            axis=0,
        )
        k = kscr[:, g * HD : (g + 1) * HD]
        scores = lax.dot_general(
            q, k, (((1,), (1,)), ((), ())), preferred_element_type=jnp.float32
        ) * scale
        weights, totals = [], []
        for r in range(repeat):
            part = jnp.where(visible, scores[r * rows : (r + 1) * rows], BIG_NEGATIVE)
            high = jnp.max(part, axis=1, keepdims=True)
            part = jnp.exp(part - high)
            totals.append(jnp.sum(part, axis=1, keepdims=True))
            weights.append(part.astype(jnp.bfloat16))
        v = vscr[:, g * HD : (g + 1) * HD]
        summed = jnp.dot(jnp.concatenate(weights, axis=0), v, preferred_element_type=jnp.float32)
        for r, h in enumerate(heads):
            out_ref[:, h * HD : (h + 1) * HD] = (summed[r * rows : (r + 1) * rows] / totals[r]).astype(
                out_ref.dtype
            )


def attend(meta, scalars, queries, own_k, own_v, data):
    devices, block_rows, rows, tails = meta[:4]
    kv_cols = own_k.shape[1]
    q_heads = queries.shape[1] // HD
    count = devices * block_rows + rows * (1 + tails)
    flops = 4 * rows * count * HD * q_heads
    arrays = [queries, own_k, own_v, *data]
    nbytes = sum(a.size * a.dtype.itemsize for a in arrays)
    smem = pl.BlockSpec(memory_space=pltpu.SMEM)
    vmem = pl.BlockSpec(memory_space=pltpu.VMEM)
    return pl.pallas_call(
        functools.partial(attend_kernel, meta),
        out_shape=jax.ShapeDtypeStruct(queries.shape, jnp.bfloat16),
        in_specs=[smem] * len(scalars) + [vmem] * len(arrays),
        out_specs=vmem,
        scratch_shapes=[
            pltpu.VMEM((count, kv_cols), jnp.bfloat16),
            pltpu.VMEM((count, kv_cols), jnp.bfloat16),
        ],
        cost_estimate=pl.CostEstimate(
            flops=flops,
            transcendentals=rows * count * q_heads,
            bytes_accessed=nbytes + queries.size * 2,
        ),
    )(*scalars, *arrays)


def token_info(index, suffix_lengths, request_group):
    ends = jnp.cumsum(suffix_lengths)
    request = jnp.sum((index[:, None] >= ends[None, :]).astype(jnp.int32), axis=1)
    onehot = request[:, None] == jnp.arange(suffix_lengths.shape[0], dtype=jnp.int32)[None, :]
    first = jnp.sum(jnp.where(onehot, (ends - suffix_lengths)[None, :], 0), axis=1)
    group = jnp.sum(jnp.where(onehot, request_group[None, :], 0), axis=1)
    return (request, index - first, group)


def shifted(array, axis, by, wrap):
    length = lax.axis_size(axis)
    pairs = [(i, (i + by) % length) for i in range(length) if wrap or i + by < length]
    return lax.ppermute(array, axis, pairs)


def body(
    queries,
    suffix_keys,
    suffix_values,
    prefix_keys,
    prefix_values,
    suffix_lengths,
    request_group,
    block_group,
):
    rows = queries.shape[0]
    kv_cols = suffix_keys.shape[1]
    kv_heads = kv_cols // HD
    q_heads = queries.shape[1] // HD
    repeat = q_heads // kv_heads
    devices = lax.axis_size("seq")
    me = lax.axis_index("seq")
    block_rows = prefix_keys.shape[0]
    prefix_len = block_rows * devices // GROUPS
    span = max(1, min(2048 // rows, devices // 8))
    scale = HD ** (-0.5)
    index = me * rows + jnp.arange(rows, dtype=jnp.int32)
    request, offset, group = token_info(index, suffix_lengths, request_group)

    prefix_kv = jnp.concatenate([prefix_keys, prefix_values], axis=1)
    suffix_kv = jnp.concatenate([suffix_keys, suffix_values], axis=1)

    def rotated_keys(raw, back):
        key_index = (me - back) * rows + jnp.arange(rows, dtype=jnp.int32)
        key_request, key_offset, _ = token_info(key_index, suffix_lengths, request_group)
        k_rot = rotate(raw.reshape(rows, kv_heads, HD), key_offset + prefix_len).reshape(rows, kv_cols)
        return key_index, key_request, k_rot

    if devices <= 16:
        _, own_offset, _ = token_info(index, suffix_lengths, request_group)
        own_k_rot = rotate(suffix_keys.reshape(rows, kv_heads, HD), own_offset + prefix_len).reshape(
            rows, kv_cols
        )
        stacked, both, early_kv = lax.optimization_barrier(
            (
                jnp.stack([own_k_rot, suffix_values], axis=0),
                jnp.concatenate([prefix_kv, suffix_kv], axis=0),
                prefix_kv,
            )
        )
        cache = lax.all_to_all(stacked, "tp", split_axis=1, concat_axis=2, tiled=True)
        received = {}
        late = list(range(span + 1, devices))[: max(0, devices - 1 - 5)]
        for by in range(1, devices):
            if by <= span:
                received[by] = shifted(both, "seq", by, True)
            elif by not in late:
                received[by] = shifted(early_kv, "seq", by, True)
        gates = tuple(received[devices - 1 - i] for i in range(len(late)))
        gates, payload = lax.optimization_barrier((gates, prefix_kv))
        for i, by in enumerate(late):
            received[devices - 1 - i] = gates[i]
            received[by] = shifted(payload, "seq", by, True)
        data = [prefix_kv] + [received[by] for by in range(1, devices)]
        scalars = [me.astype(jnp.int32).reshape(1), suffix_lengths, request_group, block_group]
        meta = (devices, block_rows, rows, min(span, devices - 1), prefix_len, repeat, scale)
        attended = attend(meta, scalars, queries, suffix_keys, suffix_values, data)
        return (attended, cache[0], cache[1])

    prefix_parts = []
    suffix_parts = [(0, suffix_kv)]
    gathered = lax.all_gather(prefix_kv, "seq", axis=0, tiled=True)
    prefix_parts.append((None, gathered))
    for by in range(1, span + 1):
        suffix_parts.append((by, shifted(suffix_kv, "seq", by, False)))

    position = offset + prefix_len
    q_rot = rotate(queries.reshape(rows, q_heads, HD), position).reshape(rows, kv_heads, repeat, HD)

    key_chunks, value_chunks, visible_chunks = [], [], []
    for holder, kv in prefix_parts:
        count = kv.shape[0]
        if holder is None:
            holder_index = jnp.arange(count, dtype=jnp.int32) // block_rows
            row_group = jnp.take(block_group, holder_index)
            visible = row_group[None, :] == group[:, None]
        else:
            row_group = lax.dynamic_index_in_dim(block_group, holder, keepdims=False)
            visible = jnp.broadcast_to((group == row_group)[:, None], (rows, count))
        key_chunks.append(kv[:, :kv_cols])
        value_chunks.append(kv[:, kv_cols:])
        visible_chunks.append(visible)

    own_k_rot = None
    for back, kv in suffix_parts:
        key_index = (me - back) * rows + jnp.arange(rows, dtype=jnp.int32)
        key_request, key_offset, _ = token_info(key_index, suffix_lengths, request_group)
        k_rot = rotate(kv[:, :kv_cols].reshape(rows, kv_heads, HD), key_offset + prefix_len).reshape(
            rows, kv_cols
        )
        if back == 0:
            own_k_rot = k_rot
        visible = (
            (key_index[None, :] >= 0)
            & (key_request[None, :] == request[:, None])
            & (key_index[None, :] <= index[:, None])
        )
        key_chunks.append(k_rot)
        value_chunks.append(kv[:, kv_cols:])
        visible_chunks.append(visible)

    cache = lax.all_to_all(
        jnp.stack([own_k_rot, suffix_values], axis=0), "tp", split_axis=1, concat_axis=2, tiled=True
    )

    def scores_of(keys, visible):
        keys_split = keys.reshape(keys.shape[0], kv_heads, HD)
        scores = (
            jnp.einsum("bgrd,kgd->bgrk", q_rot, keys_split, preferred_element_type=jnp.float32)
            * scale
        )
        return jnp.where(visible[:, None, None, :], scores, BIG_NEGATIVE)

    def summed_of(scores, high, values, visible):
        weights = jnp.where(visible[:, None, None, :], jnp.exp(scores - high[..., None]), 0.0)
        summed = jnp.einsum(
            "bgrk,kgd->bgrd",
            weights.astype(jnp.bfloat16),
            values.reshape(values.shape[0], kv_heads, HD),
            preferred_element_type=jnp.float32,
        )
        return jnp.sum(weights, axis=-1), summed

    keys = jnp.concatenate(key_chunks, axis=0)
    values = jnp.concatenate(value_chunks, axis=0)
    visible = jnp.concatenate(visible_chunks, axis=1)
    count = keys.shape[0]
    if count * rows * q_heads * 4 <= (8 << 20):
        scores = scores_of(keys, visible)
        high = jnp.max(scores, axis=-1)
        total, summed = summed_of(scores, high, values, visible)
    else:
        width = 512
        steps = count // width
        tail = steps * width
        piece_k = keys[:tail].reshape(steps, width, kv_cols)
        piece_v = values[:tail].reshape(steps, width, kv_cols)
        piece_m = jnp.moveaxis(visible[:, :tail].reshape(rows, steps, width), 1, 0)

        def high_step(high, piece):
            k, m = piece
            return jnp.maximum(high, jnp.max(scores_of(k, m), axis=-1)), None

        high = jnp.max(scores_of(keys[tail:], visible[:, tail:]), axis=-1)
        high, _ = lax.scan(high_step, high, (piece_k, piece_m))

        def sum_step(carry, piece):
            k, v, m = piece
            total, summed = summed_of(scores_of(k, m), high, v, m)
            return (carry[0] + total, carry[1] + summed), None

        start = summed_of(scores_of(keys[tail:], visible[:, tail:]), high, values[tail:], visible[:, tail:])
        (total, summed), _ = lax.scan(sum_step, start, (piece_k, piece_v, piece_m))
    attended = (summed / total[..., None]).reshape(rows, q_heads * HD).astype(jnp.bfloat16)
    return (attended, cache[0], cache[1])


def solution(mesh):
    return jax.shard_map(
        body,
        mesh=mesh,
        in_specs=(
            P("seq", "tp"),
            P("seq", "tp"),
            P("seq", "tp"),
            P("seq", "tp"),
            P("seq", "tp"),
            P(),
            P(),
            P(),
        ),
        out_specs=(P("seq", "tp"), P(("seq", "tp"), None), P(("seq", "tp"), None)),
        check_vma=False,
    )
```

```python
import functools
import math

import jax
import jax.numpy as jnp
from jax import lax
from jax.experimental import pallas as pl
from jax.experimental.pallas import tpu as pltpu
from jax.sharding import PartitionSpec as P

HD = 128
GROUPS = 4


BIG_NEGATIVE = -1e30


def rotate(values, position):
    half = values.shape[-1] // 2
    freq = jnp.exp(
        jnp.arange(half, dtype=jnp.float32) * (-2.0 * math.log(500000.0) / values.shape[-1])
    )
    angle = position.astype(jnp.float32)[:, None] * freq[None, :]
    cosine = jnp.cos(angle)[:, None, :]
    sine = jnp.sin(angle)[:, None, :]
    floats = values.astype(jnp.float32)
    lower = floats[..., :half]
    upper = floats[..., half:]
    return jnp.concatenate(
        [lower * cosine - upper * sine, upper * cosine + lower * sine], axis=-1
    ).astype(jnp.bfloat16)


def attend_kernel(meta, *refs):
    devices, block_rows, rows, tails, prefix_len, repeat, scale = meta
    me_ref, lens_ref, rg_ref, bg_ref, q_ref, own_k_ref, own_v_ref = refs[:7]
    data = refs[7 : 7 + devices]
    out_ref, kscr, vscr = refs[7 + devices :]
    kv_cols = kscr.shape[1]
    count = kscr.shape[0]
    base = devices * block_rows
    q_heads = q_ref.shape[1] // HD
    me = me_ref[0]
    reqs = lens_ref.shape[0]
    width = -(-reqs // HD) * HD
    height = -(-reqs // 8) * 8
    never = 1 << 30
    lane = lax.broadcasted_iota(jnp.int32, (1, width), 1)
    sub = lax.broadcasted_iota(jnp.int32, (height, 1), 0)
    start_row = jnp.full((1, width), never, jnp.int32)
    group_row = jnp.zeros((1, width), jnp.int32)
    start_col = jnp.full((height, 1), never, jnp.int32)
    at = 0
    for j in range(reqs):
        start_row = jnp.where(lane == j, at, start_row)
        group_row = jnp.where(lane == j, rg_ref[j], group_row)
        start_col = jnp.where(sub == j, at, start_col)
        at = at + lens_ref[j]

    def info(index):
        after = index >= start_row
        request = jnp.sum(after.astype(jnp.float32), axis=1, keepdims=True).astype(jnp.int32) - 1
        first = jnp.max(jnp.where(after, start_row, 0).astype(jnp.float32), axis=1, keepdims=True)
        group = jnp.sum(
            jnp.where(lane == request, group_row, 0).astype(jnp.float32), axis=1, keepdims=True
        )
        return request, index - first.astype(jnp.int32), group.astype(jnp.int32)

    def request_of_row(index):
        after = index >= start_col
        return jnp.sum(after.astype(jnp.float32), axis=0, keepdims=True).astype(jnp.int32) - 1

    head_lane = lax.broadcasted_iota(jnp.int32, (1, HD), 1)
    pair = jnp.where(head_lane < HD // 2, head_lane, head_lane - HD // 2)
    freq = jnp.exp(pair.astype(jnp.float32) * (-2.0 * math.log(500000.0) / HD))
    sign = jnp.where(head_lane < HD // 2, -1.0, 1.0).astype(jnp.float32)

    def tables(offset):
        angle = (offset + prefix_len).astype(jnp.float32) * freq
        return jnp.cos(angle), jnp.sin(angle) * sign

    def rotated(x, cosine, sine):
        return (x * cosine + pltpu.roll(x, HD // 2, 1) * sine).astype(jnp.bfloat16)

    for c in range(devices):
        kscr[c * block_rows : (c + 1) * block_rows, :] = data[c][0:block_rows, 0:kv_cols]
        vscr[c * block_rows : (c + 1) * block_rows, :] = data[c][0:block_rows, kv_cols : 2 * kv_cols]
    for b in range(0, tails + 1):
        low = base + b * rows
        index = (me - b) * rows + lax.broadcasted_iota(jnp.int32, (rows, 1), 0)
        _, offset, _ = info(index)
        cosine, sine = tables(offset)
        for g in range(kv_cols // HD):
            if b == 0:
                x = own_k_ref[:, g * HD : (g + 1) * HD]
            else:
                x = data[b][block_rows : block_rows + rows, g * HD : (g + 1) * HD]
            kscr[low : low + rows, g * HD : (g + 1) * HD] = rotated(x.astype(jnp.float32), cosine, sine)
        if b == 0:
            vscr[low : low + rows, :] = own_v_ref[...]
        else:
            vscr[low : low + rows, :] = data[b][block_rows : block_rows + rows, kv_cols : 2 * kv_cols]

    token = me * rows + lax.broadcasted_iota(jnp.int32, (rows, 1), 0)
    request, offset, group = info(token)
    col = lax.broadcasted_iota(jnp.int32, (1, count), 1)
    key_group = jnp.full((1, count), -1, jnp.int32)
    for c in range(devices):
        holder = lax.rem(me - c + devices, devices)
        key_group = jnp.where(col >= c * block_rows, bg_ref[holder], key_group)
    key_index = jnp.full((1, count), -1, jnp.int32)
    for b in range(tails + 1):
        low = base + b * rows
        key_index = jnp.where(col >= low, (me - b) * rows + col - low, key_index)
    key_request = request_of_row(key_index)
    visible = ((col < base) & (key_group == group)) | (
        (key_request == request) & (key_index <= token)
    )
    cosine, sine = tables(offset)
    for g in range(q_heads // repeat):
        heads = range(g * repeat, (g + 1) * repeat)
        q = jnp.concatenate(
            [rotated(q_ref[:, h * HD : (h + 1) * HD].astype(jnp.float32), cosine, sine) for h in heads],
            axis=0,
        )
        k = kscr[:, g * HD : (g + 1) * HD]
        scores = lax.dot_general(
            q, k, (((1,), (1,)), ((), ())), preferred_element_type=jnp.float32
        )
        weights, totals = [], []
        for r in range(repeat):
            part = jnp.where(visible, scores[r * rows : (r + 1) * rows], BIG_NEGATIVE)
            high = jnp.max(part, axis=1, keepdims=True)
            part = jnp.exp2((part - high) * (scale * math.log2(math.e)))
            totals.append(jnp.sum(part, axis=1, keepdims=True))
            weights.append(part.astype(jnp.bfloat16))
        v = vscr[:, g * HD : (g + 1) * HD]
        summed = jnp.dot(jnp.concatenate(weights, axis=0), v, preferred_element_type=jnp.float32)
        for r, h in enumerate(heads):
            out_ref[:, h * HD : (h + 1) * HD] = (summed[r * rows : (r + 1) * rows] / totals[r]).astype(
                out_ref.dtype
            )


def attend(meta, scalars, queries, own_k, own_v, data):
    devices, block_rows, rows, tails = meta[:4]
    kv_cols = own_k.shape[1]
    q_heads = queries.shape[1] // HD
    count = devices * block_rows + rows * (1 + tails)
    flops = 4 * rows * count * HD * q_heads
    arrays = [queries, own_k, own_v, *data]
    nbytes = sum(a.size * a.dtype.itemsize for a in arrays)
    smem = pl.BlockSpec(memory_space=pltpu.SMEM)
    vmem = pl.BlockSpec(memory_space=pltpu.VMEM)
    return pl.pallas_call(
        functools.partial(attend_kernel, meta),
        out_shape=jax.ShapeDtypeStruct(queries.shape, jnp.bfloat16),
        in_specs=[smem] * len(scalars) + [vmem] * len(arrays),
        out_specs=vmem,
        scratch_shapes=[
            pltpu.VMEM((count, kv_cols), jnp.bfloat16),
            pltpu.VMEM((count, kv_cols), jnp.bfloat16),
        ],
        cost_estimate=pl.CostEstimate(
            flops=flops,
            transcendentals=rows * count * q_heads,
            bytes_accessed=nbytes + queries.size * 2,
        ),
    )(*scalars, *arrays)


def token_info(index, suffix_lengths, request_group):
    ends = jnp.cumsum(suffix_lengths)
    request = jnp.sum((index[:, None] >= ends[None, :]).astype(jnp.int32), axis=1)
    onehot = request[:, None] == jnp.arange(suffix_lengths.shape[0], dtype=jnp.int32)[None, :]
    first = jnp.sum(jnp.where(onehot, (ends - suffix_lengths)[None, :], 0), axis=1)
    group = jnp.sum(jnp.where(onehot, request_group[None, :], 0), axis=1)
    return (request, index - first, group)


def shifted(array, axis, by, wrap):
    length = lax.axis_size(axis)
    pairs = [(i, (i + by) % length) for i in range(length) if wrap or i + by < length]
    return lax.ppermute(array, axis, pairs)


def body(
    queries,
    suffix_keys,
    suffix_values,
    prefix_keys,
    prefix_values,
    suffix_lengths,
    request_group,
    block_group,
):
    rows = queries.shape[0]
    kv_cols = suffix_keys.shape[1]
    kv_heads = kv_cols // HD
    q_heads = queries.shape[1] // HD
    repeat = q_heads // kv_heads
    devices = lax.axis_size("seq")
    me = lax.axis_index("seq")
    block_rows = prefix_keys.shape[0]
    prefix_len = block_rows * devices // GROUPS
    span = max(1, min(2048 // rows, devices // 8))
    scale = HD ** (-0.5)
    index = me * rows + jnp.arange(rows, dtype=jnp.int32)
    request, offset, group = token_info(index, suffix_lengths, request_group)

    prefix_kv = jnp.concatenate([prefix_keys, prefix_values], axis=1)
    suffix_kv = jnp.concatenate([suffix_keys, suffix_values], axis=1)

    def rotated_keys(raw, back):
        key_index = (me - back) * rows + jnp.arange(rows, dtype=jnp.int32)
        key_request, key_offset, _ = token_info(key_index, suffix_lengths, request_group)
        k_rot = rotate(raw.reshape(rows, kv_heads, HD), key_offset + prefix_len).reshape(rows, kv_cols)
        return key_index, key_request, k_rot

    if devices <= 16:
        _, own_offset, _ = token_info(index, suffix_lengths, request_group)
        own_k_rot = rotate(suffix_keys.reshape(rows, kv_heads, HD), own_offset + prefix_len).reshape(
            rows, kv_cols
        )
        stacked, both, early_kv = lax.optimization_barrier(
            (
                jnp.stack([own_k_rot, suffix_values], axis=0),
                jnp.concatenate([prefix_kv, suffix_kv], axis=0),
                prefix_kv,
            )
        )
        cache = lax.all_to_all(stacked, "tp", split_axis=1, concat_axis=2, tiled=True)
        received = {}
        late = list(range(span + 1, devices))[: max(0, devices - 1 - 5)]
        for by in range(1, devices):
            if by <= span:
                received[by] = shifted(both, "seq", by, True)
            elif by not in late:
                received[by] = shifted(early_kv, "seq", by, True)
        gates = tuple(received[devices - 1 - i] for i in range(len(late)))
        gates, payload = lax.optimization_barrier((gates, prefix_kv))
        for i, by in enumerate(late):
            received[devices - 1 - i] = gates[i]
            received[by] = shifted(payload, "seq", by, True)
        data = [prefix_kv] + [received[by] for by in range(1, devices)]
        scalars = [me.astype(jnp.int32).reshape(1), suffix_lengths, request_group, block_group]
        meta = (devices, block_rows, rows, min(span, devices - 1), prefix_len, repeat, scale)
        attended = attend(meta, scalars, queries, suffix_keys, suffix_values, data)
        return (attended, cache[0], cache[1])

    prefix_parts = []
    suffix_parts = [(0, suffix_kv)]
    gathered = lax.all_gather(prefix_kv, "seq", axis=0, tiled=True)
    prefix_parts.append((None, gathered))
    for by in range(1, span + 1):
        suffix_parts.append((by, shifted(suffix_kv, "seq", by, False)))

    position = offset + prefix_len
    q_rot = rotate(queries.reshape(rows, q_heads, HD), position).reshape(rows, kv_heads, repeat, HD)

    key_chunks, value_chunks, visible_chunks = [], [], []
    for holder, kv in prefix_parts:
        count = kv.shape[0]
        if holder is None:
            holder_index = jnp.arange(count, dtype=jnp.int32) // block_rows
            row_group = jnp.take(block_group, holder_index)
            visible = row_group[None, :] == group[:, None]
        else:
            row_group = lax.dynamic_index_in_dim(block_group, holder, keepdims=False)
            visible = jnp.broadcast_to((group == row_group)[:, None], (rows, count))
        key_chunks.append(kv[:, :kv_cols])
        value_chunks.append(kv[:, kv_cols:])
        visible_chunks.append(visible)

    own_k_rot = None
    for back, kv in suffix_parts:
        key_index = (me - back) * rows + jnp.arange(rows, dtype=jnp.int32)
        key_request, key_offset, _ = token_info(key_index, suffix_lengths, request_group)
        k_rot = rotate(kv[:, :kv_cols].reshape(rows, kv_heads, HD), key_offset + prefix_len).reshape(
            rows, kv_cols
        )
        if back == 0:
            own_k_rot = k_rot
        visible = (
            (key_index[None, :] >= 0)
            & (key_request[None, :] == request[:, None])
            & (key_index[None, :] <= index[:, None])
        )
        key_chunks.append(k_rot)
        value_chunks.append(kv[:, kv_cols:])
        visible_chunks.append(visible)

    cache = lax.all_to_all(
        jnp.stack([own_k_rot, suffix_values], axis=0), "tp", split_axis=1, concat_axis=2, tiled=True
    )

    def scores_of(keys, visible):
        keys_split = keys.reshape(keys.shape[0], kv_heads, HD)
        scores = (
            jnp.einsum("bgrd,kgd->bgrk", q_rot, keys_split, preferred_element_type=jnp.float32)
            * scale
        )
        return jnp.where(visible[:, None, None, :], scores, BIG_NEGATIVE)

    def summed_of(scores, high, values, visible):
        weights = jnp.where(visible[:, None, None, :], jnp.exp(scores - high[..., None]), 0.0)
        summed = jnp.einsum(
            "bgrk,kgd->bgrd",
            weights.astype(jnp.bfloat16),
            values.reshape(values.shape[0], kv_heads, HD),
            preferred_element_type=jnp.float32,
        )
        return jnp.sum(weights, axis=-1), summed

    keys = jnp.concatenate(key_chunks, axis=0)
    values = jnp.concatenate(value_chunks, axis=0)
    visible = jnp.concatenate(visible_chunks, axis=1)
    count = keys.shape[0]
    if count * rows * q_heads * 4 <= (8 << 20):
        scores = scores_of(keys, visible)
        high = jnp.max(scores, axis=-1)
        total, summed = summed_of(scores, high, values, visible)
    else:
        width = 512
        steps = count // width
        tail = steps * width
        piece_k = keys[:tail].reshape(steps, width, kv_cols)
        piece_v = values[:tail].reshape(steps, width, kv_cols)
        piece_m = jnp.moveaxis(visible[:, :tail].reshape(rows, steps, width), 1, 0)

        def high_step(high, piece):
            k, m = piece
            return jnp.maximum(high, jnp.max(scores_of(k, m), axis=-1)), None

        high = jnp.max(scores_of(keys[tail:], visible[:, tail:]), axis=-1)
        high, _ = lax.scan(high_step, high, (piece_k, piece_m))

        def sum_step(carry, piece):
            k, v, m = piece
            total, summed = summed_of(scores_of(k, m), high, v, m)
            return (carry[0] + total, carry[1] + summed), None

        start = summed_of(scores_of(keys[tail:], visible[:, tail:]), high, values[tail:], visible[:, tail:])
        (total, summed), _ = lax.scan(sum_step, start, (piece_k, piece_v, piece_m))
    attended = (summed / total[..., None]).reshape(rows, q_heads * HD).astype(jnp.bfloat16)
    return (attended, cache[0], cache[1])


def solution(mesh):
    return jax.shard_map(
        body,
        mesh=mesh,
        in_specs=(
            P("seq", "tp"),
            P("seq", "tp"),
            P("seq", "tp"),
            P("seq", "tp"),
            P("seq", "tp"),
            P(),
            P(),
            P(),
        ),
        out_specs=(P("seq", "tp"), P(("seq", "tp"), None), P(("seq", "tp"), None)),
        check_vma=False,
    )
```

```python
import functools
import math

import jax
import jax.numpy as jnp
from jax import lax
from jax.experimental import pallas as pl
from jax.experimental.pallas import tpu as pltpu
from jax.sharding import PartitionSpec as P

HD = 128
GROUPS = 4


BIG_NEGATIVE = -1e30


def rotate(values, position):
    half = values.shape[-1] // 2
    freq = jnp.exp(
        jnp.arange(half, dtype=jnp.float32) * (-2.0 * math.log(500000.0) / values.shape[-1])
    )
    angle = position.astype(jnp.float32)[:, None] * freq[None, :]
    cosine = jnp.cos(angle)[:, None, :]
    sine = jnp.sin(angle)[:, None, :]
    floats = values.astype(jnp.float32)
    lower = floats[..., :half]
    upper = floats[..., half:]
    return jnp.concatenate(
        [lower * cosine - upper * sine, upper * cosine + lower * sine], axis=-1
    ).astype(jnp.bfloat16)


def attend_kernel(meta, *refs):
    devices, block_rows, rows, tails, prefix_len, repeat, scale = meta
    me_ref, lens_ref, rg_ref, bg_ref, q_ref, own_k_ref, own_v_ref = refs[:7]
    data = refs[7 : 7 + devices]
    out_ref, kscr, vscr = refs[7 + devices :]
    kv_cols = kscr.shape[1]
    count = kscr.shape[0]
    base = devices * block_rows
    q_heads = q_ref.shape[1] // HD
    me = me_ref[0]
    reqs = lens_ref.shape[0]
    width = -(-reqs // HD) * HD
    height = -(-reqs // 8) * 8
    never = 1 << 30
    lane = lax.broadcasted_iota(jnp.int32, (1, width), 1)
    sub = lax.broadcasted_iota(jnp.int32, (height, 1), 0)
    start_row = jnp.full((1, width), never, jnp.int32)
    group_row = jnp.zeros((1, width), jnp.int32)
    start_col = jnp.full((height, 1), never, jnp.int32)
    at = 0
    for j in range(reqs):
        start_row = jnp.where(lane == j, at, start_row)
        group_row = jnp.where(lane == j, rg_ref[j], group_row)
        start_col = jnp.where(sub == j, at, start_col)
        at = at + lens_ref[j]

    def info(index):
        after = index >= start_row
        request = jnp.sum(after.astype(jnp.float32), axis=1, keepdims=True).astype(jnp.int32) - 1
        first = jnp.max(jnp.where(after, start_row, 0).astype(jnp.float32), axis=1, keepdims=True)
        group = jnp.sum(
            jnp.where(lane == request, group_row, 0).astype(jnp.float32), axis=1, keepdims=True
        )
        return request, index - first.astype(jnp.int32), group.astype(jnp.int32)

    def request_of_row(index):
        after = index >= start_col
        return jnp.sum(after.astype(jnp.float32), axis=0, keepdims=True).astype(jnp.int32) - 1

    head_lane = lax.broadcasted_iota(jnp.int32, (1, HD), 1)
    pair = jnp.where(head_lane < HD // 2, head_lane, head_lane - HD // 2)
    freq = jnp.exp(pair.astype(jnp.float32) * (-2.0 * math.log(500000.0) / HD))
    sign = jnp.where(head_lane < HD // 2, -1.0, 1.0).astype(jnp.float32)

    def tables(offset):
        angle = (offset + prefix_len).astype(jnp.float32) * freq
        return jnp.cos(angle), jnp.sin(angle) * sign

    def rotated(x, cosine, sine):
        return (x * cosine + pltpu.roll(x, HD // 2, 1) * sine).astype(jnp.bfloat16)

    for c in range(devices):
        kscr[c * block_rows : (c + 1) * block_rows, :] = data[c][0:block_rows, 0:kv_cols]
        vscr[c * block_rows : (c + 1) * block_rows, :] = data[c][0:block_rows, kv_cols : 2 * kv_cols]
    for b in range(0, tails + 1):
        low = base + b * rows
        index = (me - b) * rows + lax.broadcasted_iota(jnp.int32, (rows, 1), 0)
        _, offset, _ = info(index)
        cosine, sine = tables(offset)
        for g in range(kv_cols // HD):
            if b == 0:
                kscr[low : low + rows, g * HD : (g + 1) * HD] = own_k_ref[:, g * HD : (g + 1) * HD]
            else:
                x = data[b][block_rows : block_rows + rows, g * HD : (g + 1) * HD]
                kscr[low : low + rows, g * HD : (g + 1) * HD] = rotated(x.astype(jnp.float32), cosine, sine)
        if b == 0:
            vscr[low : low + rows, :] = own_v_ref[...]
        else:
            vscr[low : low + rows, :] = data[b][block_rows : block_rows + rows, kv_cols : 2 * kv_cols]

    token = me * rows + lax.broadcasted_iota(jnp.int32, (rows, 1), 0)
    request, offset, group = info(token)
    col = lax.broadcasted_iota(jnp.int32, (1, count), 1)
    key_group = jnp.full((1, count), -1, jnp.int32)
    for c in range(devices):
        holder = lax.rem(me - c + devices, devices)
        key_group = jnp.where(col >= c * block_rows, bg_ref[holder], key_group)
    key_index = jnp.full((1, count), -1, jnp.int32)
    for b in range(tails + 1):
        low = base + b * rows
        key_index = jnp.where(col >= low, (me - b) * rows + col - low, key_index)
    key_request = request_of_row(key_index)
    visible = ((col < base) & (key_group == group)) | (
        (key_request == request) & (key_index <= token)
    )
    cosine, sine = tables(offset)
    for g in range(q_heads // repeat):
        heads = range(g * repeat, (g + 1) * repeat)
        q = jnp.concatenate(
            [rotated(q_ref[:, h * HD : (h + 1) * HD].astype(jnp.float32), cosine, sine) for h in heads],
            axis=0,
        )
        k = kscr[:, g * HD : (g + 1) * HD]
        scores = lax.dot_general(
            q, k, (((1,), (1,)), ((), ())), preferred_element_type=jnp.float32
        )
        weights, totals = [], []
        for r in range(repeat):
            part = jnp.where(visible, scores[r * rows : (r + 1) * rows], BIG_NEGATIVE)
            high = jnp.max(part, axis=1, keepdims=True)
            part = jnp.exp2((part - high) * (scale * math.log2(math.e)))
            totals.append(jnp.sum(part, axis=1, keepdims=True))
            weights.append(part.astype(jnp.bfloat16))
        v = vscr[:, g * HD : (g + 1) * HD]
        summed = jnp.dot(jnp.concatenate(weights, axis=0), v, preferred_element_type=jnp.float32)
        for r, h in enumerate(heads):
            out_ref[:, h * HD : (h + 1) * HD] = (summed[r * rows : (r + 1) * rows] / totals[r]).astype(
                out_ref.dtype
            )


def attend(meta, scalars, queries, own_k, own_v, data):
    devices, block_rows, rows, tails = meta[:4]
    kv_cols = own_k.shape[1]
    q_heads = queries.shape[1] // HD
    count = devices * block_rows + rows * (1 + tails)
    flops = 4 * rows * count * HD * q_heads
    arrays = [queries, own_k, own_v, *data]
    nbytes = sum(a.size * a.dtype.itemsize for a in arrays)
    smem = pl.BlockSpec(memory_space=pltpu.SMEM)
    vmem = pl.BlockSpec(memory_space=pltpu.VMEM)
    return pl.pallas_call(
        functools.partial(attend_kernel, meta),
        out_shape=jax.ShapeDtypeStruct(queries.shape, jnp.bfloat16),
        in_specs=[smem] * len(scalars) + [vmem] * len(arrays),
        out_specs=vmem,
        scratch_shapes=[
            pltpu.VMEM((count, kv_cols), jnp.bfloat16),
            pltpu.VMEM((count, kv_cols), jnp.bfloat16),
        ],
        cost_estimate=pl.CostEstimate(
            flops=flops,
            transcendentals=rows * count * q_heads,
            bytes_accessed=nbytes + queries.size * 2,
        ),
    )(*scalars, *arrays)


def token_info(index, suffix_lengths, request_group):
    ends = jnp.cumsum(suffix_lengths)
    request = jnp.sum((index[:, None] >= ends[None, :]).astype(jnp.int32), axis=1)
    onehot = request[:, None] == jnp.arange(suffix_lengths.shape[0], dtype=jnp.int32)[None, :]
    first = jnp.sum(jnp.where(onehot, (ends - suffix_lengths)[None, :], 0), axis=1)
    group = jnp.sum(jnp.where(onehot, request_group[None, :], 0), axis=1)
    return (request, index - first, group)


def shifted(array, axis, by, wrap):
    length = lax.axis_size(axis)
    pairs = [(i, (i + by) % length) for i in range(length) if wrap or i + by < length]
    return lax.ppermute(array, axis, pairs)


def body(
    queries,
    suffix_keys,
    suffix_values,
    prefix_keys,
    prefix_values,
    suffix_lengths,
    request_group,
    block_group,
):
    rows = queries.shape[0]
    kv_cols = suffix_keys.shape[1]
    kv_heads = kv_cols // HD
    q_heads = queries.shape[1] // HD
    repeat = q_heads // kv_heads
    devices = lax.axis_size("seq")
    me = lax.axis_index("seq")
    block_rows = prefix_keys.shape[0]
    prefix_len = block_rows * devices // GROUPS
    span = max(1, min(2048 // rows, devices // 8))
    scale = HD ** (-0.5)
    index = me * rows + jnp.arange(rows, dtype=jnp.int32)
    request, offset, group = token_info(index, suffix_lengths, request_group)

    prefix_kv = jnp.concatenate([prefix_keys, prefix_values], axis=1)
    suffix_kv = jnp.concatenate([suffix_keys, suffix_values], axis=1)

    def rotated_keys(raw, back):
        key_index = (me - back) * rows + jnp.arange(rows, dtype=jnp.int32)
        key_request, key_offset, _ = token_info(key_index, suffix_lengths, request_group)
        k_rot = rotate(raw.reshape(rows, kv_heads, HD), key_offset + prefix_len).reshape(rows, kv_cols)
        return key_index, key_request, k_rot

    if devices <= 16:
        received = {}
        late = list(range(span + 1, devices))[: max(0, devices - 1 - 5)]
        for by in range(1, devices):
            if by <= span:
                received[by] = shifted(jnp.concatenate([prefix_kv, suffix_kv], axis=0), "seq", by, True)
            elif by not in late:
                received[by] = shifted(prefix_kv, "seq", by, True)
        cache_keys_in, cache_values_in = suffix_keys, suffix_values
        if late:
            first_gate, cache_keys_in, cache_values_in = lax.optimization_barrier(
                (received[devices - 1], suffix_keys, suffix_values)
            )
            received[devices - 1] = first_gate
            gates = (received[1],) + tuple(received[devices - 1 - i] for i in range(len(late)))
            gates, payload = lax.optimization_barrier((gates, prefix_kv))
            received[1] = gates[0]
            for i, by in enumerate(late):
                received[devices - 1 - i] = gates[i + 1]
                received[by] = shifted(payload, "seq", by, True)
        data = [prefix_kv] + [received[by] for by in range(1, devices)]
        _, own_offset, _ = token_info(index, suffix_lengths, request_group)
        own_k_rot = rotate(cache_keys_in.reshape(rows, kv_heads, HD), own_offset + prefix_len).reshape(
            rows, kv_cols
        )
        cache = lax.all_to_all(
            jnp.stack([own_k_rot, cache_values_in], axis=0), "tp", split_axis=1, concat_axis=2, tiled=True
        )
        scalars = [me.astype(jnp.int32).reshape(1), suffix_lengths, request_group, block_group]
        meta = (devices, block_rows, rows, min(span, devices - 1), prefix_len, repeat, scale)
        attended = attend(meta, scalars, queries, own_k_rot, suffix_values, data)
        return (attended, cache[0], cache[1])

    prefix_parts = []
    suffix_parts = [(0, suffix_kv)]
    gathered = lax.all_gather(prefix_kv, "seq", axis=0, tiled=True)
    prefix_parts.append((None, gathered))
    for by in range(1, span + 1):
        suffix_parts.append((by, shifted(suffix_kv, "seq", by, False)))

    position = offset + prefix_len
    q_rot = rotate(queries.reshape(rows, q_heads, HD), position).reshape(rows, kv_heads, repeat, HD)

    key_chunks, value_chunks, visible_chunks = [], [], []
    for holder, kv in prefix_parts:
        count = kv.shape[0]
        if holder is None:
            holder_index = jnp.arange(count, dtype=jnp.int32) // block_rows
            row_group = jnp.take(block_group, holder_index)
            visible = row_group[None, :] == group[:, None]
        else:
            row_group = lax.dynamic_index_in_dim(block_group, holder, keepdims=False)
            visible = jnp.broadcast_to((group == row_group)[:, None], (rows, count))
        key_chunks.append(kv[:, :kv_cols])
        value_chunks.append(kv[:, kv_cols:])
        visible_chunks.append(visible)

    own_k_rot = None
    for back, kv in suffix_parts:
        key_index = (me - back) * rows + jnp.arange(rows, dtype=jnp.int32)
        key_request, key_offset, _ = token_info(key_index, suffix_lengths, request_group)
        k_rot = rotate(kv[:, :kv_cols].reshape(rows, kv_heads, HD), key_offset + prefix_len).reshape(
            rows, kv_cols
        )
        if back == 0:
            own_k_rot = k_rot
        visible = (
            (key_index[None, :] >= 0)
            & (key_request[None, :] == request[:, None])
            & (key_index[None, :] <= index[:, None])
        )
        key_chunks.append(k_rot)
        value_chunks.append(kv[:, kv_cols:])
        visible_chunks.append(visible)

    cache = lax.all_to_all(
        jnp.stack([own_k_rot, suffix_values], axis=0), "tp", split_axis=1, concat_axis=2, tiled=True
    )

    def scores_of(keys, visible):
        keys_split = keys.reshape(keys.shape[0], kv_heads, HD)
        scores = (
            jnp.einsum("bgrd,kgd->bgrk", q_rot, keys_split, preferred_element_type=jnp.float32)
            * scale
        )
        return jnp.where(visible[:, None, None, :], scores, BIG_NEGATIVE)

    def summed_of(scores, high, values, visible):
        weights = jnp.where(visible[:, None, None, :], jnp.exp(scores - high[..., None]), 0.0)
        summed = jnp.einsum(
            "bgrk,kgd->bgrd",
            weights.astype(jnp.bfloat16),
            values.reshape(values.shape[0], kv_heads, HD),
            preferred_element_type=jnp.float32,
        )
        return jnp.sum(weights, axis=-1), summed

    keys = jnp.concatenate(key_chunks, axis=0)
    values = jnp.concatenate(value_chunks, axis=0)
    visible = jnp.concatenate(visible_chunks, axis=1)
    count = keys.shape[0]
    if count * rows * q_heads * 4 <= (8 << 20):
        scores = scores_of(keys, visible)
        high = jnp.max(scores, axis=-1)
        total, summed = summed_of(scores, high, values, visible)
    else:
        width = 512
        steps = count // width
        tail = steps * width
        piece_k = keys[:tail].reshape(steps, width, kv_cols)
        piece_v = values[:tail].reshape(steps, width, kv_cols)
        piece_m = jnp.moveaxis(visible[:, :tail].reshape(rows, steps, width), 1, 0)

        def high_step(high, piece):
            k, m = piece
            return jnp.maximum(high, jnp.max(scores_of(k, m), axis=-1)), None

        high = jnp.max(scores_of(keys[tail:], visible[:, tail:]), axis=-1)
        high, _ = lax.scan(high_step, high, (piece_k, piece_m))

        def sum_step(carry, piece):
            k, v, m = piece
            total, summed = summed_of(scores_of(k, m), high, v, m)
            return (carry[0] + total, carry[1] + summed), None

        start = summed_of(scores_of(keys[tail:], visible[:, tail:]), high, values[tail:], visible[:, tail:])
        (total, summed), _ = lax.scan(sum_step, start, (piece_k, piece_v, piece_m))
    attended = (summed / total[..., None]).reshape(rows, q_heads * HD).astype(jnp.bfloat16)
    return (attended, cache[0], cache[1])


def solution(mesh):
    return jax.shard_map(
        body,
        mesh=mesh,
        in_specs=(
            P("seq", "tp"),
            P("seq", "tp"),
            P("seq", "tp"),
            P("seq", "tp"),
            P("seq", "tp"),
            P(),
            P(),
            P(),
        ),
        out_specs=(P("seq", "tp"), P(("seq", "tp"), None), P(("seq", "tp"), None)),
        check_vma=False,
    )
```

```python
import functools
import math

import jax
import jax.numpy as jnp
from jax import lax
from jax.experimental import pallas as pl
from jax.experimental.pallas import tpu as pltpu
from jax.sharding import PartitionSpec as P

HD = 128
GROUPS = 4


BIG_NEGATIVE = -1e30


def rotate(values, position):
    half = values.shape[-1] // 2
    freq = jnp.exp(
        jnp.arange(half, dtype=jnp.float32) * (-2.0 * math.log(500000.0) / values.shape[-1])
    )
    angle = position.astype(jnp.float32)[:, None] * freq[None, :]
    cosine = jnp.cos(angle)[:, None, :]
    sine = jnp.sin(angle)[:, None, :]
    floats = values.astype(jnp.float32)
    lower = floats[..., :half]
    upper = floats[..., half:]
    return jnp.concatenate(
        [lower * cosine - upper * sine, upper * cosine + lower * sine], axis=-1
    ).astype(jnp.bfloat16)


def attend_kernel(meta, *refs):
    devices, block_rows, rows, tails, prefix_len, repeat, scale = meta
    me_ref, lens_ref, rg_ref, bg_ref, freq_ref, q_ref, own_k_ref, own_v_ref = refs[:8]
    data = refs[8 : 8 + devices]
    out_ref, kscr, vscr = refs[8 + devices :]
    kv_cols = kscr.shape[1]
    count = kscr.shape[0]
    base = devices * block_rows
    q_heads = q_ref.shape[1] // HD
    me = me_ref[0]
    reqs = lens_ref.shape[0]
    width = -(-reqs // HD) * HD
    height = -(-reqs // 8) * 8
    never = 1 << 30
    lane = lax.broadcasted_iota(jnp.int32, (1, width), 1)
    sub = lax.broadcasted_iota(jnp.int32, (height, 1), 0)
    start_row = jnp.full((1, width), never, jnp.int32)
    group_row = jnp.zeros((1, width), jnp.int32)
    start_col = jnp.full((height, 1), never, jnp.int32)
    at = 0
    for j in range(reqs):
        start_row = jnp.where(lane == j, at, start_row)
        group_row = jnp.where(lane == j, rg_ref[j], group_row)
        start_col = jnp.where(sub == j, at, start_col)
        at = at + lens_ref[j]

    def info(index):
        after = index >= start_row
        request = jnp.sum(after.astype(jnp.float32), axis=1, keepdims=True).astype(jnp.int32) - 1
        first = jnp.max(jnp.where(after, start_row, 0).astype(jnp.float32), axis=1, keepdims=True)
        group = jnp.sum(
            jnp.where(lane == request, group_row, 0).astype(jnp.float32), axis=1, keepdims=True
        )
        return request, index - first.astype(jnp.int32), group.astype(jnp.int32)

    def request_of_row(index):
        after = index >= start_col
        return jnp.sum(after.astype(jnp.float32), axis=0, keepdims=True).astype(jnp.int32) - 1

    head_lane = lax.broadcasted_iota(jnp.int32, (1, HD), 1)
    freq = freq_ref[...]
    sign = jnp.where(head_lane < HD // 2, -1.0, 1.0).astype(jnp.float32)

    def tables(offset):
        angle = (offset + prefix_len).astype(jnp.float32) * freq
        return jnp.cos(angle), jnp.sin(angle) * sign

    def rotated(x, cosine, sine):
        return (x * cosine + pltpu.roll(x, HD // 2, 1) * sine).astype(jnp.bfloat16)

    for c in range(devices):
        kscr[c * block_rows : (c + 1) * block_rows, :] = data[c][0:block_rows, 0:kv_cols]
        vscr[c * block_rows : (c + 1) * block_rows, :] = data[c][0:block_rows, kv_cols : 2 * kv_cols]
    for b in range(0, tails + 1):
        low = base + b * rows
        index = (me - b) * rows + lax.broadcasted_iota(jnp.int32, (rows, 1), 0)
        _, offset, _ = info(index)
        cosine, sine = tables(offset)
        for g in range(kv_cols // HD):
            if b == 0:
                kscr[low : low + rows, g * HD : (g + 1) * HD] = own_k_ref[:, g * HD : (g + 1) * HD]
            else:
                x = data[b][block_rows : block_rows + rows, g * HD : (g + 1) * HD]
                kscr[low : low + rows, g * HD : (g + 1) * HD] = rotated(x.astype(jnp.float32), cosine, sine)
        if b == 0:
            vscr[low : low + rows, :] = own_v_ref[...]
        else:
            vscr[low : low + rows, :] = data[b][block_rows : block_rows + rows, kv_cols : 2 * kv_cols]

    token = me * rows + lax.broadcasted_iota(jnp.int32, (rows, 1), 0)
    request, offset, group = info(token)
    col = lax.broadcasted_iota(jnp.int32, (1, count), 1)
    key_group = jnp.full((1, count), -1, jnp.int32)
    for c in range(devices):
        holder = lax.rem(me - c + devices, devices)
        key_group = jnp.where(col >= c * block_rows, bg_ref[holder], key_group)
    key_index = jnp.full((1, count), -1, jnp.int32)
    for b in range(tails + 1):
        low = base + b * rows
        key_index = jnp.where(col >= low, (me - b) * rows + col - low, key_index)
    key_request = request_of_row(key_index)
    visible = ((col < base) & (key_group == group)) | (
        (key_request == request) & (key_index <= token)
    )
    cosine, sine = tables(offset)
    for g in range(q_heads // repeat):
        heads = range(g * repeat, (g + 1) * repeat)
        q = jnp.concatenate(
            [rotated(q_ref[:, h * HD : (h + 1) * HD].astype(jnp.float32), cosine, sine) for h in heads],
            axis=0,
        )
        k = kscr[:, g * HD : (g + 1) * HD]
        scores = lax.dot_general(
            q, k, (((1,), (1,)), ((), ())), preferred_element_type=jnp.float32
        )
        weights, totals = [], []
        for r in range(repeat):
            part = jnp.where(visible, scores[r * rows : (r + 1) * rows], BIG_NEGATIVE)
            high = jnp.max(part, axis=1, keepdims=True)
            part = jnp.exp2((part - high) * (scale * math.log2(math.e)))
            totals.append(jnp.sum(part, axis=1, keepdims=True))
            weights.append(part.astype(jnp.bfloat16))
        v = vscr[:, g * HD : (g + 1) * HD]
        summed = jnp.dot(jnp.concatenate(weights, axis=0), v, preferred_element_type=jnp.float32)
        for r, h in enumerate(heads):
            out_ref[:, h * HD : (h + 1) * HD] = (summed[r * rows : (r + 1) * rows] / totals[r]).astype(
                out_ref.dtype
            )


def attend(meta, scalars, freq, queries, own_k, own_v, data):
    devices, block_rows, rows, tails = meta[:4]
    kv_cols = own_k.shape[1]
    q_heads = queries.shape[1] // HD
    count = devices * block_rows + rows * (1 + tails)
    flops = 4 * rows * count * HD * q_heads
    arrays = [queries, own_k, own_v, *data]
    nbytes = sum(a.size * a.dtype.itemsize for a in arrays)
    smem = pl.BlockSpec(memory_space=pltpu.SMEM)
    vmem = pl.BlockSpec(memory_space=pltpu.VMEM)
    return pl.pallas_call(
        functools.partial(attend_kernel, meta),
        out_shape=jax.ShapeDtypeStruct(queries.shape, jnp.bfloat16),
        in_specs=[smem] * len(scalars) + [vmem] * (1 + len(arrays)),
        out_specs=vmem,
        scratch_shapes=[
            pltpu.VMEM((count, kv_cols), jnp.bfloat16),
            pltpu.VMEM((count, kv_cols), jnp.bfloat16),
        ],
        cost_estimate=pl.CostEstimate(
            flops=flops,
            transcendentals=rows * count * q_heads,
            bytes_accessed=nbytes + queries.size * 2,
        ),
    )(*scalars, freq, *arrays)


def token_info(index, suffix_lengths, request_group):
    ends = jnp.cumsum(suffix_lengths)
    request = jnp.sum((index[:, None] >= ends[None, :]).astype(jnp.int32), axis=1)
    onehot = request[:, None] == jnp.arange(suffix_lengths.shape[0], dtype=jnp.int32)[None, :]
    first = jnp.sum(jnp.where(onehot, (ends - suffix_lengths)[None, :], 0), axis=1)
    group = jnp.sum(jnp.where(onehot, request_group[None, :], 0), axis=1)
    return (request, index - first, group)


def shifted(array, axis, by, wrap):
    length = lax.axis_size(axis)
    pairs = [(i, (i + by) % length) for i in range(length) if wrap or i + by < length]
    return lax.ppermute(array, axis, pairs)


def body(
    queries,
    suffix_keys,
    suffix_values,
    prefix_keys,
    prefix_values,
    suffix_lengths,
    request_group,
    block_group,
):
    rows = queries.shape[0]
    kv_cols = suffix_keys.shape[1]
    kv_heads = kv_cols // HD
    q_heads = queries.shape[1] // HD
    repeat = q_heads // kv_heads
    devices = lax.axis_size("seq")
    me = lax.axis_index("seq")
    block_rows = prefix_keys.shape[0]
    prefix_len = block_rows * devices // GROUPS
    span = max(1, min(2048 // rows, devices // 8))
    scale = HD ** (-0.5)
    index = me * rows + jnp.arange(rows, dtype=jnp.int32)
    request, offset, group = token_info(index, suffix_lengths, request_group)

    prefix_kv = jnp.concatenate([prefix_keys, prefix_values], axis=1)
    suffix_kv = jnp.concatenate([suffix_keys, suffix_values], axis=1)

    def rotated_keys(raw, back):
        key_index = (me - back) * rows + jnp.arange(rows, dtype=jnp.int32)
        key_request, key_offset, _ = token_info(key_index, suffix_lengths, request_group)
        k_rot = rotate(raw.reshape(rows, kv_heads, HD), key_offset + prefix_len).reshape(rows, kv_cols)
        return key_index, key_request, k_rot

    if devices <= 16:
        received = {}
        late = list(range(span + 1, devices))[: max(0, devices - 1 - 5)]
        for by in range(1, devices):
            if by <= span:
                received[by] = shifted(jnp.concatenate([prefix_kv, suffix_kv], axis=0), "seq", by, True)
            elif by not in late:
                received[by] = shifted(prefix_kv, "seq", by, True)
        gates = tuple(received[devices - 1 - i] for i in range(len(late)))
        gates, payload, cache_keys_in, cache_values_in = lax.optimization_barrier(
            (gates, prefix_kv, suffix_keys, suffix_values)
        )
        for i, by in enumerate(late):
            received[devices - 1 - i] = gates[i]
            received[by] = shifted(payload, "seq", by, True)
        data = [prefix_kv] + [received[by] for by in range(1, devices)]
        if not late:
            cache_keys_in, cache_values_in = suffix_keys, suffix_values
        _, own_offset, _ = token_info(index, suffix_lengths, request_group)
        own_k_rot = rotate(cache_keys_in.reshape(rows, kv_heads, HD), own_offset + prefix_len).reshape(
            rows, kv_cols
        )
        cache = lax.all_to_all(
            jnp.stack([own_k_rot, cache_values_in], axis=0), "tp", split_axis=1, concat_axis=2, tiled=True
        )
        half = HD // 2
        freq = jnp.exp(jnp.arange(half, dtype=jnp.float32) * (-2.0 * math.log(500000.0) / HD))
        freq = jnp.concatenate([freq, freq])[None, :]
        scalars = [me.astype(jnp.int32).reshape(1), suffix_lengths, request_group, block_group]
        meta = (devices, block_rows, rows, min(span, devices - 1), prefix_len, repeat, scale)
        attended = attend(meta, scalars, freq, queries, own_k_rot, suffix_values, data)
        return (attended, cache[0], cache[1])

    prefix_parts = []
    suffix_parts = [(0, suffix_kv)]
    gathered = lax.all_gather(prefix_kv, "seq", axis=0, tiled=True)
    prefix_parts.append((None, gathered))
    for by in range(1, span + 1):
        suffix_parts.append((by, shifted(suffix_kv, "seq", by, False)))

    position = offset + prefix_len
    q_rot = rotate(queries.reshape(rows, q_heads, HD), position).reshape(rows, kv_heads, repeat, HD)

    key_chunks, value_chunks, visible_chunks = [], [], []
    for holder, kv in prefix_parts:
        count = kv.shape[0]
        if holder is None:
            holder_index = jnp.arange(count, dtype=jnp.int32) // block_rows
            row_group = jnp.take(block_group, holder_index)
            visible = row_group[None, :] == group[:, None]
        else:
            row_group = lax.dynamic_index_in_dim(block_group, holder, keepdims=False)
            visible = jnp.broadcast_to((group == row_group)[:, None], (rows, count))
        key_chunks.append(kv[:, :kv_cols])
        value_chunks.append(kv[:, kv_cols:])
        visible_chunks.append(visible)

    own_k_rot = None
    for back, kv in suffix_parts:
        key_index = (me - back) * rows + jnp.arange(rows, dtype=jnp.int32)
        key_request, key_offset, _ = token_info(key_index, suffix_lengths, request_group)
        k_rot = rotate(kv[:, :kv_cols].reshape(rows, kv_heads, HD), key_offset + prefix_len).reshape(
            rows, kv_cols
        )
        if back == 0:
            own_k_rot = k_rot
        visible = (
            (key_index[None, :] >= 0)
            & (key_request[None, :] == request[:, None])
            & (key_index[None, :] <= index[:, None])
        )
        key_chunks.append(k_rot)
        value_chunks.append(kv[:, kv_cols:])
        visible_chunks.append(visible)

    cache = lax.all_to_all(
        jnp.stack([own_k_rot, suffix_values], axis=0), "tp", split_axis=1, concat_axis=2, tiled=True
    )

    def scores_of(keys, visible):
        keys_split = keys.reshape(keys.shape[0], kv_heads, HD)
        scores = (
            jnp.einsum("bgrd,kgd->bgrk", q_rot, keys_split, preferred_element_type=jnp.float32)
            * scale
        )
        return jnp.where(visible[:, None, None, :], scores, BIG_NEGATIVE)

    def summed_of(scores, high, values, visible):
        weights = jnp.where(visible[:, None, None, :], jnp.exp(scores - high[..., None]), 0.0)
        summed = jnp.einsum(
            "bgrk,kgd->bgrd",
            weights.astype(jnp.bfloat16),
            values.reshape(values.shape[0], kv_heads, HD),
            preferred_element_type=jnp.float32,
        )
        return jnp.sum(weights, axis=-1), summed

    keys = jnp.concatenate(key_chunks, axis=0)
    values = jnp.concatenate(value_chunks, axis=0)
    visible = jnp.concatenate(visible_chunks, axis=1)
    count = keys.shape[0]
    if count * rows * q_heads * 4 <= (8 << 20):
        scores = scores_of(keys, visible)
        high = jnp.max(scores, axis=-1)
        total, summed = summed_of(scores, high, values, visible)
    else:
        width = 512
        steps = count // width
        tail = steps * width
        piece_k = keys[:tail].reshape(steps, width, kv_cols)
        piece_v = values[:tail].reshape(steps, width, kv_cols)
        piece_m = jnp.moveaxis(visible[:, :tail].reshape(rows, steps, width), 1, 0)

        def high_step(high, piece):
            k, m = piece
            return jnp.maximum(high, jnp.max(scores_of(k, m), axis=-1)), None

        high = jnp.max(scores_of(keys[tail:], visible[:, tail:]), axis=-1)
        high, _ = lax.scan(high_step, high, (piece_k, piece_m))

        def sum_step(carry, piece):
            k, v, m = piece
            total, summed = summed_of(scores_of(k, m), high, v, m)
            return (carry[0] + total, carry[1] + summed), None

        start = summed_of(scores_of(keys[tail:], visible[:, tail:]), high, values[tail:], visible[:, tail:])
        (total, summed), _ = lax.scan(sum_step, start, (piece_k, piece_v, piece_m))
    attended = (summed / total[..., None]).reshape(rows, q_heads * HD).astype(jnp.bfloat16)
    return (attended, cache[0], cache[1])


def solution(mesh):
    return jax.shard_map(
        body,
        mesh=mesh,
        in_specs=(
            P("seq", "tp"),
            P("seq", "tp"),
            P("seq", "tp"),
            P("seq", "tp"),
            P("seq", "tp"),
            P(),
            P(),
            P(),
        ),
        out_specs=(P("seq", "tp"), P(("seq", "tp"), None), P(("seq", "tp"), None)),
        check_vma=False,
    )
```

```python
import functools
import math

import jax
import jax.numpy as jnp
from jax import lax
from jax.experimental import pallas as pl
from jax.experimental.pallas import tpu as pltpu
from jax.sharding import PartitionSpec as P

HD = 128
GROUPS = 4


BIG_NEGATIVE = -1e30


def rotate(values, position):
    half = values.shape[-1] // 2
    freq = jnp.exp(
        jnp.arange(half, dtype=jnp.float32) * (-2.0 * math.log(500000.0) / values.shape[-1])
    )
    angle = position.astype(jnp.float32)[:, None] * freq[None, :]
    cosine = jnp.cos(angle)[:, None, :]
    sine = jnp.sin(angle)[:, None, :]
    floats = values.astype(jnp.float32)
    lower = floats[..., :half]
    upper = floats[..., half:]
    return jnp.concatenate(
        [lower * cosine - upper * sine, upper * cosine + lower * sine], axis=-1
    ).astype(jnp.bfloat16)


def attend_kernel(meta, *refs):
    devices, block_rows, rows, tails, prefix_len, repeat, scale = meta
    me_ref, lens_ref, rg_ref, bg_ref, freq_ref, q_ref, own_k_ref, own_v_ref = refs[:8]
    data = refs[8 : 8 + devices]
    out_ref, kscr, vscr, raw, sems = refs[8 + devices :]
    kv_cols = kscr.shape[1]
    count = kscr.shape[0]
    base = devices * block_rows
    q_heads = q_ref.shape[1] // HD
    me = me_ref[0]
    reqs = lens_ref.shape[0]
    width = -(-reqs // HD) * HD
    height = -(-reqs // 8) * 8
    never = 1 << 30
    lane = lax.broadcasted_iota(jnp.int32, (1, width), 1)
    sub = lax.broadcasted_iota(jnp.int32, (height, 1), 0)
    start_row = jnp.full((1, width), never, jnp.int32)
    group_row = jnp.zeros((1, width), jnp.int32)
    start_col = jnp.full((height, 1), never, jnp.int32)
    at = 0
    for j in range(reqs):
        start_row = jnp.where(lane == j, at, start_row)
        group_row = jnp.where(lane == j, rg_ref[j], group_row)
        start_col = jnp.where(sub == j, at, start_col)
        at = at + lens_ref[j]

    def info(index):
        after = index >= start_row
        request = jnp.sum(after.astype(jnp.float32), axis=1, keepdims=True).astype(jnp.int32) - 1
        first = jnp.max(jnp.where(after, start_row, 0).astype(jnp.float32), axis=1, keepdims=True)
        group = jnp.sum(
            jnp.where(lane == request, group_row, 0).astype(jnp.float32), axis=1, keepdims=True
        )
        return request, index - first.astype(jnp.int32), group.astype(jnp.int32)

    def request_of_row(index):
        after = index >= start_col
        return jnp.sum(after.astype(jnp.float32), axis=0, keepdims=True).astype(jnp.int32) - 1

    head_lane = lax.broadcasted_iota(jnp.int32, (1, HD), 1)
    freq = freq_ref[...]
    sign = jnp.where(head_lane < HD // 2, -1.0, 1.0).astype(jnp.float32)

    def tables(offset):
        angle = (offset + prefix_len).astype(jnp.float32) * freq
        return jnp.cos(angle), jnp.sin(angle) * sign

    def rotated(x, cosine, sine):
        return (x * cosine + pltpu.roll(x, HD // 2, 1) * sine).astype(jnp.bfloat16)

    copies = []
    for c in range(devices):
        rows_c = pl.ds(c * block_rows, block_rows)
        copies.append(pltpu.make_async_copy(
            data[c].at[pl.ds(0, block_rows), pl.ds(0, kv_cols)], kscr.at[rows_c, :], sems.at[len(copies)]
        ))
        copies.append(pltpu.make_async_copy(
            data[c].at[pl.ds(0, block_rows), pl.ds(kv_cols, kv_cols)], vscr.at[rows_c, :], sems.at[len(copies)]
        ))
    for b in range(1, tails + 1):
        low = base + b * rows
        copies.append(pltpu.make_async_copy(
            data[b].at[pl.ds(block_rows, rows), pl.ds(0, kv_cols)], raw.at[b - 1], sems.at[len(copies)]
        ))
        copies.append(pltpu.make_async_copy(
            data[b].at[pl.ds(block_rows, rows), pl.ds(kv_cols, kv_cols)], vscr.at[pl.ds(low, rows), :],
            sems.at[len(copies)],
        ))
    for copy in copies:
        copy.start()
    for copy in copies:
        copy.wait()
    for b in range(0, tails + 1):
        low = base + b * rows
        index = (me - b) * rows + lax.broadcasted_iota(jnp.int32, (rows, 1), 0)
        _, offset, _ = info(index)
        cosine, sine = tables(offset)
        for g in range(kv_cols // HD):
            if b == 0:
                kscr[low : low + rows, g * HD : (g + 1) * HD] = own_k_ref[:, g * HD : (g + 1) * HD]
            else:
                x = raw[b - 1, :, g * HD : (g + 1) * HD]
                kscr[low : low + rows, g * HD : (g + 1) * HD] = rotated(x.astype(jnp.float32), cosine, sine)
        if b == 0:
            vscr[low : low + rows, :] = own_v_ref[...]

    token = me * rows + lax.broadcasted_iota(jnp.int32, (rows, 1), 0)
    request, offset, group = info(token)
    col = lax.broadcasted_iota(jnp.int32, (1, count), 1)
    key_group = jnp.full((1, count), -1, jnp.int32)
    for c in range(devices):
        holder = lax.rem(me - c + devices, devices)
        key_group = jnp.where(col >= c * block_rows, bg_ref[holder], key_group)
    key_index = jnp.full((1, count), -1, jnp.int32)
    for b in range(tails + 1):
        low = base + b * rows
        key_index = jnp.where(col >= low, (me - b) * rows + col - low, key_index)
    key_request = request_of_row(key_index)
    visible = ((col < base) & (key_group == group)) | (
        (key_request == request) & (key_index <= token)
    )
    cosine, sine = tables(offset)
    for g in range(q_heads // repeat):
        heads = range(g * repeat, (g + 1) * repeat)
        q = jnp.concatenate(
            [rotated(q_ref[:, h * HD : (h + 1) * HD].astype(jnp.float32), cosine, sine) for h in heads],
            axis=0,
        )
        k = kscr[:, g * HD : (g + 1) * HD]
        scores = lax.dot_general(
            q, k, (((1,), (1,)), ((), ())), preferred_element_type=jnp.float32
        )
        weights, totals = [], []
        for r in range(repeat):
            part = jnp.where(visible, scores[r * rows : (r + 1) * rows], BIG_NEGATIVE)
            high = jnp.max(part, axis=1, keepdims=True)
            part = jnp.exp2((part - high) * (scale * math.log2(math.e)))
            totals.append(jnp.sum(part, axis=1, keepdims=True))
            weights.append(part.astype(jnp.bfloat16))
        v = vscr[:, g * HD : (g + 1) * HD]
        summed = jnp.dot(jnp.concatenate(weights, axis=0), v, preferred_element_type=jnp.float32)
        for r, h in enumerate(heads):
            out_ref[:, h * HD : (h + 1) * HD] = (summed[r * rows : (r + 1) * rows] / totals[r]).astype(
                out_ref.dtype
            )


def attend(meta, scalars, freq, queries, own_k, own_v, data):
    devices, block_rows, rows, tails = meta[:4]
    kv_cols = own_k.shape[1]
    q_heads = queries.shape[1] // HD
    count = devices * block_rows + rows * (1 + tails)
    flops = 4 * rows * count * HD * q_heads
    arrays = [queries, own_k, own_v, *data]
    nbytes = sum(a.size * a.dtype.itemsize for a in arrays)
    smem = pl.BlockSpec(memory_space=pltpu.SMEM)
    vmem = pl.BlockSpec(memory_space=pltpu.VMEM)
    return pl.pallas_call(
        functools.partial(attend_kernel, meta),
        out_shape=jax.ShapeDtypeStruct(queries.shape, jnp.bfloat16),
        in_specs=[smem] * len(scalars) + [vmem] * 4 + [pl.BlockSpec(memory_space=pl.ANY)] * len(data),
        out_specs=vmem,
        scratch_shapes=[
            pltpu.VMEM((count, kv_cols), jnp.bfloat16),
            pltpu.VMEM((count, kv_cols), jnp.bfloat16),
            pltpu.VMEM((max(tails, 1), rows, kv_cols), jnp.bfloat16),
            pltpu.SemaphoreType.DMA((2 * devices + 2 * tails,)),
        ],
        cost_estimate=pl.CostEstimate(
            flops=flops,
            transcendentals=rows * count * q_heads,
            bytes_accessed=nbytes + queries.size * 2,
        ),
    )(*scalars, freq, *arrays)


def token_info(index, suffix_lengths, request_group):
    ends = jnp.cumsum(suffix_lengths)
    request = jnp.sum((index[:, None] >= ends[None, :]).astype(jnp.int32), axis=1)
    onehot = request[:, None] == jnp.arange(suffix_lengths.shape[0], dtype=jnp.int32)[None, :]
    first = jnp.sum(jnp.where(onehot, (ends - suffix_lengths)[None, :], 0), axis=1)
    group = jnp.sum(jnp.where(onehot, request_group[None, :], 0), axis=1)
    return (request, index - first, group)


def shifted(array, axis, by, wrap):
    length = lax.axis_size(axis)
    pairs = [(i, (i + by) % length) for i in range(length) if wrap or i + by < length]
    return lax.ppermute(array, axis, pairs)


def body(
    queries,
    suffix_keys,
    suffix_values,
    prefix_keys,
    prefix_values,
    suffix_lengths,
    request_group,
    block_group,
):
    rows = queries.shape[0]
    kv_cols = suffix_keys.shape[1]
    kv_heads = kv_cols // HD
    q_heads = queries.shape[1] // HD
    repeat = q_heads // kv_heads
    devices = lax.axis_size("seq")
    me = lax.axis_index("seq")
    block_rows = prefix_keys.shape[0]
    prefix_len = block_rows * devices // GROUPS
    span = max(1, min(2048 // rows, devices // 8))
    scale = HD ** (-0.5)
    index = me * rows + jnp.arange(rows, dtype=jnp.int32)
    request, offset, group = token_info(index, suffix_lengths, request_group)

    prefix_kv = jnp.concatenate([prefix_keys, prefix_values], axis=1)
    suffix_kv = jnp.concatenate([suffix_keys, suffix_values], axis=1)

    def rotated_keys(raw, back):
        key_index = (me - back) * rows + jnp.arange(rows, dtype=jnp.int32)
        key_request, key_offset, _ = token_info(key_index, suffix_lengths, request_group)
        k_rot = rotate(raw.reshape(rows, kv_heads, HD), key_offset + prefix_len).reshape(rows, kv_cols)
        return key_index, key_request, k_rot

    if devices <= 16:
        received = {}
        late = list(range(span + 1, devices))[: max(0, devices - 1 - 5)]
        for by in range(1, devices):
            if by <= span:
                received[by] = shifted(jnp.concatenate([prefix_kv, suffix_kv], axis=0), "seq", by, True)
            elif by not in late:
                received[by] = shifted(prefix_kv, "seq", by, True)
        gates = tuple(received[devices - 1 - i] for i in range(len(late)))
        gates, payload, cache_keys_in, cache_values_in = lax.optimization_barrier(
            (gates, prefix_kv, suffix_keys, suffix_values)
        )
        for i, by in enumerate(late):
            received[devices - 1 - i] = gates[i]
            received[by] = shifted(payload, "seq", by, True)
        data = [prefix_kv] + [received[by] for by in range(1, devices)]
        if not late:
            cache_keys_in, cache_values_in = suffix_keys, suffix_values
        _, own_offset, _ = token_info(index, suffix_lengths, request_group)
        own_k_rot = rotate(cache_keys_in.reshape(rows, kv_heads, HD), own_offset + prefix_len).reshape(
            rows, kv_cols
        )
        cache = lax.all_to_all(
            jnp.stack([own_k_rot, cache_values_in], axis=0), "tp", split_axis=1, concat_axis=2, tiled=True
        )
        half = HD // 2
        freq = jnp.exp(jnp.arange(half, dtype=jnp.float32) * (-2.0 * math.log(500000.0) / HD))
        freq = jnp.concatenate([freq, freq])[None, :]
        scalars = [me.astype(jnp.int32).reshape(1), suffix_lengths, request_group, block_group]
        meta = (devices, block_rows, rows, min(span, devices - 1), prefix_len, repeat, scale)
        attended = attend(meta, scalars, freq, queries, own_k_rot, suffix_values, data)
        return (attended, cache[0], cache[1])

    prefix_parts = []
    suffix_parts = [(0, suffix_kv)]
    gathered = lax.all_gather(prefix_kv, "seq", axis=0, tiled=True)
    prefix_parts.append((None, gathered))
    for by in range(1, span + 1):
        suffix_parts.append((by, shifted(suffix_kv, "seq", by, False)))

    position = offset + prefix_len
    q_rot = rotate(queries.reshape(rows, q_heads, HD), position).reshape(rows, kv_heads, repeat, HD)

    key_chunks, value_chunks, visible_chunks = [], [], []
    for holder, kv in prefix_parts:
        count = kv.shape[0]
        if holder is None:
            holder_index = jnp.arange(count, dtype=jnp.int32) // block_rows
            row_group = jnp.take(block_group, holder_index)
            visible = row_group[None, :] == group[:, None]
        else:
            row_group = lax.dynamic_index_in_dim(block_group, holder, keepdims=False)
            visible = jnp.broadcast_to((group == row_group)[:, None], (rows, count))
        key_chunks.append(kv[:, :kv_cols])
        value_chunks.append(kv[:, kv_cols:])
        visible_chunks.append(visible)

    own_k_rot = None
    for back, kv in suffix_parts:
        key_index = (me - back) * rows + jnp.arange(rows, dtype=jnp.int32)
        key_request, key_offset, _ = token_info(key_index, suffix_lengths, request_group)
        k_rot = rotate(kv[:, :kv_cols].reshape(rows, kv_heads, HD), key_offset + prefix_len).reshape(
            rows, kv_cols
        )
        if back == 0:
            own_k_rot = k_rot
        visible = (
            (key_index[None, :] >= 0)
            & (key_request[None, :] == request[:, None])
            & (key_index[None, :] <= index[:, None])
        )
        key_chunks.append(k_rot)
        value_chunks.append(kv[:, kv_cols:])
        visible_chunks.append(visible)

    cache = lax.all_to_all(
        jnp.stack([own_k_rot, suffix_values], axis=0), "tp", split_axis=1, concat_axis=2, tiled=True
    )

    def scores_of(keys, visible):
        keys_split = keys.reshape(keys.shape[0], kv_heads, HD)
        scores = (
            jnp.einsum("bgrd,kgd->bgrk", q_rot, keys_split, preferred_element_type=jnp.float32)
            * scale
        )
        return jnp.where(visible[:, None, None, :], scores, BIG_NEGATIVE)

    def summed_of(scores, high, values, visible):
        weights = jnp.where(visible[:, None, None, :], jnp.exp(scores - high[..., None]), 0.0)
        summed = jnp.einsum(
            "bgrk,kgd->bgrd",
            weights.astype(jnp.bfloat16),
            values.reshape(values.shape[0], kv_heads, HD),
            preferred_element_type=jnp.float32,
        )
        return jnp.sum(weights, axis=-1), summed

    keys = jnp.concatenate(key_chunks, axis=0)
    values = jnp.concatenate(value_chunks, axis=0)
    visible = jnp.concatenate(visible_chunks, axis=1)
    count = keys.shape[0]
    if count * rows * q_heads * 4 <= (8 << 20):
        scores = scores_of(keys, visible)
        high = jnp.max(scores, axis=-1)
        total, summed = summed_of(scores, high, values, visible)
    else:
        width = 512
        steps = count // width
        tail = steps * width
        piece_k = keys[:tail].reshape(steps, width, kv_cols)
        piece_v = values[:tail].reshape(steps, width, kv_cols)
        piece_m = jnp.moveaxis(visible[:, :tail].reshape(rows, steps, width), 1, 0)

        def high_step(high, piece):
            k, m = piece
            return jnp.maximum(high, jnp.max(scores_of(k, m), axis=-1)), None

        high = jnp.max(scores_of(keys[tail:], visible[:, tail:]), axis=-1)
        high, _ = lax.scan(high_step, high, (piece_k, piece_m))

        def sum_step(carry, piece):
            k, v, m = piece
            total, summed = summed_of(scores_of(k, m), high, v, m)
            return (carry[0] + total, carry[1] + summed), None

        start = summed_of(scores_of(keys[tail:], visible[:, tail:]), high, values[tail:], visible[:, tail:])
        (total, summed), _ = lax.scan(sum_step, start, (piece_k, piece_v, piece_m))
    attended = (summed / total[..., None]).reshape(rows, q_heads * HD).astype(jnp.bfloat16)
    return (attended, cache[0], cache[1])


def solution(mesh):
    return jax.shard_map(
        body,
        mesh=mesh,
        in_specs=(
            P("seq", "tp"),
            P("seq", "tp"),
            P("seq", "tp"),
            P("seq", "tp"),
            P("seq", "tp"),
            P(),
            P(),
            P(),
        ),
        out_specs=(P("seq", "tp"), P(("seq", "tp"), None), P(("seq", "tp"), None)),
        check_vma=False,
    )
```

```python
import functools
import math

import jax
import jax.numpy as jnp
from jax import lax
from jax.experimental import pallas as pl
from jax.experimental.pallas import tpu as pltpu
from jax.sharding import PartitionSpec as P

HD = 128
GROUPS = 4


BIG_NEGATIVE = -1e30


def rotate(values, position):
    half = values.shape[-1] // 2
    freq = jnp.exp(
        jnp.arange(half, dtype=jnp.float32) * (-2.0 * math.log(500000.0) / values.shape[-1])
    )
    angle = position.astype(jnp.float32)[:, None] * freq[None, :]
    cosine = jnp.cos(angle)[:, None, :]
    sine = jnp.sin(angle)[:, None, :]
    floats = values.astype(jnp.float32)
    lower = floats[..., :half]
    upper = floats[..., half:]
    return jnp.concatenate(
        [lower * cosine - upper * sine, upper * cosine + lower * sine], axis=-1
    ).astype(jnp.bfloat16)


def attend_kernel(meta, *refs):
    devices, block_rows, rows, tails, prefix_len, repeat, scale = meta
    me_ref, lens_ref, rg_ref, bg_ref, freq_ref, q_ref, own_k_ref, own_v_ref = refs[:8]
    data = refs[8 : 8 + devices]
    out_ref, kscr, vscr, raw, sems = refs[8 + devices :]
    kv_cols = kscr.shape[1]
    count = kscr.shape[0]
    base = devices * block_rows
    q_heads = q_ref.shape[1] // HD
    me = me_ref[0]
    reqs = lens_ref.shape[0]
    width = -(-reqs // HD) * HD
    height = -(-reqs // 8) * 8
    never = 1 << 30
    lane = lax.broadcasted_iota(jnp.int32, (1, width), 1)
    sub = lax.broadcasted_iota(jnp.int32, (height, 1), 0)
    start_row = jnp.full((1, width), never, jnp.int32)
    group_row = jnp.zeros((1, width), jnp.int32)
    start_col = jnp.full((height, 1), never, jnp.int32)
    at = 0
    for j in range(reqs):
        start_row = jnp.where(lane == j, at, start_row)
        group_row = jnp.where(lane == j, rg_ref[j], group_row)
        start_col = jnp.where(sub == j, at, start_col)
        at = at + lens_ref[j]

    def info(index):
        after = index >= start_row
        request = jnp.sum(after.astype(jnp.float32), axis=1, keepdims=True).astype(jnp.int32) - 1
        first = jnp.max(jnp.where(after, start_row, 0).astype(jnp.float32), axis=1, keepdims=True)
        group = jnp.sum(
            jnp.where(lane == request, group_row, 0).astype(jnp.float32), axis=1, keepdims=True
        )
        return request, index - first.astype(jnp.int32), group.astype(jnp.int32)

    def request_of_row(index):
        after = index >= start_col
        return jnp.sum(after.astype(jnp.float32), axis=0, keepdims=True).astype(jnp.int32) - 1

    head_lane = lax.broadcasted_iota(jnp.int32, (1, HD), 1)
    freq = freq_ref[...]
    sign = jnp.where(head_lane < HD // 2, -1.0, 1.0).astype(jnp.float32)

    def tables(offset):
        angle = (offset + prefix_len).astype(jnp.float32) * freq
        return jnp.cos(angle), jnp.sin(angle) * sign

    def rotated(x, cosine, sine):
        return (x * cosine + pltpu.roll(x, HD // 2, 1) * sine).astype(jnp.bfloat16)

    copies = []
    for c in range(devices):
        rows_c = pl.ds(c * block_rows, block_rows)
        copies.append(pltpu.make_async_copy(
            data[c].at[pl.ds(0, block_rows), pl.ds(0, kv_cols)], kscr.at[rows_c, :], sems.at[len(copies)]
        ))
        copies.append(pltpu.make_async_copy(
            data[c].at[pl.ds(0, block_rows), pl.ds(kv_cols, kv_cols)], vscr.at[rows_c, :], sems.at[len(copies)]
        ))
    for b in range(1, tails + 1):
        low = base + b * rows
        copies.append(pltpu.make_async_copy(
            data[b].at[pl.ds(block_rows, rows), pl.ds(0, kv_cols)], raw.at[b - 1], sems.at[len(copies)]
        ))
        copies.append(pltpu.make_async_copy(
            data[b].at[pl.ds(block_rows, rows), pl.ds(kv_cols, kv_cols)], vscr.at[pl.ds(low, rows), :],
            sems.at[len(copies)],
        ))
    for copy in copies:
        copy.start()
    for copy in copies[2 * devices :]:
        copy.wait()
    for b in range(0, tails + 1):
        low = base + b * rows
        index = (me - b) * rows + lax.broadcasted_iota(jnp.int32, (rows, 1), 0)
        _, offset, _ = info(index)
        cosine, sine = tables(offset)
        for g in range(kv_cols // HD):
            if b == 0:
                kscr[low : low + rows, g * HD : (g + 1) * HD] = own_k_ref[:, g * HD : (g + 1) * HD]
            else:
                x = raw[b - 1, :, g * HD : (g + 1) * HD]
                kscr[low : low + rows, g * HD : (g + 1) * HD] = rotated(x.astype(jnp.float32), cosine, sine)
        if b == 0:
            vscr[low : low + rows, :] = own_v_ref[...]

    token = me * rows + lax.broadcasted_iota(jnp.int32, (rows, 1), 0)
    request, offset, group = info(token)
    col = lax.broadcasted_iota(jnp.int32, (1, count), 1)
    key_group = jnp.full((1, count), -1, jnp.int32)
    for c in range(devices):
        holder = lax.rem(me - c + devices, devices)
        key_group = jnp.where(col >= c * block_rows, bg_ref[holder], key_group)
    key_index = jnp.full((1, count), -1, jnp.int32)
    for b in range(tails + 1):
        low = base + b * rows
        key_index = jnp.where(col >= low, (me - b) * rows + col - low, key_index)
    key_request = request_of_row(key_index)
    visible = ((col < base) & (key_group == group)) | (
        (key_request == request) & (key_index <= token)
    )
    cosine, sine = tables(offset)
    for copy in copies[: 2 * devices]:
        copy.wait()
    for g in range(q_heads // repeat):
        heads = range(g * repeat, (g + 1) * repeat)
        q = jnp.concatenate(
            [rotated(q_ref[:, h * HD : (h + 1) * HD].astype(jnp.float32), cosine, sine) for h in heads],
            axis=0,
        )
        k = kscr[:, g * HD : (g + 1) * HD]
        scores = lax.dot_general(
            q, k, (((1,), (1,)), ((), ())), preferred_element_type=jnp.float32
        )
        weights, totals = [], []
        for r in range(repeat):
            part = jnp.where(visible, scores[r * rows : (r + 1) * rows], BIG_NEGATIVE)
            high = jnp.max(part, axis=1, keepdims=True)
            part = jnp.exp2((part - high) * (scale * math.log2(math.e)))
            totals.append(jnp.sum(part, axis=1, keepdims=True))
            weights.append(part.astype(jnp.bfloat16))
        v = vscr[:, g * HD : (g + 1) * HD]
        summed = jnp.dot(jnp.concatenate(weights, axis=0), v, preferred_element_type=jnp.float32)
        for r, h in enumerate(heads):
            out_ref[:, h * HD : (h + 1) * HD] = (summed[r * rows : (r + 1) * rows] / totals[r]).astype(
                out_ref.dtype
            )


def attend(meta, scalars, freq, queries, own_k, own_v, data):
    devices, block_rows, rows, tails = meta[:4]
    kv_cols = own_k.shape[1]
    q_heads = queries.shape[1] // HD
    count = devices * block_rows + rows * (1 + tails)
    flops = 4 * rows * count * HD * q_heads
    arrays = [queries, own_k, own_v, *data]
    nbytes = sum(a.size * a.dtype.itemsize for a in arrays)
    smem = pl.BlockSpec(memory_space=pltpu.SMEM)
    vmem = pl.BlockSpec(memory_space=pltpu.VMEM)
    return pl.pallas_call(
        functools.partial(attend_kernel, meta),
        out_shape=jax.ShapeDtypeStruct(queries.shape, jnp.bfloat16),
        in_specs=[smem] * len(scalars) + [vmem] * 4 + [pl.BlockSpec(memory_space=pl.ANY)] * len(data),
        out_specs=vmem,
        scratch_shapes=[
            pltpu.VMEM((count, kv_cols), jnp.bfloat16),
            pltpu.VMEM((count, kv_cols), jnp.bfloat16),
            pltpu.VMEM((max(tails, 1), rows, kv_cols), jnp.bfloat16),
            pltpu.SemaphoreType.DMA((2 * devices + 2 * tails,)),
        ],
        cost_estimate=pl.CostEstimate(
            flops=flops,
            transcendentals=rows * count * q_heads,
            bytes_accessed=nbytes + queries.size * 2,
        ),
    )(*scalars, freq, *arrays)


def token_info(index, suffix_lengths, request_group):
    ends = jnp.cumsum(suffix_lengths)
    request = jnp.sum((index[:, None] >= ends[None, :]).astype(jnp.int32), axis=1)
    onehot = request[:, None] == jnp.arange(suffix_lengths.shape[0], dtype=jnp.int32)[None, :]
    first = jnp.sum(jnp.where(onehot, (ends - suffix_lengths)[None, :], 0), axis=1)
    group = jnp.sum(jnp.where(onehot, request_group[None, :], 0), axis=1)
    return (request, index - first, group)


def shifted(array, axis, by, wrap):
    length = lax.axis_size(axis)
    pairs = [(i, (i + by) % length) for i in range(length) if wrap or i + by < length]
    return lax.ppermute(array, axis, pairs)


def body(
    queries,
    suffix_keys,
    suffix_values,
    prefix_keys,
    prefix_values,
    suffix_lengths,
    request_group,
    block_group,
):
    rows = queries.shape[0]
    kv_cols = suffix_keys.shape[1]
    kv_heads = kv_cols // HD
    q_heads = queries.shape[1] // HD
    repeat = q_heads // kv_heads
    devices = lax.axis_size("seq")
    me = lax.axis_index("seq")
    block_rows = prefix_keys.shape[0]
    prefix_len = block_rows * devices // GROUPS
    span = max(1, min(2048 // rows, devices // 8))
    scale = HD ** (-0.5)
    index = me * rows + jnp.arange(rows, dtype=jnp.int32)
    request, offset, group = token_info(index, suffix_lengths, request_group)

    prefix_kv = jnp.concatenate([prefix_keys, prefix_values], axis=1)
    suffix_kv = jnp.concatenate([suffix_keys, suffix_values], axis=1)

    def rotated_keys(raw, back):
        key_index = (me - back) * rows + jnp.arange(rows, dtype=jnp.int32)
        key_request, key_offset, _ = token_info(key_index, suffix_lengths, request_group)
        k_rot = rotate(raw.reshape(rows, kv_heads, HD), key_offset + prefix_len).reshape(rows, kv_cols)
        return key_index, key_request, k_rot

    if devices <= 16:
        received = {}
        late = list(range(span + 1, devices))[: max(0, devices - 1 - 5)]
        for by in range(1, devices):
            if by <= span:
                received[by] = shifted(jnp.concatenate([prefix_kv, suffix_kv], axis=0), "seq", by, True)
            elif by not in late:
                received[by] = shifted(prefix_kv, "seq", by, True)
        gates = tuple(received[devices - 1 - i] for i in range(len(late)))
        gates, payload, cache_keys_in, cache_values_in = lax.optimization_barrier(
            (gates, prefix_kv, suffix_keys, suffix_values)
        )
        for i, by in enumerate(late):
            received[devices - 1 - i] = gates[i]
            received[by] = shifted(payload, "seq", by, True)
        data = [prefix_kv] + [received[by] for by in range(1, devices)]
        if not late:
            cache_keys_in, cache_values_in = suffix_keys, suffix_values
        _, own_offset, _ = token_info(index, suffix_lengths, request_group)
        own_k_rot = rotate(cache_keys_in.reshape(rows, kv_heads, HD), own_offset + prefix_len).reshape(
            rows, kv_cols
        )
        cache = lax.all_to_all(
            jnp.stack([own_k_rot, cache_values_in], axis=0), "tp", split_axis=1, concat_axis=2, tiled=True
        )
        half = HD // 2
        freq = jnp.exp(jnp.arange(half, dtype=jnp.float32) * (-2.0 * math.log(500000.0) / HD))
        freq = jnp.concatenate([freq, freq])[None, :]
        scalars = [me.astype(jnp.int32).reshape(1), suffix_lengths, request_group, block_group]
        meta = (devices, block_rows, rows, min(span, devices - 1), prefix_len, repeat, scale)
        attended = attend(meta, scalars, freq, queries, own_k_rot, suffix_values, data)
        return (attended, cache[0], cache[1])

    prefix_parts = []
    suffix_parts = [(0, suffix_kv)]
    gathered = lax.all_gather(prefix_kv, "seq", axis=0, tiled=True)
    prefix_parts.append((None, gathered))
    for by in range(1, span + 1):
        suffix_parts.append((by, shifted(suffix_kv, "seq", by, False)))

    position = offset + prefix_len
    q_rot = rotate(queries.reshape(rows, q_heads, HD), position).reshape(rows, kv_heads, repeat, HD)

    key_chunks, value_chunks, visible_chunks = [], [], []
    for holder, kv in prefix_parts:
        count = kv.shape[0]
        if holder is None:
            holder_index = jnp.arange(count, dtype=jnp.int32) // block_rows
            row_group = jnp.take(block_group, holder_index)
            visible = row_group[None, :] == group[:, None]
        else:
            row_group = lax.dynamic_index_in_dim(block_group, holder, keepdims=False)
            visible = jnp.broadcast_to((group == row_group)[:, None], (rows, count))
        key_chunks.append(kv[:, :kv_cols])
        value_chunks.append(kv[:, kv_cols:])
        visible_chunks.append(visible)

    own_k_rot = None
    for back, kv in suffix_parts:
        key_index = (me - back) * rows + jnp.arange(rows, dtype=jnp.int32)
        key_request, key_offset, _ = token_info(key_index, suffix_lengths, request_group)
        k_rot = rotate(kv[:, :kv_cols].reshape(rows, kv_heads, HD), key_offset + prefix_len).reshape(
            rows, kv_cols
        )
        if back == 0:
            own_k_rot = k_rot
        visible = (
            (key_index[None, :] >= 0)
            & (key_request[None, :] == request[:, None])
            & (key_index[None, :] <= index[:, None])
        )
        key_chunks.append(k_rot)
        value_chunks.append(kv[:, kv_cols:])
        visible_chunks.append(visible)

    cache = lax.all_to_all(
        jnp.stack([own_k_rot, suffix_values], axis=0), "tp", split_axis=1, concat_axis=2, tiled=True
    )

    def scores_of(keys, visible):
        keys_split = keys.reshape(keys.shape[0], kv_heads, HD)
        scores = (
            jnp.einsum("bgrd,kgd->bgrk", q_rot, keys_split, preferred_element_type=jnp.float32)
            * scale
        )
        return jnp.where(visible[:, None, None, :], scores, BIG_NEGATIVE)

    def summed_of(scores, high, values, visible):
        weights = jnp.where(visible[:, None, None, :], jnp.exp(scores - high[..., None]), 0.0)
        summed = jnp.einsum(
            "bgrk,kgd->bgrd",
            weights.astype(jnp.bfloat16),
            values.reshape(values.shape[0], kv_heads, HD),
            preferred_element_type=jnp.float32,
        )
        return jnp.sum(weights, axis=-1), summed

    keys = jnp.concatenate(key_chunks, axis=0)
    values = jnp.concatenate(value_chunks, axis=0)
    visible = jnp.concatenate(visible_chunks, axis=1)
    count = keys.shape[0]
    if count * rows * q_heads * 4 <= (8 << 20):
        scores = scores_of(keys, visible)
        high = jnp.max(scores, axis=-1)
        total, summed = summed_of(scores, high, values, visible)
    else:
        width = 512
        steps = count // width
        tail = steps * width
        piece_k = keys[:tail].reshape(steps, width, kv_cols)
        piece_v = values[:tail].reshape(steps, width, kv_cols)
        piece_m = jnp.moveaxis(visible[:, :tail].reshape(rows, steps, width), 1, 0)

        def high_step(high, piece):
            k, m = piece
            return jnp.maximum(high, jnp.max(scores_of(k, m), axis=-1)), None

        high = jnp.max(scores_of(keys[tail:], visible[:, tail:]), axis=-1)
        high, _ = lax.scan(high_step, high, (piece_k, piece_m))

        def sum_step(carry, piece):
            k, v, m = piece
            total, summed = summed_of(scores_of(k, m), high, v, m)
            return (carry[0] + total, carry[1] + summed), None

        start = summed_of(scores_of(keys[tail:], visible[:, tail:]), high, values[tail:], visible[:, tail:])
        (total, summed), _ = lax.scan(sum_step, start, (piece_k, piece_v, piece_m))
    attended = (summed / total[..., None]).reshape(rows, q_heads * HD).astype(jnp.bfloat16)
    return (attended, cache[0], cache[1])


def solution(mesh):
    return jax.shard_map(
        body,
        mesh=mesh,
        in_specs=(
            P("seq", "tp"),
            P("seq", "tp"),
            P("seq", "tp"),
            P("seq", "tp"),
            P("seq", "tp"),
            P(),
            P(),
            P(),
        ),
        out_specs=(P("seq", "tp"), P(("seq", "tp"), None), P(("seq", "tp"), None)),
        check_vma=False,
    )
```

```python
import functools
import math

import jax
import jax.numpy as jnp
from jax import lax
from jax.experimental import pallas as pl
from jax.experimental.pallas import tpu as pltpu
from jax.sharding import PartitionSpec as P

HD = 128
GROUPS = 4


BIG_NEGATIVE = -1e30


def rotate(values, position):
    half = values.shape[-1] // 2
    freq = jnp.exp(
        jnp.arange(half, dtype=jnp.float32) * (-2.0 * math.log(500000.0) / values.shape[-1])
    )
    angle = position.astype(jnp.float32)[:, None] * freq[None, :]
    cosine = jnp.cos(angle)[:, None, :]
    sine = jnp.sin(angle)[:, None, :]
    floats = values.astype(jnp.float32)
    lower = floats[..., :half]
    upper = floats[..., half:]
    return jnp.concatenate(
        [lower * cosine - upper * sine, upper * cosine + lower * sine], axis=-1
    ).astype(jnp.bfloat16)


def attend_kernel(meta, *refs):
    devices, block_rows, rows, tails, prefix_len, repeat, scale = meta
    me_ref, lens_ref, rg_ref, bg_ref, freq_ref, q_ref, own_k_ref, own_v_ref = refs[:8]
    data = refs[8 : 8 + devices]
    out_ref, kscr, vscr = refs[8 + devices :]
    kv_cols = kscr.shape[1]
    count = kscr.shape[0]
    base = devices * block_rows
    q_heads = q_ref.shape[1] // HD
    me = me_ref[0]
    reqs = lens_ref.shape[0]
    width = -(-reqs // HD) * HD
    height = -(-reqs // 8) * 8
    never = 1 << 30
    lane = lax.broadcasted_iota(jnp.int32, (1, width), 1)
    sub = lax.broadcasted_iota(jnp.int32, (height, 1), 0)
    start_row = jnp.full((1, width), never, jnp.int32)
    group_row = jnp.zeros((1, width), jnp.int32)
    start_col = jnp.full((height, 1), never, jnp.int32)
    at = 0
    for j in range(reqs):
        start_row = jnp.where(lane == j, at, start_row)
        group_row = jnp.where(lane == j, rg_ref[j], group_row)
        start_col = jnp.where(sub == j, at, start_col)
        at = at + lens_ref[j]

    def info(index):
        after = index >= start_row
        request = jnp.sum(after.astype(jnp.float32), axis=1, keepdims=True).astype(jnp.int32) - 1
        first = jnp.max(jnp.where(after, start_row, 0).astype(jnp.float32), axis=1, keepdims=True)
        group = jnp.sum(
            jnp.where(lane == request, group_row, 0).astype(jnp.float32), axis=1, keepdims=True
        )
        return request, index - first.astype(jnp.int32), group.astype(jnp.int32)

    def request_of_row(index):
        after = index >= start_col
        return jnp.sum(after.astype(jnp.float32), axis=0, keepdims=True).astype(jnp.int32) - 1

    head_lane = lax.broadcasted_iota(jnp.int32, (1, HD), 1)
    freq = freq_ref[...]
    sign = jnp.where(head_lane < HD // 2, -1.0, 1.0).astype(jnp.float32)

    def tables(offset):
        angle = (offset + prefix_len).astype(jnp.float32) * freq
        return jnp.cos(angle), jnp.sin(angle) * sign

    def rotated(x, cosine, sine):
        return (x * cosine + pltpu.roll(x, HD // 2, 1) * sine).astype(jnp.bfloat16)

    for c in range(devices):
        kscr[c * block_rows : (c + 1) * block_rows, :] = data[c][0:block_rows, 0:kv_cols]
        vscr[c * block_rows : (c + 1) * block_rows, :] = data[c][0:block_rows, kv_cols : 2 * kv_cols]
    for b in range(0, tails + 1):
        low = base + b * rows
        index = (me - b) * rows + lax.broadcasted_iota(jnp.int32, (rows, 1), 0)
        _, offset, _ = info(index)
        cosine, sine = tables(offset)
        for g in range(kv_cols // HD):
            if b == 0:
                kscr[low : low + rows, g * HD : (g + 1) * HD] = own_k_ref[:, g * HD : (g + 1) * HD]
            else:
                x = data[b][block_rows : block_rows + rows, g * HD : (g + 1) * HD]
                kscr[low : low + rows, g * HD : (g + 1) * HD] = rotated(x.astype(jnp.float32), cosine, sine)
        if b == 0:
            vscr[low : low + rows, :] = own_v_ref[...]
        else:
            vscr[low : low + rows, :] = data[b][block_rows : block_rows + rows, kv_cols : 2 * kv_cols]

    token = me * rows + lax.broadcasted_iota(jnp.int32, (rows, 1), 0)
    request, offset, group = info(token)
    col = lax.broadcasted_iota(jnp.int32, (1, count), 1)
    key_group = jnp.full((1, count), -1, jnp.int32)
    for c in range(devices):
        holder = lax.rem(me - c + devices, devices)
        key_group = jnp.where(col >= c * block_rows, bg_ref[holder], key_group)
    key_index = jnp.full((1, count), -1, jnp.int32)
    for b in range(tails + 1):
        low = base + b * rows
        key_index = jnp.where(col >= low, (me - b) * rows + col - low, key_index)
    key_request = request_of_row(key_index)
    visible = ((col < base) & (key_group == group)) | (
        (key_request == request) & (key_index <= token)
    )
    cosine, sine = tables(offset)
    for g in range(q_heads // repeat):
        heads = range(g * repeat, (g + 1) * repeat)
        q = jnp.concatenate(
            [rotated(q_ref[:, h * HD : (h + 1) * HD].astype(jnp.float32), cosine, sine) for h in heads],
            axis=0,
        )
        k = kscr[:, g * HD : (g + 1) * HD]
        scores = lax.dot_general(
            q, k, (((1,), (1,)), ((), ())), preferred_element_type=jnp.float32
        )
        weights, totals = [], []
        for r in range(repeat):
            part = jnp.where(visible, scores[r * rows : (r + 1) * rows], BIG_NEGATIVE)
            high = jnp.max(part, axis=1, keepdims=True)
            part = jnp.exp2((part - high) * (scale * math.log2(math.e)))
            totals.append(jnp.sum(part, axis=1, keepdims=True))
            weights.append(part.astype(jnp.bfloat16))
        v = vscr[:, g * HD : (g + 1) * HD]
        summed = jnp.dot(jnp.concatenate(weights, axis=0), v, preferred_element_type=jnp.float32)
        for r, h in enumerate(heads):
            out_ref[:, h * HD : (h + 1) * HD] = (summed[r * rows : (r + 1) * rows] / totals[r]).astype(
                out_ref.dtype
            )


def attend(meta, scalars, freq, queries, own_k, own_v, data):
    devices, block_rows, rows, tails = meta[:4]
    kv_cols = own_k.shape[1]
    q_heads = queries.shape[1] // HD
    count = devices * block_rows + rows * (1 + tails)
    flops = 4 * rows * count * HD * q_heads
    arrays = [queries, own_k, own_v, *data]
    nbytes = sum(a.size * a.dtype.itemsize for a in arrays)
    smem = pl.BlockSpec(memory_space=pltpu.SMEM)
    vmem = pl.BlockSpec(memory_space=pltpu.VMEM)
    return pl.pallas_call(
        functools.partial(attend_kernel, meta),
        out_shape=jax.ShapeDtypeStruct(queries.shape, jnp.bfloat16),
        in_specs=[smem] * len(scalars) + [vmem] * (1 + len(arrays)),
        out_specs=vmem,
        scratch_shapes=[
            pltpu.VMEM((count, kv_cols), jnp.bfloat16),
            pltpu.VMEM((count, kv_cols), jnp.bfloat16),
        ],
        cost_estimate=pl.CostEstimate(
            flops=flops,
            transcendentals=rows * count * q_heads,
            bytes_accessed=nbytes + queries.size * 2,
        ),
        compiler_params=pltpu.CompilerParams(vmem_limit_bytes=16 * 1024 * 1024),
    )(*scalars, freq, *arrays)


def token_info(index, suffix_lengths, request_group):
    ends = jnp.cumsum(suffix_lengths)
    request = jnp.sum((index[:, None] >= ends[None, :]).astype(jnp.int32), axis=1)
    onehot = request[:, None] == jnp.arange(suffix_lengths.shape[0], dtype=jnp.int32)[None, :]
    first = jnp.sum(jnp.where(onehot, (ends - suffix_lengths)[None, :], 0), axis=1)
    group = jnp.sum(jnp.where(onehot, request_group[None, :], 0), axis=1)
    return (request, index - first, group)


def shifted(array, axis, by, wrap):
    length = lax.axis_size(axis)
    pairs = [(i, (i + by) % length) for i in range(length) if wrap or i + by < length]
    return lax.ppermute(array, axis, pairs)


def body(
    queries,
    suffix_keys,
    suffix_values,
    prefix_keys,
    prefix_values,
    suffix_lengths,
    request_group,
    block_group,
):
    rows = queries.shape[0]
    kv_cols = suffix_keys.shape[1]
    kv_heads = kv_cols // HD
    q_heads = queries.shape[1] // HD
    repeat = q_heads // kv_heads
    devices = lax.axis_size("seq")
    me = lax.axis_index("seq")
    block_rows = prefix_keys.shape[0]
    prefix_len = block_rows * devices // GROUPS
    span = max(1, min(2048 // rows, devices // 8))
    scale = HD ** (-0.5)
    index = me * rows + jnp.arange(rows, dtype=jnp.int32)
    request, offset, group = token_info(index, suffix_lengths, request_group)

    prefix_kv = jnp.concatenate([prefix_keys, prefix_values], axis=1)
    suffix_kv = jnp.concatenate([suffix_keys, suffix_values], axis=1)

    def rotated_keys(raw, back):
        key_index = (me - back) * rows + jnp.arange(rows, dtype=jnp.int32)
        key_request, key_offset, _ = token_info(key_index, suffix_lengths, request_group)
        k_rot = rotate(raw.reshape(rows, kv_heads, HD), key_offset + prefix_len).reshape(rows, kv_cols)
        return key_index, key_request, k_rot

    if devices <= 16:
        received = {}
        late = list(range(span + 1, devices))[: max(0, devices - 1 - 5)]
        for by in range(1, devices):
            if by <= span:
                received[by] = shifted(jnp.concatenate([prefix_kv, suffix_kv], axis=0), "seq", by, True)
            elif by not in late:
                received[by] = shifted(prefix_kv, "seq", by, True)
        gates = tuple(received[devices - 1 - i] for i in range(len(late)))
        gates, payload, cache_keys_in, cache_values_in = lax.optimization_barrier(
            (gates, prefix_kv, suffix_keys, suffix_values)
        )
        for i, by in enumerate(late):
            received[devices - 1 - i] = gates[i]
            received[by] = shifted(payload, "seq", by, True)
        data = [prefix_kv] + [received[by] for by in range(1, devices)]
        if not late:
            cache_keys_in, cache_values_in = suffix_keys, suffix_values
        _, own_offset, _ = token_info(index, suffix_lengths, request_group)
        own_k_rot = rotate(cache_keys_in.reshape(rows, kv_heads, HD), own_offset + prefix_len).reshape(
            rows, kv_cols
        )
        cache = lax.all_to_all(
            jnp.stack([own_k_rot, cache_values_in], axis=0), "tp", split_axis=1, concat_axis=2, tiled=True
        )
        half = HD // 2
        freq = jnp.exp(jnp.arange(half, dtype=jnp.float32) * (-2.0 * math.log(500000.0) / HD))
        freq = jnp.concatenate([freq, freq])[None, :]
        scalars = [me.astype(jnp.int32).reshape(1), suffix_lengths, request_group, block_group]
        meta = (devices, block_rows, rows, min(span, devices - 1), prefix_len, repeat, scale)
        attended = attend(meta, scalars, freq, queries, own_k_rot, suffix_values, data)
        return (attended, cache[0], cache[1])

    prefix_parts = []
    suffix_parts = [(0, suffix_kv)]
    gathered = lax.all_gather(prefix_kv, "seq", axis=0, tiled=True)
    prefix_parts.append((None, gathered))
    for by in range(1, span + 1):
        suffix_parts.append((by, shifted(suffix_kv, "seq", by, False)))

    position = offset + prefix_len
    q_rot = rotate(queries.reshape(rows, q_heads, HD), position).reshape(rows, kv_heads, repeat, HD)

    key_chunks, value_chunks, visible_chunks = [], [], []
    for holder, kv in prefix_parts:
        count = kv.shape[0]
        if holder is None:
            holder_index = jnp.arange(count, dtype=jnp.int32) // block_rows
            row_group = jnp.take(block_group, holder_index)
            visible = row_group[None, :] == group[:, None]
        else:
            row_group = lax.dynamic_index_in_dim(block_group, holder, keepdims=False)
            visible = jnp.broadcast_to((group == row_group)[:, None], (rows, count))
        key_chunks.append(kv[:, :kv_cols])
        value_chunks.append(kv[:, kv_cols:])
        visible_chunks.append(visible)

    own_k_rot = None
    for back, kv in suffix_parts:
        key_index = (me - back) * rows + jnp.arange(rows, dtype=jnp.int32)
        key_request, key_offset, _ = token_info(key_index, suffix_lengths, request_group)
        k_rot = rotate(kv[:, :kv_cols].reshape(rows, kv_heads, HD), key_offset + prefix_len).reshape(
            rows, kv_cols
        )
        if back == 0:
            own_k_rot = k_rot
        visible = (
            (key_index[None, :] >= 0)
            & (key_request[None, :] == request[:, None])
            & (key_index[None, :] <= index[:, None])
        )
        key_chunks.append(k_rot)
        value_chunks.append(kv[:, kv_cols:])
        visible_chunks.append(visible)

    cache = lax.all_to_all(
        jnp.stack([own_k_rot, suffix_values], axis=0), "tp", split_axis=1, concat_axis=2, tiled=True
    )

    def scores_of(keys, visible):
        keys_split = keys.reshape(keys.shape[0], kv_heads, HD)
        scores = (
            jnp.einsum("bgrd,kgd->bgrk", q_rot, keys_split, preferred_element_type=jnp.float32)
            * scale
        )
        return jnp.where(visible[:, None, None, :], scores, BIG_NEGATIVE)

    def summed_of(scores, high, values, visible):
        weights = jnp.where(visible[:, None, None, :], jnp.exp(scores - high[..., None]), 0.0)
        summed = jnp.einsum(
            "bgrk,kgd->bgrd",
            weights.astype(jnp.bfloat16),
            values.reshape(values.shape[0], kv_heads, HD),
            preferred_element_type=jnp.float32,
        )
        return jnp.sum(weights, axis=-1), summed

    keys = jnp.concatenate(key_chunks, axis=0)
    values = jnp.concatenate(value_chunks, axis=0)
    visible = jnp.concatenate(visible_chunks, axis=1)
    count = keys.shape[0]
    if count * rows * q_heads * 4 <= (8 << 20):
        scores = scores_of(keys, visible)
        high = jnp.max(scores, axis=-1)
        total, summed = summed_of(scores, high, values, visible)
    else:
        width = 512
        steps = count // width
        tail = steps * width
        piece_k = keys[:tail].reshape(steps, width, kv_cols)
        piece_v = values[:tail].reshape(steps, width, kv_cols)
        piece_m = jnp.moveaxis(visible[:, :tail].reshape(rows, steps, width), 1, 0)

        def high_step(high, piece):
            k, m = piece
            return jnp.maximum(high, jnp.max(scores_of(k, m), axis=-1)), None

        high = jnp.max(scores_of(keys[tail:], visible[:, tail:]), axis=-1)
        high, _ = lax.scan(high_step, high, (piece_k, piece_m))

        def sum_step(carry, piece):
            k, v, m = piece
            total, summed = summed_of(scores_of(k, m), high, v, m)
            return (carry[0] + total, carry[1] + summed), None

        start = summed_of(scores_of(keys[tail:], visible[:, tail:]), high, values[tail:], visible[:, tail:])
        (total, summed), _ = lax.scan(sum_step, start, (piece_k, piece_v, piece_m))
    attended = (summed / total[..., None]).reshape(rows, q_heads * HD).astype(jnp.bfloat16)
    return (attended, cache[0], cache[1])


def solution(mesh):
    return jax.shard_map(
        body,
        mesh=mesh,
        in_specs=(
            P("seq", "tp"),
            P("seq", "tp"),
            P("seq", "tp"),
            P("seq", "tp"),
            P("seq", "tp"),
            P(),
            P(),
            P(),
        ),
        out_specs=(P("seq", "tp"), P(("seq", "tp"), None), P(("seq", "tp"), None)),
        check_vma=False,
    )
```
